128 devices in a mesh: blk: 32 (over y, x, core), grp: 4 (over z).
Axes of the slice: x: 4, y: 4, z: 4, core: 2. Of those that a mesh axis runs over, the one named last changes fastest.
Arguments:
- sky_map: bfloat16 [256, 1048576], P(None, ('blk', 'grp')), may hold values from -128 to 128
- fg_templates: bfloat16 [256, 16], replicated, may hold values from -0.375 to 0.375
- cycle_len: int32 [512], P(('blk', 'grp')), may hold values from 512 to 2048, as said below
- beam_profile: float32 [8, 1024], replicated, may hold values from 0.2 to 2
- beam_index: int32 [256], P('blk'), may hold values from 0 to 7
Outputs:
- filtered: float32 [1024, 256, 2, 1024], P(None, 'blk', None, 'grp')
The draws below stay inside these ranges and needn't reach their ends.
Inputs may be any that keep to these rules, and one draw needn't show every extreme that they name: `cycle_len`: some cycle has exactly 2048 pixels.
All inputs are finite; a program needn't handle non-finite values.
Results may differ from the reference program's by a relative error of at most 0.0064.
Values may be sent and summed in bfloat16 or wider, within the bound.
No kernel may reach another device: no remote copies, remote signals or barrier semaphores. Data moves between devices by JAX's collectives and lax.ppermute only.
A program may use at most 192 MiB of HBM per device.

```python
import math
import jax
import jax.numpy as jnp
from jax import lax

NCH = 256
NMODE = 16
RPIX = 2048
L = 1024
NPROF = 8
MW = 1024
NRING = 512


def draw_sky_map(key, part):
    keys = jax.random.split(key, 3)
    cycle_scale = jnp.exp(jax.random.uniform(keys[0], (NRING,), jnp.float32, jnp.log(0.4), jnp.log(4.0)))
    chan_scale = jnp.exp(jax.random.uniform(keys[1], (NCH,), jnp.float32, jnp.log(0.5), jnp.log(2.0)))
    base = jnp.clip(jax.random.normal(keys[2], (NCH, NRING, RPIX), jnp.float32), -4.0, 4.0)
    values = base * chan_scale[:, None, None] * cycle_scale[None, :, None]
    return values.reshape(NCH, NRING * RPIX).astype(jnp.bfloat16)


def draw_cycle_len(key, part):
    first, second = jax.random.split(key)
    lengths = jax.random.randint(first, (NRING,), RPIX // 4, RPIX + 1, jnp.int32)
    spot = jax.random.randint(second, (), 0, NRING, jnp.int32)
    return lengths.at[spot].set(RPIX)


def plant(values, stream_key, smallest, high):
    dims = values.shape
    index_at = [jax.random.randint(jax.random.fold_in(stream_key, axis), (), 0, dims[axis]) for axis in range(len(dims))]
    values = values.at[tuple(index_at)].set(smallest)
    longest = dims.index(max(dims))
    index_at[longest] = (index_at[longest] + 1) % dims[longest]
    return values.at[tuple(index_at)].set(high)


def normal_values(own_key, dims, width, most, kind=jnp.bfloat16):
    drawn = width * jax.random.normal(own_key, dims, jnp.float32)
    return jnp.clip(drawn, min=-most, max=most).astype(kind)


def setup_inputs(seed: int = 0) -> dict:
    arg_keys = jax.random.split(jax.random.key(seed), 6)
    sky_map = draw_sky_map(jax.random.fold_in(arg_keys[5], 71), 0)
    fg_templates = normal_values(arg_keys[1], (NCH, NMODE), NCH ** -0.5, 0.375)
    cycle_len = draw_cycle_len(jax.random.fold_in(arg_keys[5], 71), 0)
    beam_profile = jnp.clip(jnp.exp(jax.random.uniform(arg_keys[3], (NPROF, L), jnp.float32, math.log(0.2), math.log(2.0))), 0.2, 2.0)
    beam_index = plant(jax.random.randint(arg_keys[4], (NCH,), 0, NPROF), jax.random.fold_in(arg_keys[4], 1), 0, NPROF - 1).astype(jnp.int32)
    return {"sky_map": sky_map, "fg_templates": fg_templates, "cycle_len": cycle_len, "beam_profile": beam_profile, "beam_index": beam_index}


def cycle_table(length, m_width):
    slots = jnp.arange(RPIX, dtype=jnp.int32)
    orders = jnp.arange(m_width, dtype=jnp.int32)
    phase = orders[None, :] * (2 * slots[:, None] + 1) % (2 * length)
    angle = jnp.pi * phase.astype(jnp.float32) / length.astype(jnp.float32)
    weight = jnp.where(slots < length, 1.0, 0.0).astype(jnp.float32) * lax.rsqrt(length.astype(jnp.float32))
    table = jnp.concatenate([jnp.cos(angle), -jnp.sin(angle)], axis=1) * weight[:, None]
    return table.astype(jnp.bfloat16)

def theta_table(cycle_ids, n_cycle):
    degrees = jnp.arange(L, dtype=jnp.int32)
    odd = 2 * cycle_ids + 1
    phase = degrees[:, None] * odd[None, :] % (4 * n_cycle)
    angle = jnp.pi * phase.astype(jnp.float32) / (2.0 * n_cycle)
    weight = jnp.sin(jnp.pi * odd.astype(jnp.float32) / (2.0 * n_cycle)) * (2.0 / jnp.sqrt(jnp.float32(n_cycle)))
    return (jnp.cos(angle) * weight[None, :]).astype(jnp.bfloat16)

def reference(sky_map, fg_templates, cycle_len, beam_profile, beam_index):
    slots = jnp.arange(RPIX, dtype=jnp.int32)
    valid = (slots[None, :] < cycle_len[:, None]).reshape(-1)
    masked = jnp.where(valid[None, :], sky_map, jnp.zeros((), jnp.bfloat16))
    mode_amps = jnp.dot(fg_templates.T.astype(jnp.float32), masked.astype(jnp.float32), preferred_element_type=jnp.float32).astype(jnp.bfloat16)
    gram_sum = jnp.dot(mode_amps.astype(jnp.float32), mode_amps.T.astype(jnp.float32), preferred_element_type=jnp.float32)
    cross_sum = lax.dot_general(mode_amps.astype(jnp.float32), masked.astype(jnp.float32), (((1,), (1,)), ((), ())), preferred_element_type=jnp.float32)
    coef = jnp.linalg.solve(gram_sum, cross_sum)
    amps_wide = mode_amps.astype(jnp.float32)

    def per_cycle(inputs):
        index, length = inputs
        start = (index * RPIX).astype(jnp.int32)
        block = lax.dynamic_slice_in_dim(masked, start, RPIX, 1)
        modes = lax.dynamic_slice_in_dim(amps_wide, start, RPIX, 1)
        cleaned = (block.astype(jnp.float32) - jnp.dot(coef.T, modes, precision=lax.Precision.HIGHEST)).astype(jnp.bfloat16)
        return jnp.dot(cleaned.astype(jnp.float32), cycle_table(length, MW).astype(jnp.float32), preferred_element_type=jnp.float32).astype(jnp.bfloat16)
    fourier = lax.map(per_cycle, (jnp.arange(NRING, dtype=jnp.int32), cycle_len))
    theta_tab = theta_table(jnp.arange(NRING, dtype=jnp.int32), NRING)
    harmonic = jnp.dot(theta_tab.astype(jnp.float32), fourier.reshape(NRING, -1).astype(jnp.float32), preferred_element_type=jnp.float32)
    harmonic = harmonic.reshape(L, NCH, 2, MW)
    profiles = beam_profile[beam_index]
    shaped = harmonic * profiles.T[:, :, None, None]
    mweight = 0.25 + jnp.arange(MW, dtype=jnp.int32).astype(jnp.float32) / MW
    weighted = shaped * mweight[None, None, None, :]
    power = lax.optimization_barrier(jnp.sum(weighted * weighted, axis=(0, 2, 3)))
    return weighted * lax.rsqrt(power / (2.0 * L * MW) + 1e-06)[None, :, None, None]
```

```python
import jax
import jax.numpy as jnp
from jax import lax
from jax.sharding import PartitionSpec as P

RPIX = 2048
L = 1024
M_DEV = 256
J_LO = 128


def cos_sin_of_phase(phase, length):
    angle = jnp.pi * phase.astype(jnp.float32) / length.astype(jnp.float32)
    return jnp.cos(angle), jnp.sin(angle)


def cycle_table(length, m_width):
    n_hi = RPIX // J_LO
    period = 2 * length
    orders = jnp.arange(m_width, dtype=jnp.int32)
    j_hi = jnp.arange(n_hi, dtype=jnp.int32)
    j_lo = jnp.arange(J_LO, dtype=jnp.int32)
    phase_hi = (2 * J_LO * j_hi[:, None]) % period * orders[None, :] % period
    phase_lo = orders[None, :] * (2 * j_lo[:, None] + 1) % period
    ca, sa = cos_sin_of_phase(phase_hi, length)
    cb, sb = cos_sin_of_phase(phase_lo, length)
    ca, sa = ca[:, None, :], sa[:, None, :]
    cb, sb = cb[None, :, :], sb[None, :, :]
    cos_t = (ca * cb - sa * sb).reshape(RPIX, m_width)
    sin_t = (sa * cb + ca * sb).reshape(RPIX, m_width)
    slots = jnp.arange(RPIX, dtype=jnp.int32)
    weight = jnp.where(slots < length, 1.0, 0.0).astype(jnp.float32) * lax.rsqrt(
        length.astype(jnp.float32)
    )
    table = jnp.concatenate([cos_t, -sin_t], axis=1) * weight[:, None]
    return table.astype(jnp.bfloat16)


def theta_table(cycle_ids, n_cycle):
    degrees = jnp.arange(L, dtype=jnp.int32)
    odd = 2 * cycle_ids + 1
    phase = degrees[:, None] * odd[None, :] % (4 * n_cycle)
    angle = jnp.pi * phase.astype(jnp.float32) / (2.0 * n_cycle)
    weight = jnp.sin(jnp.pi * odd.astype(jnp.float32) / (2.0 * n_cycle)) * (
        2.0 / jnp.sqrt(jnp.float32(n_cycle))
    )
    return (jnp.cos(angle) * weight[None, :]).astype(jnp.bfloat16)


def body(sky_map, fg_templates, cycle_len, beam_profile, beam_index):
    n_blk = lax.axis_size("blk")
    n_grp = lax.axis_size("grp")
    cycle_dev = cycle_len.shape[0]
    n_chan = sky_map.shape[0]
    n_mode = fg_templates.shape[1]
    chan_dev = n_chan // n_blk
    m_width = M_DEV * n_grp
    n_cycle = cycle_dev * n_blk * n_grp
    slots = jnp.arange(RPIX, dtype=jnp.int32)
    valid = (slots[None, :] < cycle_len[:, None]).reshape(-1)
    masked = jnp.where(valid[None, :], sky_map, jnp.zeros((), jnp.bfloat16))
    mode_amps = jnp.dot(fg_templates.T, masked, preferred_element_type=jnp.float32).astype(
        jnp.bfloat16
    )
    gram_part = jnp.dot(mode_amps, mode_amps.T, preferred_element_type=jnp.float32)
    cross_part = lax.dot_general(
        mode_amps, masked, (((1,), (1,)), ((), ())), preferred_element_type=jnp.float32
    )
    amps_wide = mode_amps.astype(jnp.float32)
    sums = lax.psum(jnp.concatenate([gram_part, cross_part], axis=1), ("blk", "grp"))
    gram_sum = sums[:, :n_mode]
    cross_sum = sums[:, n_mode:]
    lower = jnp.linalg.cholesky(gram_sum)
    basis = jax.scipy.linalg.solve_triangular(lower, amps_wide, lower=True)
    projected = jax.scipy.linalg.solve_triangular(lower, cross_sum, lower=True)
    correction = jnp.dot(projected.T, basis, precision=lax.Precision.HIGHEST)
    cleaned = (masked.astype(jnp.float32) - correction).astype(jnp.bfloat16)
    pieces = []
    for local in range(cycle_dev):
        block = cleaned[:, local * RPIX : (local + 1) * RPIX]
        table = cycle_table(cycle_len[local], m_width)
        pieces.append(
            jnp.dot(block, table, preferred_element_type=jnp.float32).astype(jnp.bfloat16)
        )
    fourier = jnp.stack(pieces, 0).reshape(cycle_dev, n_chan, 2, m_width)
    position = jnp.arange(n_cycle, dtype=jnp.int32)
    moved = lax.all_to_all(
        lax.all_to_all(fourier, "blk", split_axis=1, concat_axis=0, tiled=True),
        "grp",
        split_axis=3,
        concat_axis=0,
        tiled=True,
    )
    group_id = position // (n_blk * cycle_dev)
    block_id = position // cycle_dev % n_blk
    cycle_ids = (block_id * n_grp + group_id) * cycle_dev + position % cycle_dev
    moved = moved.reshape(n_cycle, chan_dev * 2 * M_DEV)
    theta_tab = theta_table(cycle_ids, n_cycle)
    harmonic = jnp.dot(theta_tab, moved, preferred_element_type=jnp.float32).reshape(
        L, chan_dev, 2, M_DEV
    )
    onehot = (
        beam_index[:, None] == jnp.arange(beam_profile.shape[0], dtype=jnp.int32)[None, :]
    ).astype(jnp.float32)
    profiles = jnp.dot(onehot, beam_profile, precision=lax.Precision.HIGHEST)
    shaped = harmonic * profiles.T[:, :, None, None]
    orders = lax.axis_index("grp") * M_DEV + jnp.arange(M_DEV, dtype=jnp.int32)
    mweight = 0.25 + orders.astype(jnp.float32) / m_width
    weighted = shaped * mweight[None, None, None, :]
    power_part = jnp.sum(weighted * weighted, axis=(0, 2, 3))
    power = lax.psum(power_part, "grp")
    return weighted * lax.rsqrt(power / (2.0 * L * m_width) + 1e-06)[None, :, None, None]


def solution(mesh):
    return jax.shard_map(
        body,
        mesh=mesh,
        in_specs=(P(None, ("blk", "grp")), P(), P(("blk", "grp")), P(), P("blk")),
        out_specs=P(None, "blk", None, "grp"),
        check_vma=False,
    )
```

```python
import jax
import jax.numpy as jnp
from jax import lax
from jax.sharding import PartitionSpec as P

RPIX = 2048
L = 1024
M_DEV = 256
J_LO = 128


def cos_sin_of_phase(phase, length):
    angle = jnp.pi * phase.astype(jnp.float32) / length.astype(jnp.float32)
    return jnp.cos(angle), jnp.sin(angle)


def cycle_table(length, m_width):
    n_hi = RPIX // J_LO
    period = 2 * length
    orders = jnp.arange(m_width, dtype=jnp.int32)
    j_hi = jnp.arange(n_hi, dtype=jnp.int32)
    j_lo = jnp.arange(J_LO, dtype=jnp.int32)
    phase_hi = (2 * J_LO * j_hi[:, None]) % period * orders[None, :] % period
    phase_lo = orders[None, :] * (2 * j_lo[:, None] + 1) % period
    ca, sa = cos_sin_of_phase(phase_hi, length)
    cb, sb = cos_sin_of_phase(phase_lo, length)
    ca, sa = ca[:, None, :], sa[:, None, :]
    cb, sb = cb[None, :, :], sb[None, :, :]
    cos_t = (ca * cb - sa * sb).reshape(RPIX, m_width)
    sin_t = (sa * cb + ca * sb).reshape(RPIX, m_width)
    slots = jnp.arange(RPIX, dtype=jnp.int32)
    weight = jnp.where(slots < length, 1.0, 0.0).astype(jnp.float32) * lax.rsqrt(
        length.astype(jnp.float32)
    )
    table = jnp.concatenate([cos_t, -sin_t], axis=1) * weight[:, None]
    return table.astype(jnp.bfloat16)


def theta_table(cycle_ids, n_cycle):
    degrees = jnp.arange(L, dtype=jnp.int32)
    odd = 2 * cycle_ids + 1
    phase = degrees[:, None] * odd[None, :] % (4 * n_cycle)
    angle = jnp.pi * phase.astype(jnp.float32) / (2.0 * n_cycle)
    weight = jnp.sin(jnp.pi * odd.astype(jnp.float32) / (2.0 * n_cycle)) * (
        2.0 / jnp.sqrt(jnp.float32(n_cycle))
    )
    return (jnp.cos(angle) * weight[None, :]).astype(jnp.bfloat16)


def sub_axes(n_blk, n_grp):
    return [
        ("blk", 2, 1, n_blk),
        ("blk", 4, 2, n_blk),
        ("blk", n_blk // 8, 8, n_blk),
        ("grp", n_grp, 1, n_grp),
    ]


def shift_perm(size, stride, total, k):
    pairs = []
    for i in range(total):
        c = (i // stride) % size
        pairs.append((i, i + ((c + k) % size - c) * stride))
    return pairs


def ring_sum(v, subs):
    for axis, size, stride, total in subs:
        parts = [lax.ppermute(v, axis, shift_perm(size, stride, total, k)) for k in range(1, size)]
        for part in parts:
            v = v + part
    return v


def body(sky_map, fg_templates, cycle_len, beam_profile, beam_index):
    n_blk = lax.axis_size("blk")
    n_grp = lax.axis_size("grp")
    cycle_dev = cycle_len.shape[0]
    n_chan = sky_map.shape[0]
    n_mode = fg_templates.shape[1]
    chan_dev = n_chan // n_blk
    m_width = M_DEV * n_grp
    n_cycle = cycle_dev * n_blk * n_grp
    slots = jnp.arange(RPIX, dtype=jnp.int32)
    valid = (slots[None, :] < cycle_len[:, None]).reshape(-1)
    masked = jnp.where(valid[None, :], sky_map, jnp.zeros((), jnp.bfloat16))
    mode_amps = jnp.dot(fg_templates.T, masked, preferred_element_type=jnp.float32).astype(
        jnp.bfloat16
    )
    gram_part = jnp.dot(mode_amps, mode_amps.T, preferred_element_type=jnp.float32)
    cross_part = lax.dot_general(
        mode_amps, masked, (((1,), (1,)), ((), ())), preferred_element_type=jnp.float32
    )
    amps_wide = mode_amps.astype(jnp.float32)
    subs = sub_axes(n_blk, n_grp)
    sums = ring_sum(jnp.concatenate([gram_part, cross_part], axis=1), subs)
    gram_sum = sums[:, :n_mode]
    cross_sum = sums[:, n_mode:]
    lower = jnp.linalg.cholesky(gram_sum)
    basis = jax.scipy.linalg.solve_triangular(lower, amps_wide, lower=True)
    projected = jax.scipy.linalg.solve_triangular(lower, cross_sum, lower=True)
    correction = jnp.dot(projected.T, basis, precision=lax.Precision.HIGHEST)
    cleaned = (masked.astype(jnp.float32) - correction).astype(jnp.bfloat16)
    pieces = []
    for local in range(cycle_dev):
        block = cleaned[:, local * RPIX : (local + 1) * RPIX]
        table = cycle_table(cycle_len[local], m_width)
        pieces.append(
            jnp.dot(block, table, preferred_element_type=jnp.float32).astype(jnp.bfloat16)
        )
    fourier = jnp.stack(pieces, 0).reshape(cycle_dev, n_blk, chan_dev, 2, n_grp, M_DEV)
    sendbuf = fourier.transpose(1, 4, 0, 2, 3, 5).reshape(
        n_blk * n_grp, cycle_dev, chan_dev, 2, M_DEV
    )
    moved = lax.all_to_all(sendbuf, ("blk", "grp"), 0, 0, tiled=True)
    moved = moved.reshape(n_cycle, chan_dev * 2 * M_DEV)
    theta_tab = theta_table(jnp.arange(n_cycle, dtype=jnp.int32), n_cycle)
    harmonic = jnp.dot(theta_tab, moved, preferred_element_type=jnp.float32).reshape(
        L, chan_dev, 2, M_DEV
    )
    onehot = (
        beam_index[:, None] == jnp.arange(beam_profile.shape[0], dtype=jnp.int32)[None, :]
    ).astype(jnp.float32)
    profiles = jnp.dot(onehot, beam_profile, precision=lax.Precision.HIGHEST)
    shaped = harmonic * profiles.T[:, :, None, None]
    orders = lax.axis_index("grp") * M_DEV + jnp.arange(M_DEV, dtype=jnp.int32)
    mweight = 0.25 + orders.astype(jnp.float32) / m_width
    weighted = shaped * mweight[None, None, None, :]
    power_part = jnp.sum(weighted * weighted, axis=(0, 2, 3))
    power = ring_sum(power_part, subs[3:])
    return weighted * lax.rsqrt(power / (2.0 * L * m_width) + 1e-06)[None, :, None, None]


def solution(mesh):
    return jax.shard_map(
        body,
        mesh=mesh,
        in_specs=(P(None, ("blk", "grp")), P(), P(("blk", "grp")), P(), P("blk")),
        out_specs=P(None, "blk", None, "grp"),
        check_vma=False,
    )
```

```python
import jax
import jax.numpy as jnp
from jax import lax
from jax.sharding import PartitionSpec as P

RPIX = 2048
L = 1024
M_DEV = 256
J_LO = 128


def cos_sin_of_phase(phase, length):
    angle = jnp.pi * phase.astype(jnp.float32) / length.astype(jnp.float32)
    return jnp.cos(angle), jnp.sin(angle)


def cycle_table(length, m_width):
    n_hi = RPIX // J_LO
    period = 2 * length
    orders = jnp.arange(m_width, dtype=jnp.int32)
    j_hi = jnp.arange(n_hi, dtype=jnp.int32)
    j_lo = jnp.arange(J_LO, dtype=jnp.int32)
    phase_hi = (2 * J_LO * j_hi[:, None]) % period * orders[None, :] % period
    phase_lo = orders[None, :] * (2 * j_lo[:, None] + 1) % period
    ca, sa = cos_sin_of_phase(phase_hi, length)
    cb, sb = cos_sin_of_phase(phase_lo, length)
    ca, sa = ca[:, None, :], sa[:, None, :]
    cb, sb = cb[None, :, :], sb[None, :, :]
    cos_t = (ca * cb - sa * sb).reshape(RPIX, m_width)
    sin_t = (sa * cb + ca * sb).reshape(RPIX, m_width)
    slots = jnp.arange(RPIX, dtype=jnp.int32)
    weight = jnp.where(slots < length, 1.0, 0.0).astype(jnp.float32) * lax.rsqrt(
        length.astype(jnp.float32)
    )
    table = jnp.concatenate([cos_t, -sin_t], axis=1) * weight[:, None]
    return table.astype(jnp.bfloat16)


def theta_table(cycle_ids, n_cycle):
    degrees = jnp.arange(L, dtype=jnp.int32)
    odd = 2 * cycle_ids + 1
    phase = degrees[:, None] * odd[None, :] % (4 * n_cycle)
    angle = jnp.pi * phase.astype(jnp.float32) / (2.0 * n_cycle)
    weight = jnp.sin(jnp.pi * odd.astype(jnp.float32) / (2.0 * n_cycle)) * (
        2.0 / jnp.sqrt(jnp.float32(n_cycle))
    )
    return (jnp.cos(angle) * weight[None, :]).astype(jnp.bfloat16)


def sub_axes(n_blk, n_grp):
    return [
        ("blk", 2, 1, n_blk),
        ("blk", 4, 2, n_blk),
        ("blk", n_blk // 8, 8, n_blk),
        ("grp", n_grp, 1, n_grp),
    ]


def shift_perm(size, stride, total, k):
    pairs = []
    for i in range(total):
        c = (i // stride) % size
        pairs.append((i, i + ((c + k) % size - c) * stride))
    return pairs


def ring_sum(v, subs):
    for axis, size, stride, total in subs:
        parts = [lax.ppermute(v, axis, shift_perm(size, stride, total, k)) for k in range(1, size)]
        for part in parts:
            v = v + part
    return v


def body(sky_map, fg_templates, cycle_len, beam_profile, beam_index):
    n_blk = lax.axis_size("blk")
    n_grp = lax.axis_size("grp")
    cycle_dev = cycle_len.shape[0]
    n_chan = sky_map.shape[0]
    n_mode = fg_templates.shape[1]
    chan_dev = n_chan // n_blk
    m_width = M_DEV * n_grp
    n_cycle = cycle_dev * n_blk * n_grp
    slots = jnp.arange(RPIX, dtype=jnp.int32)
    valid = (slots[None, :] < cycle_len[:, None]).reshape(-1)
    masked = jnp.where(valid[None, :], sky_map, jnp.zeros((), jnp.bfloat16))
    mode_amps = jnp.dot(fg_templates.T, masked, preferred_element_type=jnp.float32).astype(
        jnp.bfloat16
    )
    gram_part = jnp.dot(mode_amps, mode_amps.T, preferred_element_type=jnp.float32)
    cross_part = lax.dot_general(
        mode_amps, masked, (((1,), (1,)), ((), ())), preferred_element_type=jnp.float32
    )
    amps_wide = mode_amps.astype(jnp.float32)
    subs = sub_axes(n_blk, n_grp)
    sums = ring_sum(jnp.concatenate([gram_part, cross_part], axis=1), subs)
    gram_sum = sums[:, :n_mode]
    cross_sum = sums[:, n_mode:]
    lower = jnp.linalg.cholesky(gram_sum)
    basis = jax.scipy.linalg.solve_triangular(lower, amps_wide, lower=True)
    projected = jax.scipy.linalg.solve_triangular(lower, cross_sum, lower=True)
    correction = jnp.dot(projected.T, basis, precision=lax.Precision.HIGHEST)
    cleaned = (masked.astype(jnp.float32) - correction).astype(jnp.bfloat16)
    received = []
    for local in range(cycle_dev):
        block = cleaned[:, local * RPIX : (local + 1) * RPIX]
        table = cycle_table(cycle_len[local], m_width)
        piece = jnp.dot(block, table, preferred_element_type=jnp.float32).astype(jnp.bfloat16)
        sendbuf = piece.reshape(n_blk, chan_dev, 2, n_grp, M_DEV).transpose(0, 3, 1, 2, 4)
        sendbuf = sendbuf.reshape(n_blk * n_grp, chan_dev, 2, M_DEV)
        received.append(lax.all_to_all(sendbuf, ("blk", "grp"), 0, 0, tiled=True))
    moved = jnp.stack(received, 0).reshape(n_cycle, chan_dev * 2 * M_DEV)
    position = jnp.arange(n_cycle, dtype=jnp.int32)
    n_dev = n_blk * n_grp
    theta_tab = theta_table(position % n_dev * cycle_dev + position // n_dev, n_cycle)
    harmonic = jnp.dot(theta_tab, moved, preferred_element_type=jnp.float32).reshape(
        L, chan_dev, 2, M_DEV
    )
    onehot = (
        beam_index[:, None] == jnp.arange(beam_profile.shape[0], dtype=jnp.int32)[None, :]
    ).astype(jnp.float32)
    profiles = jnp.dot(onehot, beam_profile, precision=lax.Precision.HIGHEST)
    shaped = harmonic * profiles.T[:, :, None, None]
    orders = lax.axis_index("grp") * M_DEV + jnp.arange(M_DEV, dtype=jnp.int32)
    mweight = 0.25 + orders.astype(jnp.float32) / m_width
    weighted = shaped * mweight[None, None, None, :]
    power_part = jnp.sum(weighted * weighted, axis=(0, 2, 3))
    power = ring_sum(power_part, subs[3:])
    return weighted * lax.rsqrt(power / (2.0 * L * m_width) + 1e-06)[None, :, None, None]


def solution(mesh):
    return jax.shard_map(
        body,
        mesh=mesh,
        in_specs=(P(None, ("blk", "grp")), P(), P(("blk", "grp")), P(), P("blk")),
        out_specs=P(None, "blk", None, "grp"),
        check_vma=False,
    )
```

```python
import jax
import jax.numpy as jnp
from jax import lax
from jax.sharding import PartitionSpec as P
from jax.experimental import pallas as pl
from jax.experimental.pallas import tpu as pltpu

RPIX = 2048
L = 1024
M_DEV = 256
J_LO = 128


def cos_sin_of_phase(phase, length):
    angle = jnp.pi * phase.astype(jnp.float32) / length.astype(jnp.float32)
    return jnp.cos(angle), jnp.sin(angle)


def add_angles(ca, sa, cb, sb):
    return ca * cb - sa * sb, sa * cb + ca * sb


def small_tables(cycle_len, m_width):
    length = cycle_len[:, None, None]
    period = 2 * length
    orders = jnp.arange(m_width, dtype=jnp.int32)[None, None, :]
    j_hi = jnp.arange(RPIX // J_LO, dtype=jnp.int32)[None, :, None]
    j_mid = jnp.arange(J_LO // 16, dtype=jnp.int32)[None, :, None]
    j_q = jnp.arange(16, dtype=jnp.int32)[None, :, None]
    ca, sa = cos_sin_of_phase((2 * J_LO * j_hi) % period * orders % period, length)
    cm, sm = cos_sin_of_phase((32 * j_mid) % period * orders % period, length)
    cq, sq = cos_sin_of_phase(orders * (2 * j_q + 1) % period, length)
    cb, sb = add_angles(cm[:, :, None, :], sm[:, :, None, :], cq[:, None, :, :], sq[:, None, :, :])
    n_cyc = cycle_len.shape[0]
    cb = cb.reshape(n_cyc, J_LO, m_width)
    sb = sb.reshape(n_cyc, J_LO, m_width)
    return ca, sa, cb, sb


def fourier_kernel(ca_ref, sa_ref, cb_ref, sb_ref, inv_ref, len_ref, x_ref, o_ref, tab_ref):
    m_width = cb_ref.shape[2]
    inv = inv_ref[0][:, 0:1]
    length = len_ref[0][:, 0:1]

    def build(t, carry):
        ca = ca_ref[0, pl.ds(t, 1), :]
        sa = sa_ref[0, pl.ds(t, 1), :]
        cb = cb_ref[0]
        sb = sb_ref[0]
        rows = t * J_LO + lax.broadcasted_iota(jnp.int32, (J_LO, 1), 0)
        weight = jnp.where(rows < length, inv, 0.0)
        cos_t, sin_t = add_angles(ca, sa, cb, sb)
        r0 = pl.multiple_of(t * J_LO, J_LO)
        tab_ref[pl.ds(r0, J_LO), 0:m_width] = (cos_t * weight).astype(jnp.bfloat16)
        tab_ref[pl.ds(r0, J_LO), m_width : 2 * m_width] = (-sin_t * weight).astype(jnp.bfloat16)
        return carry

    lax.fori_loop(0, RPIX // J_LO, build, 0)
    width = 2 * m_width
    step = 512
    for q in range(width // step):
        o_ref[0, :, q * step : (q + 1) * step] = jnp.dot(
            x_ref[...], tab_ref[:, q * step : (q + 1) * step], preferred_element_type=jnp.float32
        ).astype(jnp.bfloat16)


def cycle_fourier(cleaned, cycle_len, m_width):
    n_cyc = cycle_len.shape[0]
    n_chan = cleaned.shape[0]
    ca, sa, cb, sb = small_tables(cycle_len, m_width)
    inv = jnp.broadcast_to(lax.rsqrt(cycle_len.astype(jnp.float32))[:, None, None], (n_cyc, 1, 128))
    lens = jnp.broadcast_to(cycle_len[:, None, None], (n_cyc, 1, 128))
    n_hi = RPIX // J_LO
    return pl.pallas_call(
        fourier_kernel,
        grid=(n_cyc,),
        in_specs=[
            pl.BlockSpec((1, n_hi, m_width), lambda k: (k, 0, 0)),
            pl.BlockSpec((1, n_hi, m_width), lambda k: (k, 0, 0)),
            pl.BlockSpec((1, J_LO, m_width), lambda k: (k, 0, 0)),
            pl.BlockSpec((1, J_LO, m_width), lambda k: (k, 0, 0)),
            pl.BlockSpec((1, 1, 128), lambda k: (k, 0, 0)),
            pl.BlockSpec((1, 1, 128), lambda k: (k, 0, 0)),
            pl.BlockSpec((n_chan, RPIX), lambda k: (0, k)),
        ],
        out_specs=pl.BlockSpec((1, n_chan, 2 * m_width), lambda k: (k, 0, 0)),
        out_shape=jax.ShapeDtypeStruct((n_cyc, n_chan, 2 * m_width), jnp.bfloat16),
        scratch_shapes=[pltpu.VMEM((RPIX, 2 * m_width), jnp.bfloat16)],
        compiler_params=pltpu.CompilerParams(vmem_limit_bytes=48 * 1024 * 1024),
    )(ca, sa, cb, sb, inv, lens, cleaned)


def theta_table(cycle_ids, n_cycle):
    degrees = jnp.arange(L, dtype=jnp.int32)
    odd = 2 * cycle_ids + 1
    phase = degrees[:, None] * odd[None, :] % (4 * n_cycle)
    angle = jnp.pi * phase.astype(jnp.float32) / (2.0 * n_cycle)
    weight = jnp.sin(jnp.pi * odd.astype(jnp.float32) / (2.0 * n_cycle)) * (
        2.0 / jnp.sqrt(jnp.float32(n_cycle))
    )
    return (jnp.cos(angle) * weight[None, :]).astype(jnp.bfloat16)


def sub_axes(n_blk, n_grp):
    return [
        ("blk", 2, 1, n_blk),
        ("blk", 4, 2, n_blk),
        ("blk", n_blk // 8, 8, n_blk),
        ("grp", n_grp, 1, n_grp),
    ]


def shift_perm(size, stride, total, k):
    pairs = []
    for i in range(total):
        c = (i // stride) % size
        pairs.append((i, i + ((c + k) % size - c) * stride))
    return pairs


def ring_sum(v, subs):
    for axis, size, stride, total in subs:
        parts = [lax.ppermute(v, axis, shift_perm(size, stride, total, k)) for k in range(1, size)]
        for part in parts:
            v = v + part
    return v


def body(sky_map, fg_templates, cycle_len, beam_profile, beam_index):
    n_blk = lax.axis_size("blk")
    n_grp = lax.axis_size("grp")
    cycle_dev = cycle_len.shape[0]
    n_chan = sky_map.shape[0]
    n_mode = fg_templates.shape[1]
    chan_dev = n_chan // n_blk
    m_width = M_DEV * n_grp
    n_cycle = cycle_dev * n_blk * n_grp
    slots = jnp.arange(RPIX, dtype=jnp.int32)
    valid = (slots[None, :] < cycle_len[:, None]).reshape(-1)
    masked = jnp.where(valid[None, :], sky_map, jnp.zeros((), jnp.bfloat16))
    mode_amps = jnp.dot(fg_templates.T, masked, preferred_element_type=jnp.float32).astype(
        jnp.bfloat16
    )
    gram_part = jnp.dot(mode_amps, mode_amps.T, preferred_element_type=jnp.float32)
    cross_part = lax.dot_general(
        mode_amps, masked, (((1,), (1,)), ((), ())), preferred_element_type=jnp.float32
    )
    amps_wide = mode_amps.astype(jnp.float32)
    subs = sub_axes(n_blk, n_grp)
    sums = ring_sum(jnp.concatenate([gram_part, cross_part], axis=1), subs)
    gram_sum = sums[:, :n_mode]
    cross_sum = sums[:, n_mode:]
    lower = jnp.linalg.cholesky(gram_sum)
    basis = jax.scipy.linalg.solve_triangular(lower, amps_wide, lower=True)
    projected = jax.scipy.linalg.solve_triangular(lower, cross_sum, lower=True)
    correction = jnp.dot(projected.T, basis, precision=lax.Precision.HIGHEST)
    cleaned = (masked.astype(jnp.float32) - correction).astype(jnp.bfloat16)
    fourier = cycle_fourier(cleaned, cycle_len, m_width)
    fourier = fourier.reshape(cycle_dev, n_blk, chan_dev, 2, n_grp, M_DEV)
    sendbuf = fourier.transpose(1, 4, 0, 2, 3, 5).reshape(
        n_blk * n_grp, cycle_dev, chan_dev, 2, M_DEV
    )
    moved = lax.all_to_all(sendbuf, ("blk", "grp"), 0, 0, tiled=True)
    moved = moved.reshape(n_cycle, chan_dev * 2 * M_DEV)
    theta_tab = theta_table(jnp.arange(n_cycle, dtype=jnp.int32), n_cycle)
    harmonic = jnp.dot(theta_tab, moved, preferred_element_type=jnp.float32).reshape(
        L, chan_dev, 2, M_DEV
    )
    onehot = (
        beam_index[:, None] == jnp.arange(beam_profile.shape[0], dtype=jnp.int32)[None, :]
    ).astype(jnp.float32)
    profiles = jnp.dot(onehot, beam_profile, precision=lax.Precision.HIGHEST)
    shaped = harmonic * profiles.T[:, :, None, None]
    orders = lax.axis_index("grp") * M_DEV + jnp.arange(M_DEV, dtype=jnp.int32)
    mweight = 0.25 + orders.astype(jnp.float32) / m_width
    weighted = shaped * mweight[None, None, None, :]
    power_part = jnp.sum(weighted * weighted, axis=(0, 2, 3))
    power = ring_sum(power_part, subs[3:])
    return weighted * lax.rsqrt(power / (2.0 * L * m_width) + 1e-06)[None, :, None, None]


def solution(mesh):
    return jax.shard_map(
        body,
        mesh=mesh,
        in_specs=(P(None, ("blk", "grp")), P(), P(("blk", "grp")), P(), P("blk")),
        out_specs=P(None, "blk", None, "grp"),
        check_vma=False,
    )
```

```python
import jax
import jax.numpy as jnp
from jax import lax
from jax.sharding import PartitionSpec as P
from jax.experimental import pallas as pl
from jax.experimental.pallas import tpu as pltpu

RPIX = 2048
L = 1024
M_DEV = 256
J_LO = 128


def cos_sin_of_phase(phase, length):
    angle = jnp.pi * phase.astype(jnp.float32) / length.astype(jnp.float32)
    return jnp.cos(angle), jnp.sin(angle)


def add_angles(ca, sa, cb, sb):
    return ca * cb - sa * sb, sa * cb + ca * sb


def small_tables(cycle_len, m_width):
    length = cycle_len[:, None, None]
    period = 2 * length
    orders = jnp.arange(m_width, dtype=jnp.int32)[None, None, :]
    j_hi = jnp.arange(RPIX // J_LO, dtype=jnp.int32)[None, :, None]
    j_mid = jnp.arange(J_LO // 16, dtype=jnp.int32)[None, :, None]
    j_q = jnp.arange(16, dtype=jnp.int32)[None, :, None]
    ca, sa = cos_sin_of_phase((2 * J_LO * j_hi) % period * orders % period, length)
    cm, sm = cos_sin_of_phase((32 * j_mid) % period * orders % period, length)
    cq, sq = cos_sin_of_phase(orders * (2 * j_q + 1) % period, length)
    cb, sb = add_angles(cm[:, :, None, :], sm[:, :, None, :], cq[:, None, :, :], sq[:, None, :, :])
    n_cyc = cycle_len.shape[0]
    cb = cb.reshape(n_cyc, J_LO, m_width)
    sb = sb.reshape(n_cyc, J_LO, m_width)
    return ca, sa, cb, sb


def table_kernel(ca_ref, sa_ref, cb_ref, sb_ref, inv_ref, len_ref, tab_ref):
    t = pl.program_id(1)
    m_width = cb_ref.shape[2]
    inv = inv_ref[0][:, 0:1]
    length = len_ref[0][:, 0:1]
    ca = ca_ref[0, pl.ds(t, 1), :]
    sa = sa_ref[0, pl.ds(t, 1), :]
    cb = cb_ref[0]
    sb = sb_ref[0]
    rows = t * J_LO + lax.broadcasted_iota(jnp.int32, (J_LO, 1), 0)
    weight = jnp.where(rows < length, inv, 0.0)
    cos_t, sin_t = add_angles(ca, sa, cb, sb)
    tab_ref[0, :, 0:m_width] = (cos_t * weight).astype(jnp.bfloat16)
    tab_ref[0, :, m_width : 2 * m_width] = (-sin_t * weight).astype(jnp.bfloat16)


def matmul_kernel(x_ref, tab_ref, o_ref):
    o_ref[0] = jnp.dot(x_ref[...], tab_ref[0], preferred_element_type=jnp.float32).astype(
        jnp.bfloat16
    )


def cycle_tables(cycle_len, m_width):
    n_cyc = cycle_len.shape[0]
    ca, sa, cb, sb = small_tables(cycle_len, m_width)
    inv = jnp.broadcast_to(lax.rsqrt(cycle_len.astype(jnp.float32))[:, None, None], (n_cyc, 1, 128))
    lens = jnp.broadcast_to(cycle_len[:, None, None], (n_cyc, 1, 128))
    n_hi = RPIX // J_LO
    return pl.pallas_call(
        table_kernel,
        grid=(n_cyc, n_hi),
        in_specs=[
            pl.BlockSpec((1, n_hi, m_width), lambda k, t: (k, 0, 0)),
            pl.BlockSpec((1, n_hi, m_width), lambda k, t: (k, 0, 0)),
            pl.BlockSpec((1, J_LO, m_width), lambda k, t: (k, 0, 0)),
            pl.BlockSpec((1, J_LO, m_width), lambda k, t: (k, 0, 0)),
            pl.BlockSpec((1, 1, 128), lambda k, t: (k, 0, 0)),
            pl.BlockSpec((1, 1, 128), lambda k, t: (k, 0, 0)),
        ],
        out_specs=pl.BlockSpec((1, J_LO, 2 * m_width), lambda k, t: (k, t, 0)),
        out_shape=jax.ShapeDtypeStruct((n_cyc, RPIX, 2 * m_width), jnp.bfloat16),
    )(ca, sa, cb, sb, inv, lens)


def cycle_fourier(cleaned, tables):
    n_cyc = tables.shape[0]
    n_chan = cleaned.shape[0]
    width = tables.shape[2]
    step = 512
    return pl.pallas_call(
        matmul_kernel,
        grid=(n_cyc, width // step),
        in_specs=[
            pl.BlockSpec((n_chan, RPIX), lambda k, q: (0, k)),
            pl.BlockSpec((1, RPIX, step), lambda k, q: (k, 0, q)),
        ],
        out_specs=pl.BlockSpec((1, n_chan, step), lambda k, q: (k, 0, q)),
        out_shape=jax.ShapeDtypeStruct((n_cyc, n_chan, width), jnp.bfloat16),
        compiler_params=pltpu.CompilerParams(vmem_limit_bytes=32 * 1024 * 1024),
    )(cleaned, tables)


def theta_table(cycle_ids, n_cycle):
    degrees = jnp.arange(L, dtype=jnp.int32)
    odd = 2 * cycle_ids + 1
    phase = degrees[:, None] * odd[None, :] % (4 * n_cycle)
    angle = jnp.pi * phase.astype(jnp.float32) / (2.0 * n_cycle)
    weight = jnp.sin(jnp.pi * odd.astype(jnp.float32) / (2.0 * n_cycle)) * (
        2.0 / jnp.sqrt(jnp.float32(n_cycle))
    )
    return (jnp.cos(angle) * weight[None, :]).astype(jnp.bfloat16)


def sub_axes(n_blk, n_grp):
    return [
        ("blk", 2, 1, n_blk),
        ("blk", 4, 2, n_blk),
        ("blk", n_blk // 8, 8, n_blk),
        ("grp", n_grp, 1, n_grp),
    ]


def shift_perm(size, stride, total, k):
    pairs = []
    for i in range(total):
        c = (i // stride) % size
        pairs.append((i, i + ((c + k) % size - c) * stride))
    return pairs


def ring_sum(v, subs):
    for axis, size, stride, total in subs:
        parts = [lax.ppermute(v, axis, shift_perm(size, stride, total, k)) for k in range(1, size)]
        for part in parts:
            v = v + part
    return v


def body(sky_map, fg_templates, cycle_len, beam_profile, beam_index):
    n_blk = lax.axis_size("blk")
    n_grp = lax.axis_size("grp")
    cycle_dev = cycle_len.shape[0]
    n_chan = sky_map.shape[0]
    n_mode = fg_templates.shape[1]
    chan_dev = n_chan // n_blk
    m_width = M_DEV * n_grp
    n_cycle = cycle_dev * n_blk * n_grp
    slots = jnp.arange(RPIX, dtype=jnp.int32)
    valid = (slots[None, :] < cycle_len[:, None]).reshape(-1)
    masked = jnp.where(valid[None, :], sky_map, jnp.zeros((), jnp.bfloat16))
    mode_amps = jnp.dot(fg_templates.T, masked, preferred_element_type=jnp.float32).astype(
        jnp.bfloat16
    )
    gram_part = jnp.dot(mode_amps, mode_amps.T, preferred_element_type=jnp.float32)
    cross_part = lax.dot_general(
        mode_amps, masked, (((1,), (1,)), ((), ())), preferred_element_type=jnp.float32
    )
    amps_wide = mode_amps.astype(jnp.float32)
    tables = cycle_tables(cycle_len, m_width)
    subs = sub_axes(n_blk, n_grp)
    sums = ring_sum(jnp.concatenate([gram_part, cross_part], axis=1), subs)
    gram_sum = sums[:, :n_mode]
    cross_sum = sums[:, n_mode:]
    lower = jnp.linalg.cholesky(gram_sum)
    basis = jax.scipy.linalg.solve_triangular(lower, amps_wide, lower=True)
    projected = jax.scipy.linalg.solve_triangular(lower, cross_sum, lower=True)
    correction = jnp.dot(projected.T, basis, precision=lax.Precision.HIGHEST)
    cleaned = (masked.astype(jnp.float32) - correction).astype(jnp.bfloat16)
    fourier = cycle_fourier(cleaned, tables)
    fourier = fourier.reshape(cycle_dev, n_blk, chan_dev, 2, n_grp, M_DEV)
    sendbuf = fourier.transpose(1, 4, 0, 2, 3, 5).reshape(
        n_blk * n_grp, cycle_dev, chan_dev, 2, M_DEV
    )
    moved = lax.all_to_all(sendbuf, ("blk", "grp"), 0, 0, tiled=True)
    moved = moved.reshape(n_cycle, chan_dev * 2 * M_DEV)
    theta_tab = theta_table(jnp.arange(n_cycle, dtype=jnp.int32), n_cycle)
    harmonic = jnp.dot(theta_tab, moved, preferred_element_type=jnp.float32).reshape(
        L, chan_dev, 2, M_DEV
    )
    onehot = (
        beam_index[:, None] == jnp.arange(beam_profile.shape[0], dtype=jnp.int32)[None, :]
    ).astype(jnp.float32)
    profiles = jnp.dot(onehot, beam_profile, precision=lax.Precision.HIGHEST)
    shaped = harmonic * profiles.T[:, :, None, None]
    orders = lax.axis_index("grp") * M_DEV + jnp.arange(M_DEV, dtype=jnp.int32)
    mweight = 0.25 + orders.astype(jnp.float32) / m_width
    weighted = shaped * mweight[None, None, None, :]
    power_part = jnp.sum(weighted * weighted, axis=(0, 2, 3))
    power = ring_sum(power_part, subs[3:])
    return weighted * lax.rsqrt(power / (2.0 * L * m_width) + 1e-06)[None, :, None, None]


def solution(mesh):
    return jax.shard_map(
        body,
        mesh=mesh,
        in_specs=(P(None, ("blk", "grp")), P(), P(("blk", "grp")), P(), P("blk")),
        out_specs=P(None, "blk", None, "grp"),
        check_vma=False,
    )
```

```python
import jax
import jax.numpy as jnp
from jax import lax
from jax.sharding import PartitionSpec as P
from jax.experimental import pallas as pl
from jax.experimental.pallas import tpu as pltpu

RPIX = 2048
L = 1024
M_DEV = 256
J_LO = 128


def cos_sin_of_phase(phase, length):
    angle = jnp.pi * phase.astype(jnp.float32) / length.astype(jnp.float32)
    return jnp.cos(angle), jnp.sin(angle)


def add_angles(ca, sa, cb, sb):
    return ca * cb - sa * sb, sa * cb + ca * sb


def small_tables(cycle_len, m_width):
    length = cycle_len[:, None, None]
    period = 2 * length
    orders = jnp.arange(m_width, dtype=jnp.int32)[None, None, :]
    j_hi = jnp.arange(RPIX // J_LO, dtype=jnp.int32)[None, :, None]
    j_mid = jnp.arange(J_LO // 16, dtype=jnp.int32)[None, :, None]
    j_q = jnp.arange(16, dtype=jnp.int32)[None, :, None]
    ca, sa = cos_sin_of_phase((2 * J_LO * j_hi) % period * orders % period, length)
    cm, sm = cos_sin_of_phase((32 * j_mid) % period * orders % period, length)
    cq, sq = cos_sin_of_phase(orders * (2 * j_q + 1) % period, length)
    cb, sb = add_angles(cm[:, :, None, :], sm[:, :, None, :], cq[:, None, :, :], sq[:, None, :, :])
    n_cyc = cycle_len.shape[0]
    cb = cb.reshape(n_cyc, J_LO, m_width)
    sb = sb.reshape(n_cyc, J_LO, m_width)
    return ca, sa, cb, sb


def fourier_kernel(ca_ref, sa_ref, cb_ref, sb_ref, inv_ref, len_ref, x_ref, o_ref, tab_ref):
    m_width = cb_ref.shape[2]
    inv = inv_ref[0][:, 0:1]
    length = len_ref[0][:, 0:1]

    def build(t, carry):
        ca = ca_ref[0, pl.ds(t, 1), :]
        sa = sa_ref[0, pl.ds(t, 1), :]
        cb = cb_ref[0]
        sb = sb_ref[0]
        rows = t * J_LO + lax.broadcasted_iota(jnp.int32, (J_LO, 1), 0)
        weight = jnp.where(rows < length, inv, 0.0)
        cos_t, sin_t = add_angles(ca, sa, cb, sb)
        r0 = pl.multiple_of(t * J_LO, J_LO)
        tab_ref[pl.ds(r0, J_LO), 0:m_width] = (cos_t * weight).astype(jnp.bfloat16)
        tab_ref[pl.ds(r0, J_LO), m_width : 2 * m_width] = (-sin_t * weight).astype(jnp.bfloat16)
        return carry

    lax.fori_loop(0, RPIX // J_LO, build, 0)
    width = 2 * m_width
    step = 512
    for q in range(width // step):
        o_ref[0, :, q * step : (q + 1) * step] = jnp.dot(
            x_ref[...], tab_ref[:, q * step : (q + 1) * step], preferred_element_type=jnp.float32
        ).astype(jnp.bfloat16)


def cycle_fourier(cleaned, cycle_len, m_width):
    n_cyc = cycle_len.shape[0]
    n_chan = cleaned.shape[0]
    ca, sa, cb, sb = small_tables(cycle_len, m_width)
    inv = jnp.broadcast_to(lax.rsqrt(cycle_len.astype(jnp.float32))[:, None, None], (n_cyc, 1, 128))
    lens = jnp.broadcast_to(cycle_len[:, None, None], (n_cyc, 1, 128))
    n_hi = RPIX // J_LO
    return pl.pallas_call(
        fourier_kernel,
        grid=(n_cyc,),
        in_specs=[
            pl.BlockSpec((1, n_hi, m_width), lambda k: (k, 0, 0)),
            pl.BlockSpec((1, n_hi, m_width), lambda k: (k, 0, 0)),
            pl.BlockSpec((1, J_LO, m_width), lambda k: (k, 0, 0)),
            pl.BlockSpec((1, J_LO, m_width), lambda k: (k, 0, 0)),
            pl.BlockSpec((1, 1, 128), lambda k: (k, 0, 0)),
            pl.BlockSpec((1, 1, 128), lambda k: (k, 0, 0)),
            pl.BlockSpec((n_chan, RPIX), lambda k: (0, k)),
        ],
        out_specs=pl.BlockSpec((1, n_chan, 2 * m_width), lambda k: (k, 0, 0)),
        out_shape=jax.ShapeDtypeStruct((n_cyc, n_chan, 2 * m_width), jnp.bfloat16),
        scratch_shapes=[pltpu.VMEM((RPIX, 2 * m_width), jnp.bfloat16)],
        compiler_params=pltpu.CompilerParams(vmem_limit_bytes=48 * 1024 * 1024),
    )(ca, sa, cb, sb, inv, lens, cleaned)


def harmonic_tile(theta_ref, mv_ref, prof_ref, mw_ref, lc):
    rows = pl.ds(lc * 256, 256)
    h = jnp.dot(theta_ref[rows, :], mv_ref[...], preferred_element_type=jnp.float32)
    return h * prof_ref[0, rows, :] * mw_ref[...]


def power_kernel(theta_ref, mv_ref, prof_ref, mw_ref, o_ref):
    total = jnp.zeros((1, 1), jnp.float32)
    for lc in range(theta_ref.shape[0] // 256):
        w = harmonic_tile(theta_ref, mv_ref, prof_ref, mw_ref, lc)
        total = total + jnp.sum(w * w, keepdims=True)
    o_ref[0] = jnp.broadcast_to(total, (1, 128))


def output_kernel(theta_ref, mv_ref, prof_ref, mw_ref, scale_ref, o_ref):
    scale = scale_ref[0][:, 0:1]
    half = mv_ref.shape[1] // 2
    for lc in range(theta_ref.shape[0] // 256):
        w = harmonic_tile(theta_ref, mv_ref, prof_ref, mw_ref, lc) * scale
        for p in range(2):
            o_ref[pl.ds(lc * 256, 256), 0, p, :] = w[:, p * half : (p + 1) * half]


def harmonic_specs(n_l, n_cycle, width):
    return [
        pl.BlockSpec((n_l, n_cycle), lambda c: (0, 0)),
        pl.BlockSpec((n_cycle, width), lambda c: (0, c)),
        pl.BlockSpec((1, n_l, 1), lambda c: (c, 0, 0)),
        pl.BlockSpec((1, width), lambda c: (0, 0)),
    ]


def theta_table(cycle_ids, n_cycle):
    degrees = jnp.arange(L, dtype=jnp.int32)
    odd = 2 * cycle_ids + 1
    phase = degrees[:, None] * odd[None, :] % (4 * n_cycle)
    angle = jnp.pi * phase.astype(jnp.float32) / (2.0 * n_cycle)
    weight = jnp.sin(jnp.pi * odd.astype(jnp.float32) / (2.0 * n_cycle)) * (
        2.0 / jnp.sqrt(jnp.float32(n_cycle))
    )
    return (jnp.cos(angle) * weight[None, :]).astype(jnp.bfloat16)


def sub_axes(n_blk, n_grp):
    return [
        ("blk", 2, 1, n_blk),
        ("blk", 4, 2, n_blk),
        ("blk", n_blk // 8, 8, n_blk),
        ("grp", n_grp, 1, n_grp),
    ]


def shift_perm(size, stride, total, k):
    pairs = []
    for i in range(total):
        c = (i // stride) % size
        pairs.append((i, i + ((c + k) % size - c) * stride))
    return pairs


def ring_sum(v, subs):
    for axis, size, stride, total in subs:
        parts = [lax.ppermute(v, axis, shift_perm(size, stride, total, k)) for k in range(1, size)]
        for part in parts:
            v = v + part
    return v


def body(sky_map, fg_templates, cycle_len, beam_profile, beam_index):
    n_blk = lax.axis_size("blk")
    n_grp = lax.axis_size("grp")
    cycle_dev = cycle_len.shape[0]
    n_chan = sky_map.shape[0]
    n_mode = fg_templates.shape[1]
    chan_dev = n_chan // n_blk
    m_width = M_DEV * n_grp
    n_cycle = cycle_dev * n_blk * n_grp
    slots = jnp.arange(RPIX, dtype=jnp.int32)
    valid = (slots[None, :] < cycle_len[:, None]).reshape(-1)
    masked = jnp.where(valid[None, :], sky_map, jnp.zeros((), jnp.bfloat16))
    mode_amps = jnp.dot(fg_templates.T, masked, preferred_element_type=jnp.float32).astype(
        jnp.bfloat16
    )
    gram_part = jnp.dot(mode_amps, mode_amps.T, preferred_element_type=jnp.float32)
    cross_part = lax.dot_general(
        mode_amps, masked, (((1,), (1,)), ((), ())), preferred_element_type=jnp.float32
    )
    amps_wide = mode_amps.astype(jnp.float32)
    subs = sub_axes(n_blk, n_grp)
    sums = ring_sum(jnp.concatenate([gram_part, cross_part], axis=1), subs)
    gram_sum = sums[:, :n_mode]
    cross_sum = sums[:, n_mode:]
    lower = jnp.linalg.cholesky(gram_sum)
    basis = jax.scipy.linalg.solve_triangular(lower, amps_wide, lower=True)
    projected = jax.scipy.linalg.solve_triangular(lower, cross_sum, lower=True)
    correction = jnp.dot(projected.T, basis, precision=lax.Precision.HIGHEST)
    cleaned = (masked.astype(jnp.float32) - correction).astype(jnp.bfloat16)
    fourier = cycle_fourier(cleaned, cycle_len, m_width)
    fourier = fourier.reshape(cycle_dev, n_blk, chan_dev, 2, n_grp, M_DEV)
    sendbuf = fourier.transpose(1, 4, 0, 2, 3, 5).reshape(
        n_blk * n_grp, cycle_dev, chan_dev, 2, M_DEV
    )
    moved = lax.all_to_all(sendbuf, ("blk", "grp"), 0, 0, tiled=True)
    moved = moved.reshape(n_cycle, chan_dev * 2 * M_DEV)
    theta_tab = theta_table(jnp.arange(n_cycle, dtype=jnp.int32), n_cycle)
    onehot = (
        beam_index[:, None] == jnp.arange(beam_profile.shape[0], dtype=jnp.int32)[None, :]
    ).astype(jnp.float32)
    profiles = jnp.dot(onehot, beam_profile, precision=lax.Precision.HIGHEST)
    orders = lax.axis_index("grp") * M_DEV + jnp.arange(M_DEV, dtype=jnp.int32)
    mweight = 0.25 + orders.astype(jnp.float32) / m_width
    mw_row = jnp.concatenate([mweight, mweight])[None, :]
    prof_col = profiles[:, :, None]
    width = 2 * M_DEV
    specs = harmonic_specs(L, n_cycle, width)
    vmem = pltpu.CompilerParams(vmem_limit_bytes=32 * 1024 * 1024)
    power_part = pl.pallas_call(
        power_kernel,
        grid=(chan_dev,),
        in_specs=specs,
        out_specs=pl.BlockSpec((1, 1, 128), lambda c: (c, 0, 0)),
        out_shape=jax.ShapeDtypeStruct((chan_dev, 1, 128), jnp.float32),
        compiler_params=vmem,
    )(theta_tab, moved, prof_col, mw_row)[:, 0, 0]
    power = ring_sum(power_part, subs[3:])
    scale = lax.rsqrt(power / (2.0 * L * m_width) + 1e-06)
    scale = jnp.broadcast_to(scale[:, None, None], (chan_dev, 1, 128))
    return pl.pallas_call(
        output_kernel,
        grid=(chan_dev,),
        in_specs=specs + [pl.BlockSpec((1, 1, 128), lambda c: (c, 0, 0))],
        out_specs=pl.BlockSpec((L, 1, 2, M_DEV), lambda c: (0, c, 0, 0)),
        out_shape=jax.ShapeDtypeStruct((L, chan_dev, 2, M_DEV), jnp.float32),
        compiler_params=vmem,
    )(theta_tab, moved, prof_col, mw_row, scale)


def solution(mesh):
    return jax.shard_map(
        body,
        mesh=mesh,
        in_specs=(P(None, ("blk", "grp")), P(), P(("blk", "grp")), P(), P("blk")),
        out_specs=P(None, "blk", None, "grp"),
        check_vma=False,
    )
```

```python
import jax
import jax.numpy as jnp
from jax import lax
from jax.sharding import PartitionSpec as P
from jax.experimental import pallas as pl
from jax.experimental.pallas import tpu as pltpu

RPIX = 2048
L = 1024
M_DEV = 256
J_LO = 128


def cos_sin_of_phase(phase, length):
    angle = jnp.pi * phase.astype(jnp.float32) / length.astype(jnp.float32)
    return jnp.cos(angle), jnp.sin(angle)


def add_angles(ca, sa, cb, sb):
    return ca * cb - sa * sb, sa * cb + ca * sb


def small_tables(cycle_len, m_width):
    length = cycle_len[:, None, None]
    period = 2 * length
    orders = jnp.arange(m_width, dtype=jnp.int32)[None, None, :]
    j_hi = jnp.arange(RPIX // J_LO, dtype=jnp.int32)[None, :, None]
    j_mid = jnp.arange(J_LO // 16, dtype=jnp.int32)[None, :, None]
    j_q = jnp.arange(16, dtype=jnp.int32)[None, :, None]
    ca, sa = cos_sin_of_phase((2 * J_LO * j_hi) % period * orders % period, length)
    cm, sm = cos_sin_of_phase((32 * j_mid) % period * orders % period, length)
    cq, sq = cos_sin_of_phase(orders * (2 * j_q + 1) % period, length)
    cb, sb = add_angles(cm[:, :, None, :], sm[:, :, None, :], cq[:, None, :, :], sq[:, None, :, :])
    n_cyc = cycle_len.shape[0]
    cb = cb.reshape(n_cyc, J_LO, m_width)
    sb = sb.reshape(n_cyc, J_LO, m_width)
    return ca, sa, cb, sb


def fourier_kernel(
    ca_ref, sa_ref, cb_ref, sb_ref, inv_ref, len_ref, sky_ref, proj_ref, basis_ref, o_ref,
    tab_ref, clean_ref,
):
    m_width = cb_ref.shape[2]
    n_grp = o_ref.shape[0] // (sky_ref.shape[0] // o_ref.shape[1])
    chan_dev = o_ref.shape[1]
    inv = inv_ref[0][:, 0:1]
    length = len_ref[0][:, 0:1]

    def build(t, carry):
        ca = ca_ref[0, pl.ds(t, 1), :]
        sa = sa_ref[0, pl.ds(t, 1), :]
        cb = cb_ref[0]
        sb = sb_ref[0]
        rows = t * J_LO + lax.broadcasted_iota(jnp.int32, (J_LO, 1), 0)
        weight = jnp.where(rows < length, inv, 0.0)
        cos_t, sin_t = add_angles(ca, sa, cb, sb)
        r0 = pl.multiple_of(t * J_LO, J_LO)
        tab_ref[pl.ds(r0, J_LO), 0:m_width] = (cos_t * weight).astype(jnp.bfloat16)
        tab_ref[pl.ds(r0, J_LO), m_width : 2 * m_width] = (-sin_t * weight).astype(jnp.bfloat16)
        return carry

    lax.fori_loop(0, RPIX // J_LO, build, 0)
    cols = lax.broadcasted_iota(jnp.int32, (1, RPIX), 1)
    masked = jnp.where(cols < length, sky_ref[...].astype(jnp.float32), 0.0)
    correction = jnp.dot(
        proj_ref[...], basis_ref[...], preferred_element_type=jnp.float32,
        precision=lax.Precision.HIGHEST,
    )
    clean_ref[...] = (masked - correction).astype(jnp.bfloat16)
    m_dev = m_width // n_grp
    step = 2 * m_dev
    n_blk = sky_ref.shape[0] // chan_dev
    for q in range(2 * m_width // step):
        res = jnp.dot(
            clean_ref[...], tab_ref[:, q * step : (q + 1) * step], preferred_element_type=jnp.float32
        )
        part = (q * step) // m_width
        for h in range(step // m_dev):
            grp_dest = (q * step - part * m_width) // m_dev + h
            for blk_dest in range(n_blk):
                slab = res[blk_dest * chan_dev : (blk_dest + 1) * chan_dev, h * m_dev : (h + 1) * m_dev]
                o_ref[blk_dest * n_grp + grp_dest, :, part * m_dev : (part + 1) * m_dev] = slab.astype(
                    jnp.bfloat16
                )


def cycle_fourier(sky_map, projected_t, basis, cycle_len, m_width, n_blk, n_grp):
    n_cyc = cycle_len.shape[0]
    n_chan = sky_map.shape[0]
    n_mode = basis.shape[0]
    n_dev = n_blk * n_grp
    chan_dev = n_chan // n_blk
    ca, sa, cb, sb = small_tables(cycle_len, m_width)
    inv = jnp.broadcast_to(lax.rsqrt(cycle_len.astype(jnp.float32))[:, None, None], (n_cyc, 1, 128))
    lens = jnp.broadcast_to(cycle_len[:, None, None], (n_cyc, 1, 128))
    n_hi = RPIX // J_LO
    m_dev = m_width // n_grp
    return pl.pallas_call(
        fourier_kernel,
        grid=(n_cyc,),
        in_specs=[
            pl.BlockSpec((1, n_hi, m_width), lambda k: (k, 0, 0)),
            pl.BlockSpec((1, n_hi, m_width), lambda k: (k, 0, 0)),
            pl.BlockSpec((1, J_LO, m_width), lambda k: (k, 0, 0)),
            pl.BlockSpec((1, J_LO, m_width), lambda k: (k, 0, 0)),
            pl.BlockSpec((1, 1, 128), lambda k: (k, 0, 0)),
            pl.BlockSpec((1, 1, 128), lambda k: (k, 0, 0)),
            pl.BlockSpec((n_chan, RPIX), lambda k: (0, k)),
            pl.BlockSpec((n_chan, n_mode), lambda k: (0, 0)),
            pl.BlockSpec((n_mode, RPIX), lambda k: (0, k)),
        ],
        out_specs=pl.BlockSpec((n_dev, None, chan_dev, 2 * m_dev), lambda k: (0, k, 0, 0)),
        out_shape=jax.ShapeDtypeStruct((n_dev, n_cyc, chan_dev, 2 * m_dev), jnp.bfloat16),
        scratch_shapes=[
            pltpu.VMEM((RPIX, 2 * m_width), jnp.bfloat16),
            pltpu.VMEM((n_chan, RPIX), jnp.bfloat16),
        ],
        compiler_params=pltpu.CompilerParams(vmem_limit_bytes=48 * 1024 * 1024),
    )(ca, sa, cb, sb, inv, lens, sky_map, projected_t, basis)


def harmonic_tile(theta_ref, mv_ref, prof_ref, mw_ref, lc):
    rows = pl.ds(lc * 256, 256)
    h = jnp.dot(theta_ref[rows, :], mv_ref[...], preferred_element_type=jnp.float32)
    return h * prof_ref[0, rows, :] * mw_ref[...]


def power_kernel(theta_ref, mv_ref, prof_ref, mw_ref, o_ref):
    total = jnp.zeros((1, 1), jnp.float32)
    for lc in range(theta_ref.shape[0] // 256):
        w = harmonic_tile(theta_ref, mv_ref, prof_ref, mw_ref, lc)
        total = total + jnp.sum(w * w, keepdims=True)
    o_ref[0] = jnp.broadcast_to(total, (1, 128))


def output_kernel(theta_ref, mv_ref, prof_ref, mw_ref, scale_ref, o_ref):
    scale = scale_ref[0][:, 0:1]
    half = mv_ref.shape[1] // 2
    for lc in range(theta_ref.shape[0] // 256):
        w = harmonic_tile(theta_ref, mv_ref, prof_ref, mw_ref, lc) * scale
        for p in range(2):
            o_ref[pl.ds(lc * 256, 256), 0, p, :] = w[:, p * half : (p + 1) * half]


def harmonic_specs(n_l, n_cycle, width):
    return [
        pl.BlockSpec((n_l, n_cycle), lambda c: (0, 0)),
        pl.BlockSpec((n_cycle, width), lambda c: (0, c)),
        pl.BlockSpec((1, n_l, 1), lambda c: (c, 0, 0)),
        pl.BlockSpec((1, width), lambda c: (0, 0)),
    ]


def theta_table(cycle_ids, n_cycle):
    degrees = jnp.arange(L, dtype=jnp.int32)
    odd = 2 * cycle_ids + 1
    phase = degrees[:, None] * odd[None, :] % (4 * n_cycle)
    angle = jnp.pi * phase.astype(jnp.float32) / (2.0 * n_cycle)
    weight = jnp.sin(jnp.pi * odd.astype(jnp.float32) / (2.0 * n_cycle)) * (
        2.0 / jnp.sqrt(jnp.float32(n_cycle))
    )
    return (jnp.cos(angle) * weight[None, :]).astype(jnp.bfloat16)


def sub_axes(n_blk, n_grp):
    return [
        ("blk", 2, 1, n_blk),
        ("blk", 4, 2, n_blk),
        ("blk", n_blk // 8, 8, n_blk),
        ("grp", n_grp, 1, n_grp),
    ]


def shift_perm(size, stride, total, k):
    pairs = []
    for i in range(total):
        c = (i // stride) % size
        pairs.append((i, i + ((c + k) % size - c) * stride))
    return pairs


def ring_sum(v, subs):
    for axis, size, stride, total in subs:
        parts = [lax.ppermute(v, axis, shift_perm(size, stride, total, k)) for k in range(1, size)]
        for part in parts:
            v = v + part
    return v


def body(sky_map, fg_templates, cycle_len, beam_profile, beam_index):
    n_blk = lax.axis_size("blk")
    n_grp = lax.axis_size("grp")
    cycle_dev = cycle_len.shape[0]
    n_chan = sky_map.shape[0]
    n_mode = fg_templates.shape[1]
    chan_dev = n_chan // n_blk
    m_width = M_DEV * n_grp
    n_cycle = cycle_dev * n_blk * n_grp
    slots = jnp.arange(RPIX, dtype=jnp.int32)
    valid = (slots[None, :] < cycle_len[:, None]).reshape(-1)
    masked = jnp.where(valid[None, :], sky_map, jnp.zeros((), jnp.bfloat16))
    mode_amps = jnp.dot(fg_templates.T, masked, preferred_element_type=jnp.float32).astype(
        jnp.bfloat16
    )
    gram_part = jnp.dot(mode_amps, mode_amps.T, preferred_element_type=jnp.float32)
    cross_part = lax.dot_general(
        mode_amps, masked, (((1,), (1,)), ((), ())), preferred_element_type=jnp.float32
    )
    amps_wide = mode_amps.astype(jnp.float32)
    subs = sub_axes(n_blk, n_grp)
    sums = ring_sum(jnp.concatenate([gram_part, cross_part], axis=1), subs)
    gram_sum = sums[:, :n_mode]
    cross_sum = sums[:, n_mode:]
    lower = jnp.linalg.cholesky(gram_sum)
    basis = jax.scipy.linalg.solve_triangular(lower, amps_wide, lower=True)
    projected = jax.scipy.linalg.solve_triangular(lower, cross_sum, lower=True)
    sendbuf = cycle_fourier(sky_map, projected.T, basis, cycle_len, m_width, n_blk, n_grp)
    moved = lax.all_to_all(sendbuf, ("blk", "grp"), 0, 0, tiled=True)
    moved = moved.reshape(n_cycle, chan_dev * 2 * M_DEV)
    theta_tab = theta_table(jnp.arange(n_cycle, dtype=jnp.int32), n_cycle)
    onehot = (
        beam_index[:, None] == jnp.arange(beam_profile.shape[0], dtype=jnp.int32)[None, :]
    ).astype(jnp.float32)
    profiles = jnp.dot(onehot, beam_profile, precision=lax.Precision.HIGHEST)
    orders = lax.axis_index("grp") * M_DEV + jnp.arange(M_DEV, dtype=jnp.int32)
    mweight = 0.25 + orders.astype(jnp.float32) / m_width
    mw_row = jnp.concatenate([mweight, mweight])[None, :]
    prof_col = profiles[:, :, None]
    width = 2 * M_DEV
    specs = harmonic_specs(L, n_cycle, width)
    vmem = pltpu.CompilerParams(vmem_limit_bytes=32 * 1024 * 1024)
    power_part = pl.pallas_call(
        power_kernel,
        grid=(chan_dev,),
        in_specs=specs,
        out_specs=pl.BlockSpec((1, 1, 128), lambda c: (c, 0, 0)),
        out_shape=jax.ShapeDtypeStruct((chan_dev, 1, 128), jnp.float32),
        compiler_params=vmem,
    )(theta_tab, moved, prof_col, mw_row)[:, 0, 0]
    power = ring_sum(power_part, subs[3:])
    scale = lax.rsqrt(power / (2.0 * L * m_width) + 1e-06)
    scale = jnp.broadcast_to(scale[:, None, None], (chan_dev, 1, 128))
    return pl.pallas_call(
        output_kernel,
        grid=(chan_dev,),
        in_specs=specs + [pl.BlockSpec((1, 1, 128), lambda c: (c, 0, 0))],
        out_specs=pl.BlockSpec((L, 1, 2, M_DEV), lambda c: (0, c, 0, 0)),
        out_shape=jax.ShapeDtypeStruct((L, chan_dev, 2, M_DEV), jnp.float32),
        compiler_params=vmem,
    )(theta_tab, moved, prof_col, mw_row, scale)


def solution(mesh):
    return jax.shard_map(
        body,
        mesh=mesh,
        in_specs=(P(None, ("blk", "grp")), P(), P(("blk", "grp")), P(), P("blk")),
        out_specs=P(None, "blk", None, "grp"),
        check_vma=False,
    )
```

```python
import jax
import jax.numpy as jnp
from jax import lax
from jax.sharding import PartitionSpec as P
from jax.experimental import pallas as pl
from jax.experimental.pallas import tpu as pltpu

RPIX = 2048
L = 1024
M_DEV = 256
J_LO = 128


def cos_sin_of_phase(phase, length):
    angle = jnp.pi * phase.astype(jnp.float32) / length.astype(jnp.float32)
    return jnp.cos(angle), jnp.sin(angle)


def add_angles(ca, sa, cb, sb):
    return ca * cb - sa * sb, sa * cb + ca * sb


def small_tables(cycle_len, m_width):
    length = cycle_len[:, None, None]
    period = 2 * length
    orders = jnp.arange(m_width, dtype=jnp.int32)[None, None, :]
    j_hi = jnp.arange(RPIX // J_LO, dtype=jnp.int32)[None, :, None]
    j_mid = jnp.arange(J_LO // 16, dtype=jnp.int32)[None, :, None]
    j_q = jnp.arange(16, dtype=jnp.int32)[None, :, None]
    ca, sa = cos_sin_of_phase((2 * J_LO * j_hi) % period * orders % period, length)
    cm, sm = cos_sin_of_phase((32 * j_mid) % period * orders % period, length)
    cq, sq = cos_sin_of_phase(orders * (2 * j_q + 1) % period, length)
    cb, sb = add_angles(cm[:, :, None, :], sm[:, :, None, :], cq[:, None, :, :], sq[:, None, :, :])
    n_cyc = cycle_len.shape[0]
    cb = cb.reshape(n_cyc, J_LO, m_width)
    sb = sb.reshape(n_cyc, J_LO, m_width)
    return ca, sa, cb, sb


def table_kernel(ca_ref, sa_ref, cb_ref, sb_ref, inv_ref, len_ref, tab_ref):
    m_width = cb_ref.shape[2]
    inv = inv_ref[0][:, 0:1]
    length = len_ref[0][:, 0:1]

    def build(t, carry):
        ca = ca_ref[0, pl.ds(t, 1), :]
        sa = sa_ref[0, pl.ds(t, 1), :]
        cb = cb_ref[0]
        sb = sb_ref[0]
        rows = t * J_LO + lax.broadcasted_iota(jnp.int32, (J_LO, 1), 0)
        weight = jnp.where(rows < length, inv, 0.0)
        cos_t, sin_t = add_angles(ca, sa, cb, sb)
        r0 = pl.multiple_of(t * J_LO, J_LO)
        tab_ref[0, pl.ds(r0, J_LO), 0:m_width] = (cos_t * weight).astype(jnp.bfloat16)
        tab_ref[0, pl.ds(r0, J_LO), m_width : 2 * m_width] = (-sin_t * weight).astype(jnp.bfloat16)
        return carry

    lax.fori_loop(0, RPIX // J_LO, build, 0)


def cycle_tables(cycle_len, m_width):
    n_cyc = cycle_len.shape[0]
    ca, sa, cb, sb = small_tables(cycle_len, m_width)
    inv = jnp.broadcast_to(lax.rsqrt(cycle_len.astype(jnp.float32))[:, None, None], (n_cyc, 1, 128))
    lens = jnp.broadcast_to(cycle_len[:, None, None], (n_cyc, 1, 128))
    n_hi = RPIX // J_LO
    return pl.pallas_call(
        table_kernel,
        grid=(n_cyc,),
        in_specs=[
            pl.BlockSpec((1, n_hi, m_width), lambda k: (k, 0, 0)),
            pl.BlockSpec((1, n_hi, m_width), lambda k: (k, 0, 0)),
            pl.BlockSpec((1, J_LO, m_width), lambda k: (k, 0, 0)),
            pl.BlockSpec((1, J_LO, m_width), lambda k: (k, 0, 0)),
            pl.BlockSpec((1, 1, 128), lambda k: (k, 0, 0)),
            pl.BlockSpec((1, 1, 128), lambda k: (k, 0, 0)),
        ],
        out_specs=pl.BlockSpec((1, RPIX, 2 * m_width), lambda k: (k, 0, 0)),
        out_shape=jax.ShapeDtypeStruct((n_cyc, RPIX, 2 * m_width), jnp.bfloat16),
        compiler_params=pltpu.CompilerParams(vmem_limit_bytes=40 * 1024 * 1024),
    )(ca, sa, cb, sb, inv, lens)


def fourier_kernel(len_ref, sky_ref, proj_ref, basis_ref, tab_ref, o_ref, clean_ref):
    m_width = tab_ref.shape[2] // 2
    n_grp = o_ref.shape[0] // (sky_ref.shape[0] // o_ref.shape[1])
    chan_dev = o_ref.shape[1]
    length = len_ref[0][:, 0:1]
    cols = lax.broadcasted_iota(jnp.int32, (1, RPIX), 1)
    masked = jnp.where(cols < length, sky_ref[...].astype(jnp.float32), 0.0)
    correction = jnp.dot(
        proj_ref[...], basis_ref[...], preferred_element_type=jnp.float32,
        precision=lax.Precision.HIGHEST,
    )
    clean_ref[...] = (masked - correction).astype(jnp.bfloat16)
    m_dev = m_width // n_grp
    step = 2 * m_dev
    n_blk = sky_ref.shape[0] // chan_dev
    for q in range(2 * m_width // step):
        res = jnp.dot(
            clean_ref[...], tab_ref[0, :, q * step : (q + 1) * step], preferred_element_type=jnp.float32
        )
        part = (q * step) // m_width
        for h in range(step // m_dev):
            grp_dest = (q * step - part * m_width) // m_dev + h
            for blk_dest in range(n_blk):
                slab = res[blk_dest * chan_dev : (blk_dest + 1) * chan_dev, h * m_dev : (h + 1) * m_dev]
                o_ref[blk_dest * n_grp + grp_dest, :, part * m_dev : (part + 1) * m_dev] = slab.astype(
                    jnp.bfloat16
                )


def cycle_fourier(sky_map, projected_t, basis, tables, cycle_len, n_blk, n_grp):
    n_cyc = cycle_len.shape[0]
    n_chan = sky_map.shape[0]
    n_mode = basis.shape[0]
    n_dev = n_blk * n_grp
    chan_dev = n_chan // n_blk
    width = tables.shape[2]
    lens = jnp.broadcast_to(cycle_len[:, None, None], (n_cyc, 1, 128))
    m_dev = width // 2 // n_grp
    return pl.pallas_call(
        fourier_kernel,
        grid=(n_cyc,),
        in_specs=[
            pl.BlockSpec((1, 1, 128), lambda k: (k, 0, 0)),
            pl.BlockSpec((n_chan, RPIX), lambda k: (0, k)),
            pl.BlockSpec((n_chan, n_mode), lambda k: (0, 0)),
            pl.BlockSpec((n_mode, RPIX), lambda k: (0, k)),
            pl.BlockSpec((1, RPIX, width), lambda k: (k, 0, 0)),
        ],
        out_specs=pl.BlockSpec((n_dev, None, chan_dev, 2 * m_dev), lambda k: (0, k, 0, 0)),
        out_shape=jax.ShapeDtypeStruct((n_dev, n_cyc, chan_dev, 2 * m_dev), jnp.bfloat16),
        scratch_shapes=[pltpu.VMEM((n_chan, RPIX), jnp.bfloat16)],
        compiler_params=pltpu.CompilerParams(vmem_limit_bytes=48 * 1024 * 1024),
    )(lens, sky_map, projected_t, basis, tables)


def harmonic_tile(theta_ref, mv_ref, prof_ref, mw_ref, lc):
    rows = pl.ds(lc * 256, 256)
    h = jnp.dot(theta_ref[rows, :], mv_ref[...], preferred_element_type=jnp.float32)
    return h * prof_ref[0, rows, :] * mw_ref[...]


def power_kernel(theta_ref, mv_ref, prof_ref, mw_ref, o_ref):
    total = jnp.zeros((1, 1), jnp.float32)
    for lc in range(theta_ref.shape[0] // 256):
        w = harmonic_tile(theta_ref, mv_ref, prof_ref, mw_ref, lc)
        total = total + jnp.sum(w * w, keepdims=True)
    o_ref[0] = jnp.broadcast_to(total, (1, 128))


def output_kernel(theta_ref, mv_ref, prof_ref, mw_ref, scale_ref, o_ref):
    scale = scale_ref[0][:, 0:1]
    half = mv_ref.shape[1] // 2
    for lc in range(theta_ref.shape[0] // 256):
        w = harmonic_tile(theta_ref, mv_ref, prof_ref, mw_ref, lc) * scale
        for p in range(2):
            o_ref[pl.ds(lc * 256, 256), 0, p, :] = w[:, p * half : (p + 1) * half]


def harmonic_specs(n_l, n_cycle, width):
    return [
        pl.BlockSpec((n_l, n_cycle), lambda c: (0, 0)),
        pl.BlockSpec((n_cycle, width), lambda c: (0, c)),
        pl.BlockSpec((1, n_l, 1), lambda c: (c, 0, 0)),
        pl.BlockSpec((1, width), lambda c: (0, 0)),
    ]


def theta_table(cycle_ids, n_cycle):
    degrees = jnp.arange(L, dtype=jnp.int32)
    odd = 2 * cycle_ids + 1
    phase = degrees[:, None] * odd[None, :] % (4 * n_cycle)
    angle = jnp.pi * phase.astype(jnp.float32) / (2.0 * n_cycle)
    weight = jnp.sin(jnp.pi * odd.astype(jnp.float32) / (2.0 * n_cycle)) * (
        2.0 / jnp.sqrt(jnp.float32(n_cycle))
    )
    return (jnp.cos(angle) * weight[None, :]).astype(jnp.bfloat16)


def sub_axes(n_blk, n_grp):
    return [
        ("blk", 2, 1, n_blk),
        ("blk", 4, 2, n_blk),
        ("blk", n_blk // 8, 8, n_blk),
        ("grp", n_grp, 1, n_grp),
    ]


def shift_perm(size, stride, total, k):
    pairs = []
    for i in range(total):
        c = (i // stride) % size
        pairs.append((i, i + ((c + k) % size - c) * stride))
    return pairs


def ring_sum(v, subs):
    for axis, size, stride, total in subs:
        parts = [lax.ppermute(v, axis, shift_perm(size, stride, total, k)) for k in range(1, size)]
        for part in parts:
            v = v + part
    return v


def body(sky_map, fg_templates, cycle_len, beam_profile, beam_index):
    n_blk = lax.axis_size("blk")
    n_grp = lax.axis_size("grp")
    cycle_dev = cycle_len.shape[0]
    n_chan = sky_map.shape[0]
    n_mode = fg_templates.shape[1]
    chan_dev = n_chan // n_blk
    m_width = M_DEV * n_grp
    n_cycle = cycle_dev * n_blk * n_grp
    slots = jnp.arange(RPIX, dtype=jnp.int32)
    valid = (slots[None, :] < cycle_len[:, None]).reshape(-1)
    masked = jnp.where(valid[None, :], sky_map, jnp.zeros((), jnp.bfloat16))
    mode_amps = jnp.dot(fg_templates.T, masked, preferred_element_type=jnp.float32).astype(
        jnp.bfloat16
    )
    gram_part = jnp.dot(mode_amps, mode_amps.T, preferred_element_type=jnp.float32)
    cross_part = lax.dot_general(
        mode_amps, masked, (((1,), (1,)), ((), ())), preferred_element_type=jnp.float32
    )
    amps_wide = mode_amps.astype(jnp.float32)
    tables = cycle_tables(cycle_len, m_width)
    subs = sub_axes(n_blk, n_grp)
    sums = ring_sum(jnp.concatenate([gram_part, cross_part], axis=1), subs)
    gram_sum = sums[:, :n_mode]
    cross_sum = sums[:, n_mode:]
    lower = jnp.linalg.cholesky(gram_sum)
    basis = jax.scipy.linalg.solve_triangular(lower, amps_wide, lower=True)
    projected = jax.scipy.linalg.solve_triangular(lower, cross_sum, lower=True)
    sendbuf = cycle_fourier(sky_map, projected.T, basis, tables, cycle_len, n_blk, n_grp)
    moved = lax.all_to_all(sendbuf, ("blk", "grp"), 0, 0, tiled=True)
    moved = moved.reshape(n_cycle, chan_dev * 2 * M_DEV)
    theta_tab = theta_table(jnp.arange(n_cycle, dtype=jnp.int32), n_cycle)
    onehot = (
        beam_index[:, None] == jnp.arange(beam_profile.shape[0], dtype=jnp.int32)[None, :]
    ).astype(jnp.float32)
    profiles = jnp.dot(onehot, beam_profile, precision=lax.Precision.HIGHEST)
    orders = lax.axis_index("grp") * M_DEV + jnp.arange(M_DEV, dtype=jnp.int32)
    mweight = 0.25 + orders.astype(jnp.float32) / m_width
    mw_row = jnp.concatenate([mweight, mweight])[None, :]
    prof_col = profiles[:, :, None]
    width = 2 * M_DEV
    specs = harmonic_specs(L, n_cycle, width)
    vmem = pltpu.CompilerParams(vmem_limit_bytes=32 * 1024 * 1024)
    power_part = pl.pallas_call(
        power_kernel,
        grid=(chan_dev,),
        in_specs=specs,
        out_specs=pl.BlockSpec((1, 1, 128), lambda c: (c, 0, 0)),
        out_shape=jax.ShapeDtypeStruct((chan_dev, 1, 128), jnp.float32),
        compiler_params=vmem,
    )(theta_tab, moved, prof_col, mw_row)[:, 0, 0]
    power = ring_sum(power_part, subs[3:])
    scale = lax.rsqrt(power / (2.0 * L * m_width) + 1e-06)
    scale = jnp.broadcast_to(scale[:, None, None], (chan_dev, 1, 128))
    return pl.pallas_call(
        output_kernel,
        grid=(chan_dev,),
        in_specs=specs + [pl.BlockSpec((1, 1, 128), lambda c: (c, 0, 0))],
        out_specs=pl.BlockSpec((L, 1, 2, M_DEV), lambda c: (0, c, 0, 0)),
        out_shape=jax.ShapeDtypeStruct((L, chan_dev, 2, M_DEV), jnp.float32),
        compiler_params=vmem,
    )(theta_tab, moved, prof_col, mw_row, scale)


def solution(mesh):
    return jax.shard_map(
        body,
        mesh=mesh,
        in_specs=(P(None, ("blk", "grp")), P(), P(("blk", "grp")), P(), P("blk")),
        out_specs=P(None, "blk", None, "grp"),
        check_vma=False,
    )
```

```python
import jax
import jax.numpy as jnp
from jax import lax
from jax.sharding import PartitionSpec as P
from jax.experimental import pallas as pl
from jax.experimental.pallas import tpu as pltpu

RPIX = 2048
L = 1024
M_DEV = 256
J_LO = 128


def cos_sin_of_phase(phase, length):
    angle = jnp.pi * phase.astype(jnp.float32) / length.astype(jnp.float32)
    return jnp.cos(angle), jnp.sin(angle)


def add_angles(ca, sa, cb, sb):
    return ca * cb - sa * sb, sa * cb + ca * sb


def small_tables(cycle_len, m_width):
    length = cycle_len[:, None, None]
    period = 2 * length
    orders = jnp.arange(m_width, dtype=jnp.int32)[None, None, :]
    j_hi = jnp.arange(RPIX // J_LO, dtype=jnp.int32)[None, :, None]
    j_mid = jnp.arange(J_LO // 16, dtype=jnp.int32)[None, :, None]
    j_q = jnp.arange(16, dtype=jnp.int32)[None, :, None]
    ca, sa = cos_sin_of_phase((2 * J_LO * j_hi) % period * orders % period, length)
    cm, sm = cos_sin_of_phase((32 * j_mid) % period * orders % period, length)
    cq, sq = cos_sin_of_phase(orders * (2 * j_q + 1) % period, length)
    cb, sb = add_angles(cm[:, :, None, :], sm[:, :, None, :], cq[:, None, :, :], sq[:, None, :, :])
    n_cyc = cycle_len.shape[0]
    cb = cb.reshape(n_cyc, J_LO, m_width)
    sb = sb.reshape(n_cyc, J_LO, m_width)
    return ca, sa, cb, sb


def small_phases(cycle_len, m_width):
    period = 2 * cycle_len[:, None, None]
    orders = jnp.arange(m_width, dtype=jnp.int32)[None, None, :]
    j_hi = jnp.arange(RPIX // J_LO, dtype=jnp.int32)[None, :, None]
    j_mid = jnp.arange(J_LO // 16, dtype=jnp.int32)[None, :, None]
    j_q = jnp.arange(16, dtype=jnp.int32)[None, :, None]
    p_hi = (2 * J_LO * j_hi) % period * orders % period
    p_mid = (32 * j_mid) % period * orders % period
    p_q = orders * (2 * j_q + 1) % period
    return jnp.concatenate([p_hi, p_q, p_mid], axis=1)


def table_kernel(phase_ref, inv_ref, len_ref, tab_ref, hi_c, hi_s, lo_c, lo_s):
    m_width = phase_ref.shape[2]
    n_hi = RPIX // J_LO
    n_mid = J_LO // 16
    inv = inv_ref[0][:, 0:1]
    length = len_ref[0][:, 0:1]
    size = length.astype(jnp.float32)

    def cos_sin(rows):
        angle = jnp.pi * phase_ref[0, rows, :].astype(jnp.float32) / size
        return jnp.cos(angle), jnp.sin(angle)

    c, s_ = cos_sin(pl.ds(0, n_hi))
    hi_c[...] = c
    hi_s[...] = s_
    cq, sq = cos_sin(pl.ds(n_hi, 16))
    cm, sm = cos_sin(pl.ds(n_hi + 16, n_mid))
    for jm in range(n_mid):
        c_lo, s_lo = add_angles(cm[jm : jm + 1], sm[jm : jm + 1], cq, sq)
        lo_c[jm * 16 : (jm + 1) * 16, :] = c_lo
        lo_s[jm * 16 : (jm + 1) * 16, :] = s_lo

    def build(t, carry):
        ca = hi_c[pl.ds(t, 1), :]
        sa = hi_s[pl.ds(t, 1), :]
        cb = lo_c[...]
        sb = lo_s[...]
        rows = t * J_LO + lax.broadcasted_iota(jnp.int32, (J_LO, 1), 0)
        weight = jnp.where(rows < length, inv, 0.0)
        cos_t, sin_t = add_angles(ca, sa, cb, sb)
        r0 = pl.multiple_of(t * J_LO, J_LO)
        tab_ref[0, pl.ds(r0, J_LO), 0:m_width] = (cos_t * weight).astype(jnp.bfloat16)
        tab_ref[0, pl.ds(r0, J_LO), m_width : 2 * m_width] = (-sin_t * weight).astype(jnp.bfloat16)
        return carry

    lax.fori_loop(0, n_hi, build, 0)


def cycle_tables(cycle_len, m_width):
    n_cyc = cycle_len.shape[0]
    phases = small_phases(cycle_len, m_width)
    inv = jnp.broadcast_to(lax.rsqrt(cycle_len.astype(jnp.float32))[:, None, None], (n_cyc, 1, 128))
    lens = jnp.broadcast_to(cycle_len[:, None, None], (n_cyc, 1, 128))
    n_hi = RPIX // J_LO
    n_rows = phases.shape[1]
    return pl.pallas_call(
        table_kernel,
        grid=(n_cyc,),
        in_specs=[
            pl.BlockSpec((1, n_rows, m_width), lambda k: (k, 0, 0)),
            pl.BlockSpec((1, 1, 128), lambda k: (k, 0, 0)),
            pl.BlockSpec((1, 1, 128), lambda k: (k, 0, 0)),
        ],
        out_specs=pl.BlockSpec((1, RPIX, 2 * m_width), lambda k: (k, 0, 0)),
        out_shape=jax.ShapeDtypeStruct((n_cyc, RPIX, 2 * m_width), jnp.bfloat16),
        scratch_shapes=[
            pltpu.VMEM((n_hi, m_width), jnp.float32),
            pltpu.VMEM((n_hi, m_width), jnp.float32),
            pltpu.VMEM((J_LO, m_width), jnp.float32),
            pltpu.VMEM((J_LO, m_width), jnp.float32),
        ],
        compiler_params=pltpu.CompilerParams(vmem_limit_bytes=40 * 1024 * 1024),
    )(phases, inv, lens)


def fourier_kernel(len_ref, sky_ref, proj_ref, basis_ref, tab_ref, o_ref, clean_ref):
    m_width = tab_ref.shape[2] // 2
    n_grp = o_ref.shape[0] // (sky_ref.shape[0] // o_ref.shape[1])
    chan_dev = o_ref.shape[1]
    length = len_ref[0][:, 0:1]
    cols = lax.broadcasted_iota(jnp.int32, (1, RPIX), 1)
    masked = jnp.where(cols < length, sky_ref[...].astype(jnp.float32), 0.0)
    correction = jnp.dot(
        proj_ref[...], basis_ref[...], preferred_element_type=jnp.float32,
        precision=lax.Precision.HIGHEST,
    )
    clean_ref[...] = (masked - correction).astype(jnp.bfloat16)
    m_dev = m_width // n_grp
    step = 2 * m_dev
    n_blk = sky_ref.shape[0] // chan_dev
    for q in range(2 * m_width // step):
        res = jnp.dot(
            clean_ref[...], tab_ref[0, :, q * step : (q + 1) * step], preferred_element_type=jnp.float32
        )
        part = (q * step) // m_width
        for h in range(step // m_dev):
            grp_dest = (q * step - part * m_width) // m_dev + h
            for blk_dest in range(n_blk):
                slab = res[blk_dest * chan_dev : (blk_dest + 1) * chan_dev, h * m_dev : (h + 1) * m_dev]
                o_ref[blk_dest * n_grp + grp_dest, :, part * m_dev : (part + 1) * m_dev] = slab.astype(
                    jnp.bfloat16
                )


def cycle_fourier(sky_map, projected_t, basis, tables, cycle_len, n_blk, n_grp):
    n_cyc = cycle_len.shape[0]
    n_chan = sky_map.shape[0]
    n_mode = basis.shape[0]
    n_dev = n_blk * n_grp
    chan_dev = n_chan // n_blk
    width = tables.shape[2]
    lens = jnp.broadcast_to(cycle_len[:, None, None], (n_cyc, 1, 128))
    m_dev = width // 2 // n_grp
    return pl.pallas_call(
        fourier_kernel,
        grid=(n_cyc,),
        in_specs=[
            pl.BlockSpec((1, 1, 128), lambda k: (k, 0, 0)),
            pl.BlockSpec((n_chan, RPIX), lambda k: (0, k)),
            pl.BlockSpec((n_chan, n_mode), lambda k: (0, 0)),
            pl.BlockSpec((n_mode, RPIX), lambda k: (0, k)),
            pl.BlockSpec((1, RPIX, width), lambda k: (k, 0, 0)),
        ],
        out_specs=pl.BlockSpec((n_dev, None, chan_dev, 2 * m_dev), lambda k: (0, k, 0, 0)),
        out_shape=jax.ShapeDtypeStruct((n_dev, n_cyc, chan_dev, 2 * m_dev), jnp.bfloat16),
        scratch_shapes=[pltpu.VMEM((n_chan, RPIX), jnp.bfloat16)],
        compiler_params=pltpu.CompilerParams(vmem_limit_bytes=48 * 1024 * 1024),
    )(lens, sky_map, projected_t, basis, tables)


def harmonic_tile(theta_ref, mv_ref, prof_ref, mw_ref, lc):
    rows = pl.ds(lc * 256, 256)
    h = jnp.dot(theta_ref[rows, :], mv_ref[...], preferred_element_type=jnp.float32)
    return h * prof_ref[0, rows, :] * mw_ref[...]


def power_kernel(theta_ref, mv_ref, prof_ref, mw_ref, o_ref):
    total = jnp.zeros((1, 1), jnp.float32)
    for lc in range(theta_ref.shape[0] // 256):
        w = harmonic_tile(theta_ref, mv_ref, prof_ref, mw_ref, lc)
        total = total + jnp.sum(w * w, keepdims=True)
    o_ref[0] = jnp.broadcast_to(total, (1, 128))


def output_kernel(theta_ref, mv_ref, prof_ref, mw_ref, scale_ref, o_ref):
    scale = scale_ref[0][:, 0:1]
    half = mv_ref.shape[1] // 2
    for lc in range(theta_ref.shape[0] // 256):
        w = harmonic_tile(theta_ref, mv_ref, prof_ref, mw_ref, lc) * scale
        for p in range(2):
            o_ref[pl.ds(lc * 256, 256), 0, p, :] = w[:, p * half : (p + 1) * half]


def harmonic_specs(n_l, n_cycle, width):
    return [
        pl.BlockSpec((n_l, n_cycle), lambda c: (0, 0)),
        pl.BlockSpec((n_cycle, width), lambda c: (0, c)),
        pl.BlockSpec((1, n_l, 1), lambda c: (c, 0, 0)),
        pl.BlockSpec((1, width), lambda c: (0, 0)),
    ]


def theta_table(cycle_ids, n_cycle):
    degrees = jnp.arange(L, dtype=jnp.int32)
    odd = 2 * cycle_ids + 1
    phase = degrees[:, None] * odd[None, :] % (4 * n_cycle)
    angle = jnp.pi * phase.astype(jnp.float32) / (2.0 * n_cycle)
    weight = jnp.sin(jnp.pi * odd.astype(jnp.float32) / (2.0 * n_cycle)) * (
        2.0 / jnp.sqrt(jnp.float32(n_cycle))
    )
    return (jnp.cos(angle) * weight[None, :]).astype(jnp.bfloat16)


def sub_axes(n_blk, n_grp):
    return [
        ("blk", 2, 1, n_blk),
        ("blk", 4, 2, n_blk),
        ("blk", n_blk // 8, 8, n_blk),
        ("grp", n_grp, 1, n_grp),
    ]


def shift_perm(size, stride, total, k):
    pairs = []
    for i in range(total):
        c = (i // stride) % size
        pairs.append((i, i + ((c + k) % size - c) * stride))
    return pairs


def ring_sum(v, subs):
    for axis, size, stride, total in subs:
        parts = [lax.ppermute(v, axis, shift_perm(size, stride, total, k)) for k in range(1, size)]
        for part in parts:
            v = v + part
    return v


def body(sky_map, fg_templates, cycle_len, beam_profile, beam_index):
    n_blk = lax.axis_size("blk")
    n_grp = lax.axis_size("grp")
    cycle_dev = cycle_len.shape[0]
    n_chan = sky_map.shape[0]
    n_mode = fg_templates.shape[1]
    chan_dev = n_chan // n_blk
    m_width = M_DEV * n_grp
    n_cycle = cycle_dev * n_blk * n_grp
    slots = jnp.arange(RPIX, dtype=jnp.int32)
    valid = (slots[None, :] < cycle_len[:, None]).reshape(-1)
    masked = jnp.where(valid[None, :], sky_map, jnp.zeros((), jnp.bfloat16))
    mode_amps = jnp.dot(fg_templates.T, masked, preferred_element_type=jnp.float32).astype(
        jnp.bfloat16
    )
    gram_part = jnp.dot(mode_amps, mode_amps.T, preferred_element_type=jnp.float32)
    cross_part = lax.dot_general(
        mode_amps, masked, (((1,), (1,)), ((), ())), preferred_element_type=jnp.float32
    )
    amps_wide = mode_amps.astype(jnp.float32)
    tables = cycle_tables(cycle_len, m_width)
    subs = sub_axes(n_blk, n_grp)
    sums = ring_sum(jnp.concatenate([gram_part, cross_part], axis=1), subs)
    gram_sum = sums[:, :n_mode]
    cross_sum = sums[:, n_mode:]
    lower = jnp.linalg.cholesky(gram_sum)
    basis = jax.scipy.linalg.solve_triangular(lower, amps_wide, lower=True)
    projected = jax.scipy.linalg.solve_triangular(lower, cross_sum, lower=True)
    sendbuf = cycle_fourier(sky_map, projected.T, basis, tables, cycle_len, n_blk, n_grp)
    moved = lax.all_to_all(sendbuf, ("blk", "grp"), 0, 0, tiled=True)
    moved = moved.reshape(n_cycle, chan_dev * 2 * M_DEV)
    theta_tab = theta_table(jnp.arange(n_cycle, dtype=jnp.int32), n_cycle)
    onehot = (
        beam_index[:, None] == jnp.arange(beam_profile.shape[0], dtype=jnp.int32)[None, :]
    ).astype(jnp.float32)
    profiles = jnp.dot(onehot, beam_profile, precision=lax.Precision.HIGHEST)
    orders = lax.axis_index("grp") * M_DEV + jnp.arange(M_DEV, dtype=jnp.int32)
    mweight = 0.25 + orders.astype(jnp.float32) / m_width
    mw_row = jnp.concatenate([mweight, mweight])[None, :]
    prof_col = profiles[:, :, None]
    width = 2 * M_DEV
    specs = harmonic_specs(L, n_cycle, width)
    vmem = pltpu.CompilerParams(vmem_limit_bytes=32 * 1024 * 1024)
    power_part = pl.pallas_call(
        power_kernel,
        grid=(chan_dev,),
        in_specs=specs,
        out_specs=pl.BlockSpec((1, 1, 128), lambda c: (c, 0, 0)),
        out_shape=jax.ShapeDtypeStruct((chan_dev, 1, 128), jnp.float32),
        compiler_params=vmem,
    )(theta_tab, moved, prof_col, mw_row)[:, 0, 0]
    power = ring_sum(power_part, subs[3:])
    scale = lax.rsqrt(power / (2.0 * L * m_width) + 1e-06)
    scale = jnp.broadcast_to(scale[:, None, None], (chan_dev, 1, 128))
    return pl.pallas_call(
        output_kernel,
        grid=(chan_dev,),
        in_specs=specs + [pl.BlockSpec((1, 1, 128), lambda c: (c, 0, 0))],
        out_specs=pl.BlockSpec((L, 1, 2, M_DEV), lambda c: (0, c, 0, 0)),
        out_shape=jax.ShapeDtypeStruct((L, chan_dev, 2, M_DEV), jnp.float32),
        compiler_params=vmem,
    )(theta_tab, moved, prof_col, mw_row, scale)


def solution(mesh):
    return jax.shard_map(
        body,
        mesh=mesh,
        in_specs=(P(None, ("blk", "grp")), P(), P(("blk", "grp")), P(), P("blk")),
        out_specs=P(None, "blk", None, "grp"),
        check_vma=False,
    )
```

```python
import jax
import jax.numpy as jnp
from jax import lax
from jax.sharding import PartitionSpec as P
from jax.experimental import pallas as pl
from jax.experimental.pallas import tpu as pltpu

RPIX = 2048
L = 1024
M_DEV = 256
J_LO = 128


def cos_sin_of_phase(phase, length):
    angle = jnp.pi * phase.astype(jnp.float32) / length.astype(jnp.float32)
    return jnp.cos(angle), jnp.sin(angle)


def add_angles(ca, sa, cb, sb):
    return ca * cb - sa * sb, sa * cb + ca * sb


def small_tables(cycle_len, m_width):
    length = cycle_len[:, None, None]
    period = 2 * length
    orders = jnp.arange(m_width, dtype=jnp.int32)[None, None, :]
    j_hi = jnp.arange(RPIX // J_LO, dtype=jnp.int32)[None, :, None]
    j_mid = jnp.arange(J_LO // 16, dtype=jnp.int32)[None, :, None]
    j_q = jnp.arange(16, dtype=jnp.int32)[None, :, None]
    ca, sa = cos_sin_of_phase((2 * J_LO * j_hi) % period * orders % period, length)
    cm, sm = cos_sin_of_phase((32 * j_mid) % period * orders % period, length)
    cq, sq = cos_sin_of_phase(orders * (2 * j_q + 1) % period, length)
    cb, sb = add_angles(cm[:, :, None, :], sm[:, :, None, :], cq[:, None, :, :], sq[:, None, :, :])
    n_cyc = cycle_len.shape[0]
    cb = cb.reshape(n_cyc, J_LO, m_width)
    sb = sb.reshape(n_cyc, J_LO, m_width)
    return ca, sa, cb, sb


def table_kernel(ca_ref, sa_ref, cb_ref, sb_ref, inv_ref, len_ref, tab_ref):
    m_width = cb_ref.shape[2]
    inv = inv_ref[0][:, 0:1]
    length = len_ref[0][:, 0:1]

    def build(t, carry):
        ca = ca_ref[0, pl.ds(t, 1), :]
        sa = sa_ref[0, pl.ds(t, 1), :]
        cb = cb_ref[0]
        sb = sb_ref[0]
        rows = t * J_LO + lax.broadcasted_iota(jnp.int32, (J_LO, 1), 0)
        weight = jnp.where(rows < length, inv, 0.0)
        cos_t, sin_t = add_angles(ca, sa, cb, sb)
        r0 = pl.multiple_of(t * J_LO, J_LO)
        tab_ref[0, pl.ds(r0, J_LO), 0:m_width] = (cos_t * weight).astype(jnp.bfloat16)
        tab_ref[0, pl.ds(r0, J_LO), m_width : 2 * m_width] = (-sin_t * weight).astype(jnp.bfloat16)
        return carry

    lax.fori_loop(0, RPIX // J_LO, build, 0)


def cycle_tables(cycle_len, m_width):
    n_cyc = cycle_len.shape[0]
    ca, sa, cb, sb = small_tables(cycle_len, m_width)
    inv = jnp.broadcast_to(lax.rsqrt(cycle_len.astype(jnp.float32))[:, None, None], (n_cyc, 1, 128))
    lens = jnp.broadcast_to(cycle_len[:, None, None], (n_cyc, 1, 128))
    n_hi = RPIX // J_LO
    return pl.pallas_call(
        table_kernel,
        grid=(n_cyc,),
        in_specs=[
            pl.BlockSpec((1, n_hi, m_width), lambda k: (k, 0, 0)),
            pl.BlockSpec((1, n_hi, m_width), lambda k: (k, 0, 0)),
            pl.BlockSpec((1, J_LO, m_width), lambda k: (k, 0, 0)),
            pl.BlockSpec((1, J_LO, m_width), lambda k: (k, 0, 0)),
            pl.BlockSpec((1, 1, 128), lambda k: (k, 0, 0)),
            pl.BlockSpec((1, 1, 128), lambda k: (k, 0, 0)),
        ],
        out_specs=pl.BlockSpec((1, RPIX, 2 * m_width), lambda k: (k, 0, 0)),
        out_shape=jax.ShapeDtypeStruct((n_cyc, RPIX, 2 * m_width), jnp.bfloat16),
        compiler_params=pltpu.CompilerParams(vmem_limit_bytes=40 * 1024 * 1024),
    )(ca, sa, cb, sb, inv, lens)


def fourier_kernel(len_ref, sky_ref, proj_ref, basis_ref, tab_ref, oa_ref, ob_ref, clean_ref):
    o_ref = oa_ref
    m_width = tab_ref.shape[2] // 2
    chan_dev = 2 * o_ref.shape[1]
    n_grp = o_ref.shape[0] // (sky_ref.shape[0] // chan_dev)
    half_c = o_ref.shape[1]
    length = len_ref[0][:, 0:1]
    cols = lax.broadcasted_iota(jnp.int32, (1, RPIX), 1)
    masked = jnp.where(cols < length, sky_ref[...].astype(jnp.float32), 0.0)
    correction = jnp.dot(
        proj_ref[...], basis_ref[...], preferred_element_type=jnp.float32,
        precision=lax.Precision.HIGHEST,
    )
    clean_ref[...] = (masked - correction).astype(jnp.bfloat16)
    m_dev = m_width // n_grp
    step = 2 * m_dev
    n_blk = sky_ref.shape[0] // chan_dev
    for q in range(2 * m_width // step):
        res = jnp.dot(
            clean_ref[...], tab_ref[0, :, q * step : (q + 1) * step], preferred_element_type=jnp.float32
        )
        part = (q * step) // m_width
        for h in range(step // m_dev):
            grp_dest = (q * step - part * m_width) // m_dev + h
            for blk_dest in range(n_blk):
                for half, ref in ((0, oa_ref), (1, ob_ref)):
                    row = blk_dest * chan_dev + half * half_c
                    slab = res[row : row + half_c, h * m_dev : (h + 1) * m_dev]
                    ref[blk_dest * n_grp + grp_dest, :, part * m_dev : (part + 1) * m_dev] = (
                        slab.astype(jnp.bfloat16)
                    )


def cycle_fourier(sky_map, projected_t, basis, tables, cycle_len, n_blk, n_grp):
    n_cyc = cycle_len.shape[0]
    n_chan = sky_map.shape[0]
    n_mode = basis.shape[0]
    n_dev = n_blk * n_grp
    chan_dev = n_chan // n_blk
    width = tables.shape[2]
    lens = jnp.broadcast_to(cycle_len[:, None, None], (n_cyc, 1, 128))
    m_dev = width // 2 // n_grp
    return pl.pallas_call(
        fourier_kernel,
        grid=(n_cyc,),
        in_specs=[
            pl.BlockSpec((1, 1, 128), lambda k: (k, 0, 0)),
            pl.BlockSpec((n_chan, RPIX), lambda k: (0, k)),
            pl.BlockSpec((n_chan, n_mode), lambda k: (0, 0)),
            pl.BlockSpec((n_mode, RPIX), lambda k: (0, k)),
            pl.BlockSpec((1, RPIX, width), lambda k: (k, 0, 0)),
        ],
        out_specs=[
            pl.BlockSpec((n_dev, None, chan_dev // 2, 2 * m_dev), lambda k: (0, k, 0, 0)),
            pl.BlockSpec((n_dev, None, chan_dev // 2, 2 * m_dev), lambda k: (0, k, 0, 0)),
        ],
        out_shape=[
            jax.ShapeDtypeStruct((n_dev, n_cyc, chan_dev // 2, 2 * m_dev), jnp.bfloat16),
            jax.ShapeDtypeStruct((n_dev, n_cyc, chan_dev // 2, 2 * m_dev), jnp.bfloat16),
        ],
        scratch_shapes=[pltpu.VMEM((n_chan, RPIX), jnp.bfloat16)],
        compiler_params=pltpu.CompilerParams(vmem_limit_bytes=48 * 1024 * 1024),
    )(lens, sky_map, projected_t, basis, tables)


def harmonic_tile(theta_ref, mv_ref, prof_ref, mw_ref, lc):
    rows = pl.ds(lc * 256, 256)
    h = jnp.dot(theta_ref[rows, :], mv_ref[...], preferred_element_type=jnp.float32)
    return h * prof_ref[0, rows, :] * mw_ref[...]


def power_kernel(theta_ref, mv_ref, prof_ref, mw_ref, o_ref):
    total = jnp.zeros((1, 1), jnp.float32)
    for lc in range(theta_ref.shape[0] // 256):
        w = harmonic_tile(theta_ref, mv_ref, prof_ref, mw_ref, lc)
        total = total + jnp.sum(w * w, keepdims=True)
    o_ref[0] = jnp.broadcast_to(total, (1, 128))


def output_kernel(theta_ref, mv_ref, prof_ref, mw_ref, scale_ref, o_ref):
    scale = scale_ref[0][:, 0:1]
    half = mv_ref.shape[1] // 2
    for lc in range(theta_ref.shape[0] // 256):
        w = harmonic_tile(theta_ref, mv_ref, prof_ref, mw_ref, lc) * scale
        for p in range(2):
            o_ref[pl.ds(lc * 256, 256), 0, p, :] = w[:, p * half : (p + 1) * half]


def output_kernel_aliased(theta_ref, mv_ref, prof_ref, mw_ref, scale_ref, prev_ref, o_ref):
    output_kernel(theta_ref, mv_ref, prof_ref, mw_ref, scale_ref, o_ref)


def harmonic_specs(n_l, n_cycle, width, offset):
    return [
        pl.BlockSpec((n_l, n_cycle), lambda c: (0, 0)),
        pl.BlockSpec((n_cycle, width), lambda c: (0, c)),
        pl.BlockSpec((1, n_l, 1), lambda c: (c + offset, 0, 0)),
        pl.BlockSpec((1, width), lambda c: (0, 0)),
    ]


def theta_table(cycle_ids, n_cycle):
    degrees = jnp.arange(L, dtype=jnp.int32)
    odd = 2 * cycle_ids + 1
    phase = degrees[:, None] * odd[None, :] % (4 * n_cycle)
    angle = jnp.pi * phase.astype(jnp.float32) / (2.0 * n_cycle)
    weight = jnp.sin(jnp.pi * odd.astype(jnp.float32) / (2.0 * n_cycle)) * (
        2.0 / jnp.sqrt(jnp.float32(n_cycle))
    )
    return (jnp.cos(angle) * weight[None, :]).astype(jnp.bfloat16)


def sub_axes(n_blk, n_grp):
    return [
        ("blk", 2, 1, n_blk),
        ("blk", 4, 2, n_blk),
        ("blk", n_blk // 8, 8, n_blk),
        ("grp", n_grp, 1, n_grp),
    ]


def shift_perm(size, stride, total, k):
    pairs = []
    for i in range(total):
        c = (i // stride) % size
        pairs.append((i, i + ((c + k) % size - c) * stride))
    return pairs


def ring_sum(v, subs):
    for axis, size, stride, total in subs:
        parts = [lax.ppermute(v, axis, shift_perm(size, stride, total, k)) for k in range(1, size)]
        for part in parts:
            v = v + part
    return v


def body(sky_map, fg_templates, cycle_len, beam_profile, beam_index):
    n_blk = lax.axis_size("blk")
    n_grp = lax.axis_size("grp")
    cycle_dev = cycle_len.shape[0]
    n_chan = sky_map.shape[0]
    n_mode = fg_templates.shape[1]
    chan_dev = n_chan // n_blk
    m_width = M_DEV * n_grp
    n_cycle = cycle_dev * n_blk * n_grp
    slots = jnp.arange(RPIX, dtype=jnp.int32)
    valid = (slots[None, :] < cycle_len[:, None]).reshape(-1)
    masked = jnp.where(valid[None, :], sky_map, jnp.zeros((), jnp.bfloat16))
    mode_amps = jnp.dot(fg_templates.T, masked, preferred_element_type=jnp.float32).astype(
        jnp.bfloat16
    )
    gram_part = jnp.dot(mode_amps, mode_amps.T, preferred_element_type=jnp.float32)
    cross_part = lax.dot_general(
        mode_amps, masked, (((1,), (1,)), ((), ())), preferred_element_type=jnp.float32
    )
    amps_wide = mode_amps.astype(jnp.float32)
    tables = cycle_tables(cycle_len, m_width)
    subs = sub_axes(n_blk, n_grp)
    sums = ring_sum(jnp.concatenate([gram_part, cross_part], axis=1), subs)
    gram_sum = sums[:, :n_mode]
    cross_sum = sums[:, n_mode:]
    lower = jnp.linalg.cholesky(gram_sum)
    basis = jax.scipy.linalg.solve_triangular(lower, amps_wide, lower=True)
    projected = jax.scipy.linalg.solve_triangular(lower, cross_sum, lower=True)
    sends = cycle_fourier(sky_map, projected.T, basis, tables, cycle_len, n_blk, n_grp)
    theta_tab = theta_table(jnp.arange(n_cycle, dtype=jnp.int32), n_cycle)
    onehot = (
        beam_index[:, None] == jnp.arange(beam_profile.shape[0], dtype=jnp.int32)[None, :]
    ).astype(jnp.float32)
    profiles = jnp.dot(onehot, beam_profile, precision=lax.Precision.HIGHEST)
    orders = lax.axis_index("grp") * M_DEV + jnp.arange(M_DEV, dtype=jnp.int32)
    mweight = 0.25 + orders.astype(jnp.float32) / m_width
    mw_row = jnp.concatenate([mweight, mweight])[None, :]
    prof_col = profiles[:, :, None]
    width = 2 * M_DEV
    half_c = chan_dev // 2
    vmem = pltpu.CompilerParams(vmem_limit_bytes=32 * 1024 * 1024)
    out = None
    for half, sendbuf in enumerate(sends):
        moved = lax.all_to_all(sendbuf, ("blk", "grp"), 0, 0, tiled=True)
        moved = moved.reshape(n_cycle, half_c * width)
        specs = harmonic_specs(L, n_cycle, width, half * half_c)
        power_part = pl.pallas_call(
            power_kernel,
            grid=(half_c,),
            in_specs=specs,
            out_specs=pl.BlockSpec((1, 1, 128), lambda c: (c, 0, 0)),
            out_shape=jax.ShapeDtypeStruct((half_c, 1, 128), jnp.float32),
            compiler_params=vmem,
        )(theta_tab, moved, prof_col, mw_row)[:, 0, 0]
        power = ring_sum(power_part, subs[3:])
        scale = lax.rsqrt(power / (2.0 * L * m_width) + 1e-06)
        scale = jnp.broadcast_to(scale[:, None, None], (half_c, 1, 128))
        args = [theta_tab, moved, prof_col, mw_row, scale]
        in_specs = specs + [pl.BlockSpec((1, 1, 128), lambda c: (c, 0, 0))]
        aliases = {}
        kernel = output_kernel
        if out is not None:
            args.append(out)
            in_specs.append(pl.BlockSpec(memory_space=pl.ANY))
            aliases = {len(args) - 1: 0}
            kernel = output_kernel_aliased
        offset = half * half_c
        out = pl.pallas_call(
            kernel,
            grid=(half_c,),
            in_specs=in_specs,
            out_specs=pl.BlockSpec((L, 1, 2, M_DEV), lambda c: (0, c + offset, 0, 0)),
            out_shape=jax.ShapeDtypeStruct((L, chan_dev, 2, M_DEV), jnp.float32),
            input_output_aliases=aliases,
            compiler_params=vmem,
        )(*args)
    return out


def solution(mesh):
    return jax.shard_map(
        body,
        mesh=mesh,
        in_specs=(P(None, ("blk", "grp")), P(), P(("blk", "grp")), P(), P("blk")),
        out_specs=P(None, "blk", None, "grp"),
        check_vma=False,
    )
```

```python
import jax
import jax.numpy as jnp
from jax import lax
from jax.sharding import PartitionSpec as P
from jax.experimental import pallas as pl
from jax.experimental.pallas import tpu as pltpu

RPIX = 2048
L = 1024
M_DEV = 256
J_LO = 128


def cos_sin_of_phase(phase, length):
    angle = jnp.pi * phase.astype(jnp.float32) / length.astype(jnp.float32)
    return jnp.cos(angle), jnp.sin(angle)


def add_angles(ca, sa, cb, sb):
    return ca * cb - sa * sb, sa * cb + ca * sb


def small_tables(cycle_len, m_width):
    length = cycle_len[:, None, None]
    period = 2 * length
    orders = jnp.arange(m_width, dtype=jnp.int32)[None, None, :]
    j_hi = jnp.arange(RPIX // J_LO, dtype=jnp.int32)[None, :, None]
    j_mid = jnp.arange(J_LO // 16, dtype=jnp.int32)[None, :, None]
    j_q = jnp.arange(16, dtype=jnp.int32)[None, :, None]
    ca, sa = cos_sin_of_phase((2 * J_LO * j_hi) % period * orders % period, length)
    cm, sm = cos_sin_of_phase((32 * j_mid) % period * orders % period, length)
    cq, sq = cos_sin_of_phase(orders * (2 * j_q + 1) % period, length)
    cb, sb = add_angles(cm[:, :, None, :], sm[:, :, None, :], cq[:, None, :, :], sq[:, None, :, :])
    n_cyc = cycle_len.shape[0]
    cb = cb.reshape(n_cyc, J_LO, m_width)
    sb = sb.reshape(n_cyc, J_LO, m_width)
    return ca, sa, cb, sb


def table_kernel(ca_ref, sa_ref, cb_ref, sb_ref, inv_ref, len_ref, tab_ref):
    m_width = cb_ref.shape[2]
    inv = inv_ref[0][:, 0:1]
    length = len_ref[0][:, 0:1]

    def build(t, carry):
        ca = ca_ref[0, pl.ds(t, 1), :]
        sa = sa_ref[0, pl.ds(t, 1), :]
        cb = cb_ref[0]
        sb = sb_ref[0]
        rows = t * J_LO + lax.broadcasted_iota(jnp.int32, (J_LO, 1), 0)
        weight = jnp.where(rows < length, inv, 0.0)
        cos_t, sin_t = add_angles(ca, sa, cb, sb)
        r0 = pl.multiple_of(t * J_LO, J_LO)
        tab_ref[0, pl.ds(r0, J_LO), 0:m_width] = (cos_t * weight).astype(jnp.bfloat16)
        tab_ref[0, pl.ds(r0, J_LO), m_width : 2 * m_width] = (-sin_t * weight).astype(jnp.bfloat16)
        return carry

    lax.fori_loop(0, RPIX // J_LO, build, 0)


def cycle_tables(cycle_len, m_width):
    n_cyc = cycle_len.shape[0]
    ca, sa, cb, sb = small_tables(cycle_len, m_width)
    inv = jnp.broadcast_to(lax.rsqrt(cycle_len.astype(jnp.float32))[:, None, None], (n_cyc, 1, 128))
    lens = jnp.broadcast_to(cycle_len[:, None, None], (n_cyc, 1, 128))
    n_hi = RPIX // J_LO
    return pl.pallas_call(
        table_kernel,
        grid=(n_cyc,),
        in_specs=[
            pl.BlockSpec((1, n_hi, m_width), lambda k: (k, 0, 0)),
            pl.BlockSpec((1, n_hi, m_width), lambda k: (k, 0, 0)),
            pl.BlockSpec((1, J_LO, m_width), lambda k: (k, 0, 0)),
            pl.BlockSpec((1, J_LO, m_width), lambda k: (k, 0, 0)),
            pl.BlockSpec((1, 1, 128), lambda k: (k, 0, 0)),
            pl.BlockSpec((1, 1, 128), lambda k: (k, 0, 0)),
        ],
        out_specs=pl.BlockSpec((1, RPIX, 2 * m_width), lambda k: (k, 0, 0)),
        out_shape=jax.ShapeDtypeStruct((n_cyc, RPIX, 2 * m_width), jnp.bfloat16),
        compiler_params=pltpu.CompilerParams(vmem_limit_bytes=40 * 1024 * 1024),
    )(ca, sa, cb, sb, inv, lens)


def fourier_kernel(len_ref, sky_ref, proj_ref, basis_ref, tab_ref, o_ref, clean_ref):
    m_width = tab_ref.shape[2] // 2
    n_grp = o_ref.shape[0] // (sky_ref.shape[0] // o_ref.shape[1])
    chan_dev = o_ref.shape[1]
    length = len_ref[0][:, 0:1]
    cols = lax.broadcasted_iota(jnp.int32, (1, RPIX), 1)
    masked = jnp.where(cols < length, sky_ref[...].astype(jnp.float32), 0.0)
    correction = jnp.dot(
        proj_ref[...], basis_ref[...], preferred_element_type=jnp.float32,
        precision=lax.Precision.HIGHEST,
    )
    clean_ref[...] = (masked - correction).astype(jnp.bfloat16)
    m_dev = m_width // n_grp
    step = 2 * m_dev
    n_blk = sky_ref.shape[0] // chan_dev
    for q in range(2 * m_width // step):
        res = jnp.dot(
            clean_ref[...], tab_ref[0, :, q * step : (q + 1) * step], preferred_element_type=jnp.float32
        )
        part = (q * step) // m_width
        for h in range(step // m_dev):
            grp_dest = (q * step - part * m_width) // m_dev + h
            for blk_dest in range(n_blk):
                slab = res[blk_dest * chan_dev : (blk_dest + 1) * chan_dev, h * m_dev : (h + 1) * m_dev]
                o_ref[blk_dest * n_grp + grp_dest, :, part * m_dev : (part + 1) * m_dev] = slab.astype(
                    jnp.bfloat16
                )


def cycle_fourier(sky_map, projected_t, basis, tables, cycle_len, n_blk, n_grp):
    n_cyc = cycle_len.shape[0]
    n_chan = sky_map.shape[0]
    n_mode = basis.shape[0]
    n_dev = n_blk * n_grp
    chan_dev = n_chan // n_blk
    width = tables.shape[2]
    lens = jnp.broadcast_to(cycle_len[:, None, None], (n_cyc, 1, 128))
    m_dev = width // 2 // n_grp
    return pl.pallas_call(
        fourier_kernel,
        grid=(n_cyc,),
        in_specs=[
            pl.BlockSpec((1, 1, 128), lambda k: (k, 0, 0)),
            pl.BlockSpec((n_chan, RPIX), lambda k: (0, k)),
            pl.BlockSpec((n_chan, n_mode), lambda k: (0, 0)),
            pl.BlockSpec((n_mode, RPIX), lambda k: (0, k)),
            pl.BlockSpec((1, RPIX, width), lambda k: (k, 0, 0)),
        ],
        out_specs=pl.BlockSpec((n_dev, None, chan_dev, 2 * m_dev), lambda k: (0, k, 0, 0)),
        out_shape=jax.ShapeDtypeStruct((n_dev, n_cyc, chan_dev, 2 * m_dev), jnp.bfloat16),
        scratch_shapes=[pltpu.VMEM((n_chan, RPIX), jnp.bfloat16)],
        compiler_params=pltpu.CompilerParams(vmem_limit_bytes=48 * 1024 * 1024),
    )(lens, sky_map, projected_t, basis, tables)


def harmonic_tile(theta_ref, mv_ref, prof_ref, mw_ref, lc):
    rows = pl.ds(lc * 256, 256)
    h = jnp.dot(theta_ref[rows, :], mv_ref[...], preferred_element_type=jnp.float32)
    return h * prof_ref[0, rows, :] * mw_ref[...]


def power_kernel(theta_ref, mv_ref, prof_ref, mw_ref, o_ref):
    total = jnp.zeros((1, 1), jnp.float32)
    for lc in range(theta_ref.shape[0] // 256):
        w = harmonic_tile(theta_ref, mv_ref, prof_ref, mw_ref, lc)
        total = total + jnp.sum(w * w, keepdims=True)
    o_ref[0] = jnp.broadcast_to(total, (1, 128))


def output_kernel(theta_ref, mv_ref, prof_ref, mw_ref, scale_ref, o_ref):
    scale = scale_ref[0][:, 0:1]
    half = mv_ref.shape[1] // 2
    for lc in range(theta_ref.shape[0] // 256):
        w = harmonic_tile(theta_ref, mv_ref, prof_ref, mw_ref, lc) * scale
        for p in range(2):
            o_ref[pl.ds(lc * 256, 256), 0, p, :] = w[:, p * half : (p + 1) * half]


def harmonic_specs(n_l, n_cycle, width):
    return [
        pl.BlockSpec((n_l, n_cycle), lambda c: (0, 0)),
        pl.BlockSpec((n_cycle, width), lambda c: (0, c)),
        pl.BlockSpec((1, n_l, 1), lambda c: (c, 0, 0)),
        pl.BlockSpec((1, width), lambda c: (0, 0)),
    ]


def theta_table(cycle_ids, n_cycle):
    degrees = jnp.arange(L, dtype=jnp.int32)
    odd = 2 * cycle_ids + 1
    phase = degrees[:, None] * odd[None, :] % (4 * n_cycle)
    angle = jnp.pi * phase.astype(jnp.float32) / (2.0 * n_cycle)
    weight = jnp.sin(jnp.pi * odd.astype(jnp.float32) / (2.0 * n_cycle)) * (
        2.0 / jnp.sqrt(jnp.float32(n_cycle))
    )
    return (jnp.cos(angle) * weight[None, :]).astype(jnp.bfloat16)


def sub_axes(n_blk, n_grp):
    return [
        ("blk", 2, 1, n_blk),
        ("blk", 4, 2, n_blk),
        ("blk", n_blk // 8, 8, n_blk),
        ("grp", n_grp, 1, n_grp),
    ]


def shift_perm(size, stride, total, k):
    pairs = []
    for i in range(total):
        c = (i // stride) % size
        pairs.append((i, i + ((c + k) % size - c) * stride))
    return pairs


def ring_sum(v, subs):
    for axis, size, stride, total in subs:
        if size & (size - 1):
            parts = [lax.ppermute(v, axis, shift_perm(size, stride, total, k)) for k in range(1, size)]
            for part in parts:
                v = v + part
            continue
        k = 1
        while k < size:
            pairs = [(i, i ^ (k * stride)) for i in range(total)]
            v = v + lax.ppermute(v, axis, pairs)
            k *= 2
    return v


def body(sky_map, fg_templates, cycle_len, beam_profile, beam_index):
    n_blk = lax.axis_size("blk")
    n_grp = lax.axis_size("grp")
    cycle_dev = cycle_len.shape[0]
    n_chan = sky_map.shape[0]
    n_mode = fg_templates.shape[1]
    chan_dev = n_chan // n_blk
    m_width = M_DEV * n_grp
    n_cycle = cycle_dev * n_blk * n_grp
    slots = jnp.arange(RPIX, dtype=jnp.int32)
    valid = (slots[None, :] < cycle_len[:, None]).reshape(-1)
    masked = jnp.where(valid[None, :], sky_map, jnp.zeros((), jnp.bfloat16))
    mode_amps = jnp.dot(fg_templates.T, masked, preferred_element_type=jnp.float32).astype(
        jnp.bfloat16
    )
    gram_part = jnp.dot(mode_amps, mode_amps.T, preferred_element_type=jnp.float32)
    cross_part = lax.dot_general(
        mode_amps, masked, (((1,), (1,)), ((), ())), preferred_element_type=jnp.float32
    )
    amps_wide = mode_amps.astype(jnp.float32)
    tables = cycle_tables(cycle_len, m_width)
    subs = sub_axes(n_blk, n_grp)
    sums = ring_sum(jnp.concatenate([gram_part, cross_part], axis=1), subs)
    gram_sum = sums[:, :n_mode]
    cross_sum = sums[:, n_mode:]
    lower = jnp.linalg.cholesky(gram_sum)
    basis = jax.scipy.linalg.solve_triangular(lower, amps_wide, lower=True)
    projected = jax.scipy.linalg.solve_triangular(lower, cross_sum, lower=True)
    sendbuf = cycle_fourier(sky_map, projected.T, basis, tables, cycle_len, n_blk, n_grp)
    moved = lax.all_to_all(sendbuf, ("blk", "grp"), 0, 0, tiled=True)
    moved = moved.reshape(n_cycle, chan_dev * 2 * M_DEV)
    theta_tab = theta_table(jnp.arange(n_cycle, dtype=jnp.int32), n_cycle)
    onehot = (
        beam_index[:, None] == jnp.arange(beam_profile.shape[0], dtype=jnp.int32)[None, :]
    ).astype(jnp.float32)
    profiles = jnp.dot(onehot, beam_profile, precision=lax.Precision.HIGHEST)
    orders = lax.axis_index("grp") * M_DEV + jnp.arange(M_DEV, dtype=jnp.int32)
    mweight = 0.25 + orders.astype(jnp.float32) / m_width
    mw_row = jnp.concatenate([mweight, mweight])[None, :]
    prof_col = profiles[:, :, None]
    width = 2 * M_DEV
    specs = harmonic_specs(L, n_cycle, width)
    vmem = pltpu.CompilerParams(vmem_limit_bytes=32 * 1024 * 1024)
    power_part = pl.pallas_call(
        power_kernel,
        grid=(chan_dev,),
        in_specs=specs,
        out_specs=pl.BlockSpec((1, 1, 128), lambda c: (c, 0, 0)),
        out_shape=jax.ShapeDtypeStruct((chan_dev, 1, 128), jnp.float32),
        compiler_params=vmem,
    )(theta_tab, moved, prof_col, mw_row)[:, 0, 0]
    power = ring_sum(power_part, subs[3:])
    scale = lax.rsqrt(power / (2.0 * L * m_width) + 1e-06)
    scale = jnp.broadcast_to(scale[:, None, None], (chan_dev, 1, 128))
    return pl.pallas_call(
        output_kernel,
        grid=(chan_dev,),
        in_specs=specs + [pl.BlockSpec((1, 1, 128), lambda c: (c, 0, 0))],
        out_specs=pl.BlockSpec((L, 1, 2, M_DEV), lambda c: (0, c, 0, 0)),
        out_shape=jax.ShapeDtypeStruct((L, chan_dev, 2, M_DEV), jnp.float32),
        compiler_params=vmem,
    )(theta_tab, moved, prof_col, mw_row, scale)


def solution(mesh):
    return jax.shard_map(
        body,
        mesh=mesh,
        in_specs=(P(None, ("blk", "grp")), P(), P(("blk", "grp")), P(), P("blk")),
        out_specs=P(None, "blk", None, "grp"),
        check_vma=False,
    )
```

```python
import jax
import jax.numpy as jnp
from jax import lax
from jax.sharding import PartitionSpec as P
from jax.experimental import pallas as pl
from jax.experimental.pallas import tpu as pltpu

RPIX = 2048
L = 1024
M_DEV = 256
J_LO = 128


def cos_sin_of_phase(phase, length):
    angle = jnp.pi * phase.astype(jnp.float32) / length.astype(jnp.float32)
    return jnp.cos(angle), jnp.sin(angle)


def add_angles(ca, sa, cb, sb):
    return ca * cb - sa * sb, sa * cb + ca * sb


def small_tables(cycle_len, m_width):
    length = cycle_len[:, None, None]
    period = 2 * length
    orders = jnp.arange(m_width, dtype=jnp.int32)[None, None, :]
    j_hi = jnp.arange(RPIX // J_LO, dtype=jnp.int32)[None, :, None]
    j_mid = jnp.arange(J_LO // 16, dtype=jnp.int32)[None, :, None]
    j_q = jnp.arange(16, dtype=jnp.int32)[None, :, None]
    ca, sa = cos_sin_of_phase((2 * J_LO * j_hi) % period * orders % period, length)
    cm, sm = cos_sin_of_phase((32 * j_mid) % period * orders % period, length)
    cq, sq = cos_sin_of_phase(orders * (2 * j_q + 1) % period, length)
    cb, sb = add_angles(cm[:, :, None, :], sm[:, :, None, :], cq[:, None, :, :], sq[:, None, :, :])
    n_cyc = cycle_len.shape[0]
    cb = cb.reshape(n_cyc, J_LO, m_width)
    sb = sb.reshape(n_cyc, J_LO, m_width)
    return ca, sa, cb, sb


def table_kernel(ca_ref, sa_ref, cb_ref, sb_ref, inv_ref, len_ref, tab_ref):
    m_width = cb_ref.shape[2]
    inv = inv_ref[0][:, 0:1]
    length = len_ref[0][:, 0:1]

    def build(t, carry):
        ca = ca_ref[0, pl.ds(t, 1), :] * inv
        sa = sa_ref[0, pl.ds(t, 1), :] * inv
        cb = cb_ref[0]
        sb = sb_ref[0]
        rows = t * J_LO + lax.broadcasted_iota(jnp.int32, (J_LO, 1), 0)
        keep = rows < length
        cos_t = ca * cb - sa * sb
        neg_sin_t = (-sa) * cb - ca * sb
        r0 = pl.multiple_of(t * J_LO, J_LO)
        tab_ref[0, pl.ds(r0, J_LO), 0:m_width] = jnp.where(keep, cos_t, 0.0).astype(jnp.bfloat16)
        tab_ref[0, pl.ds(r0, J_LO), m_width : 2 * m_width] = jnp.where(keep, neg_sin_t, 0.0).astype(
            jnp.bfloat16
        )
        return carry

    lax.fori_loop(0, RPIX // J_LO, build, 0)


def cycle_tables(cycle_len, m_width):
    n_cyc = cycle_len.shape[0]
    ca, sa, cb, sb = small_tables(cycle_len, m_width)
    inv = jnp.broadcast_to(lax.rsqrt(cycle_len.astype(jnp.float32))[:, None, None], (n_cyc, 1, 128))
    lens = jnp.broadcast_to(cycle_len[:, None, None], (n_cyc, 1, 128))
    n_hi = RPIX // J_LO
    return pl.pallas_call(
        table_kernel,
        grid=(n_cyc,),
        in_specs=[
            pl.BlockSpec((1, n_hi, m_width), lambda k: (k, 0, 0)),
            pl.BlockSpec((1, n_hi, m_width), lambda k: (k, 0, 0)),
            pl.BlockSpec((1, J_LO, m_width), lambda k: (k, 0, 0)),
            pl.BlockSpec((1, J_LO, m_width), lambda k: (k, 0, 0)),
            pl.BlockSpec((1, 1, 128), lambda k: (k, 0, 0)),
            pl.BlockSpec((1, 1, 128), lambda k: (k, 0, 0)),
        ],
        out_specs=pl.BlockSpec((1, RPIX, 2 * m_width), lambda k: (k, 0, 0)),
        out_shape=jax.ShapeDtypeStruct((n_cyc, RPIX, 2 * m_width), jnp.bfloat16),
        compiler_params=pltpu.CompilerParams(vmem_limit_bytes=40 * 1024 * 1024),
    )(ca, sa, cb, sb, inv, lens)


def fourier_kernel(len_ref, sky_ref, proj_ref, basis_ref, tab_ref, o_ref, clean_ref):
    m_width = tab_ref.shape[2] // 2
    n_grp = o_ref.shape[0] // (sky_ref.shape[0] // o_ref.shape[1])
    chan_dev = o_ref.shape[1]
    length = len_ref[0][:, 0:1]
    cols = lax.broadcasted_iota(jnp.int32, (1, RPIX), 1)
    masked = jnp.where(cols < length, sky_ref[...].astype(jnp.float32), 0.0)
    correction = jnp.dot(
        proj_ref[...], basis_ref[...], preferred_element_type=jnp.float32,
        precision=lax.Precision.HIGHEST,
    )
    clean_ref[...] = (masked - correction).astype(jnp.bfloat16)
    m_dev = m_width // n_grp
    step = 2 * m_dev
    n_blk = sky_ref.shape[0] // chan_dev
    for q in range(2 * m_width // step):
        res = jnp.dot(
            clean_ref[...], tab_ref[0, :, q * step : (q + 1) * step], preferred_element_type=jnp.float32
        )
        part = (q * step) // m_width
        for h in range(step // m_dev):
            grp_dest = (q * step - part * m_width) // m_dev + h
            for blk_dest in range(n_blk):
                slab = res[blk_dest * chan_dev : (blk_dest + 1) * chan_dev, h * m_dev : (h + 1) * m_dev]
                o_ref[blk_dest * n_grp + grp_dest, :, part * m_dev : (part + 1) * m_dev] = slab.astype(
                    jnp.bfloat16
                )


def cycle_fourier(sky_map, projected_t, basis, tables, cycle_len, n_blk, n_grp):
    n_cyc = cycle_len.shape[0]
    n_chan = sky_map.shape[0]
    n_mode = basis.shape[0]
    n_dev = n_blk * n_grp
    chan_dev = n_chan // n_blk
    width = tables.shape[2]
    lens = jnp.broadcast_to(cycle_len[:, None, None], (n_cyc, 1, 128))
    m_dev = width // 2 // n_grp
    return pl.pallas_call(
        fourier_kernel,
        grid=(n_cyc,),
        in_specs=[
            pl.BlockSpec((1, 1, 128), lambda k: (k, 0, 0)),
            pl.BlockSpec((n_chan, RPIX), lambda k: (0, k)),
            pl.BlockSpec((n_chan, n_mode), lambda k: (0, 0)),
            pl.BlockSpec((n_mode, RPIX), lambda k: (0, k)),
            pl.BlockSpec((1, RPIX, width), lambda k: (k, 0, 0)),
        ],
        out_specs=pl.BlockSpec((n_dev, None, chan_dev, 2 * m_dev), lambda k: (0, k, 0, 0)),
        out_shape=jax.ShapeDtypeStruct((n_dev, n_cyc, chan_dev, 2 * m_dev), jnp.bfloat16),
        scratch_shapes=[pltpu.VMEM((n_chan, RPIX), jnp.bfloat16)],
        compiler_params=pltpu.CompilerParams(vmem_limit_bytes=48 * 1024 * 1024),
    )(lens, sky_map, projected_t, basis, tables)


def harmonic_tile(theta_ref, mv_ref, prof_ref, mw_ref, lc):
    rows = pl.ds(lc * 256, 256)
    h = jnp.dot(theta_ref[rows, :], mv_ref[...], preferred_element_type=jnp.float32)
    return h * prof_ref[0, rows, :] * mw_ref[...]


def power_kernel(theta_ref, mv_ref, prof_ref, mw_ref, o_ref):
    total = jnp.zeros((1, 1), jnp.float32)
    for lc in range(theta_ref.shape[0] // 256):
        w = harmonic_tile(theta_ref, mv_ref, prof_ref, mw_ref, lc)
        total = total + jnp.sum(w * w, keepdims=True)
    o_ref[0] = jnp.broadcast_to(total, (1, 128))


def output_kernel(theta_ref, mv_ref, prof_ref, mw_ref, scale_ref, o_ref):
    scale = scale_ref[0][:, 0:1]
    half = mv_ref.shape[1] // 2
    for lc in range(theta_ref.shape[0] // 256):
        w = harmonic_tile(theta_ref, mv_ref, prof_ref, mw_ref, lc) * scale
        for p in range(2):
            o_ref[pl.ds(lc * 256, 256), 0, p, :] = w[:, p * half : (p + 1) * half]


def harmonic_specs(n_l, n_cycle, width):
    return [
        pl.BlockSpec((n_l, n_cycle), lambda c: (0, 0)),
        pl.BlockSpec((n_cycle, width), lambda c: (0, c)),
        pl.BlockSpec((1, n_l, 1), lambda c: (c, 0, 0)),
        pl.BlockSpec((1, width), lambda c: (0, 0)),
    ]


def theta_table(cycle_ids, n_cycle):
    degrees = jnp.arange(L, dtype=jnp.int32)
    odd = 2 * cycle_ids + 1
    phase = degrees[:, None] * odd[None, :] % (4 * n_cycle)
    angle = jnp.pi * phase.astype(jnp.float32) / (2.0 * n_cycle)
    weight = jnp.sin(jnp.pi * odd.astype(jnp.float32) / (2.0 * n_cycle)) * (
        2.0 / jnp.sqrt(jnp.float32(n_cycle))
    )
    return (jnp.cos(angle) * weight[None, :]).astype(jnp.bfloat16)


def sub_axes(n_blk, n_grp):
    return [
        ("blk", 2, 1, n_blk),
        ("blk", 4, 2, n_blk),
        ("blk", n_blk // 8, 8, n_blk),
        ("grp", n_grp, 1, n_grp),
    ]


def shift_perm(size, stride, total, k):
    pairs = []
    for i in range(total):
        c = (i // stride) % size
        pairs.append((i, i + ((c + k) % size - c) * stride))
    return pairs


def ring_sum(v, subs):
    for axis, size, stride, total in subs:
        parts = [lax.ppermute(v, axis, shift_perm(size, stride, total, k)) for k in range(1, size)]
        for part in parts:
            v = v + part
    return v


def body(sky_map, fg_templates, cycle_len, beam_profile, beam_index):
    n_blk = lax.axis_size("blk")
    n_grp = lax.axis_size("grp")
    cycle_dev = cycle_len.shape[0]
    n_chan = sky_map.shape[0]
    n_mode = fg_templates.shape[1]
    chan_dev = n_chan // n_blk
    m_width = M_DEV * n_grp
    n_cycle = cycle_dev * n_blk * n_grp
    slots = jnp.arange(RPIX, dtype=jnp.int32)
    valid = (slots[None, :] < cycle_len[:, None]).reshape(-1)
    masked = jnp.where(valid[None, :], sky_map, jnp.zeros((), jnp.bfloat16))
    mode_amps = jnp.dot(fg_templates.T, masked, preferred_element_type=jnp.float32).astype(
        jnp.bfloat16
    )
    gram_part = jnp.dot(mode_amps, mode_amps.T, preferred_element_type=jnp.float32)
    cross_part = lax.dot_general(
        mode_amps, masked, (((1,), (1,)), ((), ())), preferred_element_type=jnp.float32
    )
    amps_wide = mode_amps.astype(jnp.float32)
    tables = cycle_tables(cycle_len, m_width)
    subs = sub_axes(n_blk, n_grp)
    sums = ring_sum(jnp.concatenate([gram_part, cross_part], axis=1), subs)
    gram_sum = sums[:, :n_mode]
    cross_sum = sums[:, n_mode:]
    lower = jnp.linalg.cholesky(gram_sum)
    basis = jax.scipy.linalg.solve_triangular(lower, amps_wide, lower=True)
    projected = jax.scipy.linalg.solve_triangular(lower, cross_sum, lower=True)
    sendbuf = cycle_fourier(sky_map, projected.T, basis, tables, cycle_len, n_blk, n_grp)
    moved = lax.all_to_all(sendbuf, ("blk", "grp"), 0, 0, tiled=True)
    moved = moved.reshape(n_cycle, chan_dev * 2 * M_DEV)
    theta_tab = theta_table(jnp.arange(n_cycle, dtype=jnp.int32), n_cycle)
    onehot = (
        beam_index[:, None] == jnp.arange(beam_profile.shape[0], dtype=jnp.int32)[None, :]
    ).astype(jnp.float32)
    profiles = jnp.dot(onehot, beam_profile, precision=lax.Precision.HIGHEST)
    orders = lax.axis_index("grp") * M_DEV + jnp.arange(M_DEV, dtype=jnp.int32)
    mweight = 0.25 + orders.astype(jnp.float32) / m_width
    mw_row = jnp.concatenate([mweight, mweight])[None, :]
    prof_col = profiles[:, :, None]
    width = 2 * M_DEV
    specs = harmonic_specs(L, n_cycle, width)
    vmem = pltpu.CompilerParams(vmem_limit_bytes=32 * 1024 * 1024)
    power_part = pl.pallas_call(
        power_kernel,
        grid=(chan_dev,),
        in_specs=specs,
        out_specs=pl.BlockSpec((1, 1, 128), lambda c: (c, 0, 0)),
        out_shape=jax.ShapeDtypeStruct((chan_dev, 1, 128), jnp.float32),
        compiler_params=vmem,
    )(theta_tab, moved, prof_col, mw_row)[:, 0, 0]
    power = ring_sum(power_part, subs[3:])
    scale = lax.rsqrt(power / (2.0 * L * m_width) + 1e-06)
    scale = jnp.broadcast_to(scale[:, None, None], (chan_dev, 1, 128))
    return pl.pallas_call(
        output_kernel,
        grid=(chan_dev,),
        in_specs=specs + [pl.BlockSpec((1, 1, 128), lambda c: (c, 0, 0))],
        out_specs=pl.BlockSpec((L, 1, 2, M_DEV), lambda c: (0, c, 0, 0)),
        out_shape=jax.ShapeDtypeStruct((L, chan_dev, 2, M_DEV), jnp.float32),
        compiler_params=vmem,
    )(theta_tab, moved, prof_col, mw_row, scale)


def solution(mesh):
    return jax.shard_map(
        body,
        mesh=mesh,
        in_specs=(P(None, ("blk", "grp")), P(), P(("blk", "grp")), P(), P("blk")),
        out_specs=P(None, "blk", None, "grp"),
        check_vma=False,
    )
```

```python
import jax
import jax.numpy as jnp
from jax import lax
from jax.sharding import PartitionSpec as P
from jax.experimental import pallas as pl
from jax.experimental.pallas import tpu as pltpu

RPIX = 2048
L = 1024
M_DEV = 256
J_LO = 128


def cos_sin_of_phase(phase, length):
    angle = jnp.pi * phase.astype(jnp.float32) / length.astype(jnp.float32)
    return jnp.cos(angle), jnp.sin(angle)


def add_angles(ca, sa, cb, sb):
    return ca * cb - sa * sb, sa * cb + ca * sb


def small_tables(cycle_len, m_width):
    length = cycle_len[:, None, None]
    period = 2 * length
    orders = jnp.arange(m_width, dtype=jnp.int32)[None, None, :]
    j_hi = jnp.arange(RPIX // J_LO, dtype=jnp.int32)[None, :, None]
    j_mid = jnp.arange(J_LO // 16, dtype=jnp.int32)[None, :, None]
    j_q = jnp.arange(16, dtype=jnp.int32)[None, :, None]
    ca, sa = cos_sin_of_phase((2 * J_LO * j_hi) % period * orders % period, length)
    cm, sm = cos_sin_of_phase((32 * j_mid) % period * orders % period, length)
    cq, sq = cos_sin_of_phase(orders * (2 * j_q + 1) % period, length)
    cb, sb = add_angles(cm[:, :, None, :], sm[:, :, None, :], cq[:, None, :, :], sq[:, None, :, :])
    n_cyc = cycle_len.shape[0]
    cb = cb.reshape(n_cyc, J_LO, m_width)
    sb = sb.reshape(n_cyc, J_LO, m_width)
    return ca, sa, cb, sb


def table_kernel(ca_ref, sa_ref, cb_ref, sb_ref, inv_ref, len_ref, tab_ref):
    m_width = cb_ref.shape[2]
    inv = inv_ref[0][:, 0:1]
    length = len_ref[0][:, 0:1]

    def build(t, carry):
        ca = ca_ref[0, pl.ds(t, 1), :]
        sa = sa_ref[0, pl.ds(t, 1), :]
        cb = cb_ref[0]
        sb = sb_ref[0]
        rows = t * J_LO + lax.broadcasted_iota(jnp.int32, (J_LO, 1), 0)
        weight = jnp.where(rows < length, inv, 0.0)
        cos_t, sin_t = add_angles(ca, sa, cb, sb)
        r0 = pl.multiple_of(t * J_LO, J_LO)
        tab_ref[0, pl.ds(r0, J_LO), 0:m_width] = (cos_t * weight).astype(jnp.bfloat16)
        tab_ref[0, pl.ds(r0, J_LO), m_width : 2 * m_width] = (sin_t * -weight).astype(jnp.bfloat16)
        return carry

    lax.fori_loop(0, RPIX // J_LO, build, 0)


def cycle_tables(cycle_len, m_width):
    n_cyc = cycle_len.shape[0]
    ca, sa, cb, sb = small_tables(cycle_len, m_width)
    inv = jnp.broadcast_to(lax.rsqrt(cycle_len.astype(jnp.float32))[:, None, None], (n_cyc, 1, 128))
    lens = jnp.broadcast_to(cycle_len[:, None, None], (n_cyc, 1, 128))
    n_hi = RPIX // J_LO
    return pl.pallas_call(
        table_kernel,
        grid=(n_cyc,),
        in_specs=[
            pl.BlockSpec((1, n_hi, m_width), lambda k: (k, 0, 0)),
            pl.BlockSpec((1, n_hi, m_width), lambda k: (k, 0, 0)),
            pl.BlockSpec((1, J_LO, m_width), lambda k: (k, 0, 0)),
            pl.BlockSpec((1, J_LO, m_width), lambda k: (k, 0, 0)),
            pl.BlockSpec((1, 1, 128), lambda k: (k, 0, 0)),
            pl.BlockSpec((1, 1, 128), lambda k: (k, 0, 0)),
        ],
        out_specs=pl.BlockSpec((1, RPIX, 2 * m_width), lambda k: (k, 0, 0)),
        out_shape=jax.ShapeDtypeStruct((n_cyc, RPIX, 2 * m_width), jnp.bfloat16),
        compiler_params=pltpu.CompilerParams(vmem_limit_bytes=40 * 1024 * 1024),
    )(ca, sa, cb, sb, inv, lens)


def fourier_kernel(len_ref, sky_ref, proj_ref, basis_ref, tab_ref, o_ref, clean_ref):
    m_width = tab_ref.shape[2] // 2
    n_grp = o_ref.shape[0] // (sky_ref.shape[0] // o_ref.shape[1])
    chan_dev = o_ref.shape[1]
    length = len_ref[0][:, 0:1]
    cols = lax.broadcasted_iota(jnp.int32, (1, RPIX), 1)
    masked = jnp.where(cols < length, sky_ref[...].astype(jnp.float32), 0.0)
    correction = jnp.dot(
        proj_ref[...], basis_ref[...], preferred_element_type=jnp.float32,
        precision=lax.Precision.HIGHEST,
    )
    clean_ref[...] = (masked - correction).astype(jnp.bfloat16)
    m_dev = m_width // n_grp
    step = 2 * m_dev
    n_blk = sky_ref.shape[0] // chan_dev
    for q in range(2 * m_width // step):
        res = jnp.dot(
            clean_ref[...], tab_ref[0, :, q * step : (q + 1) * step], preferred_element_type=jnp.float32
        )
        part = (q * step) // m_width
        for h in range(step // m_dev):
            grp_dest = (q * step - part * m_width) // m_dev + h
            for blk_dest in range(n_blk):
                slab = res[blk_dest * chan_dev : (blk_dest + 1) * chan_dev, h * m_dev : (h + 1) * m_dev]
                o_ref[blk_dest * n_grp + grp_dest, :, part * m_dev : (part + 1) * m_dev] = slab.astype(
                    jnp.bfloat16
                )


def cycle_fourier(sky_map, projected_t, basis, tables, cycle_len, n_blk, n_grp):
    n_cyc = cycle_len.shape[0]
    n_chan = sky_map.shape[0]
    n_mode = basis.shape[0]
    n_dev = n_blk * n_grp
    chan_dev = n_chan // n_blk
    width = tables.shape[2]
    lens = jnp.broadcast_to(cycle_len[:, None, None], (n_cyc, 1, 128))
    m_dev = width // 2 // n_grp
    return pl.pallas_call(
        fourier_kernel,
        grid=(n_cyc,),
        in_specs=[
            pl.BlockSpec((1, 1, 128), lambda k: (k, 0, 0)),
            pl.BlockSpec((n_chan, RPIX), lambda k: (0, k)),
            pl.BlockSpec((n_chan, n_mode), lambda k: (0, 0)),
            pl.BlockSpec((n_mode, RPIX), lambda k: (0, k)),
            pl.BlockSpec((1, RPIX, width), lambda k: (k, 0, 0)),
        ],
        out_specs=pl.BlockSpec((n_dev, None, chan_dev, 2 * m_dev), lambda k: (0, k, 0, 0)),
        out_shape=jax.ShapeDtypeStruct((n_dev, n_cyc, chan_dev, 2 * m_dev), jnp.bfloat16),
        scratch_shapes=[pltpu.VMEM((n_chan, RPIX), jnp.bfloat16)],
        compiler_params=pltpu.CompilerParams(vmem_limit_bytes=48 * 1024 * 1024),
    )(lens, sky_map, projected_t, basis, tables)


CH_STEP = 2


def harmonic_tile(theta_ref, mv_ref, prof_ref, mw_ref, lc, ci):
    rows = pl.ds(lc * 256, 256)
    width = mw_ref.shape[1]
    h = jnp.dot(
        theta_ref[rows, :], mv_ref[:, ci * width : (ci + 1) * width], preferred_element_type=jnp.float32
    )
    return h * prof_ref[ci, rows, :] * mw_ref[...]


def power_kernel(theta_ref, mv_ref, prof_ref, mw_ref, o_ref):
    for ci in range(prof_ref.shape[0]):
        total = jnp.zeros((1, 1), jnp.float32)
        for lc in range(theta_ref.shape[0] // 256):
            w = harmonic_tile(theta_ref, mv_ref, prof_ref, mw_ref, lc, ci)
            total = total + jnp.sum(w * w, keepdims=True)
        o_ref[ci] = jnp.broadcast_to(total, (1, 128))


def output_kernel(theta_ref, mv_ref, prof_ref, mw_ref, scale_ref, o_ref):
    half = mw_ref.shape[1] // 2
    for ci in range(prof_ref.shape[0]):
        scale = scale_ref[ci][:, 0:1]
        for lc in range(theta_ref.shape[0] // 256):
            w = harmonic_tile(theta_ref, mv_ref, prof_ref, mw_ref, lc, ci) * scale
            for p in range(2):
                o_ref[pl.ds(lc * 256, 256), ci, p, :] = w[:, p * half : (p + 1) * half]


def harmonic_specs(n_l, n_cycle, width):
    return [
        pl.BlockSpec((n_l, n_cycle), lambda c: (0, 0)),
        pl.BlockSpec((n_cycle, CH_STEP * width), lambda c: (0, c)),
        pl.BlockSpec((CH_STEP, n_l, 1), lambda c: (c, 0, 0)),
        pl.BlockSpec((1, width), lambda c: (0, 0)),
    ]


def theta_table(cycle_ids, n_cycle):
    degrees = jnp.arange(L, dtype=jnp.int32)
    odd = 2 * cycle_ids + 1
    phase = degrees[:, None] * odd[None, :] % (4 * n_cycle)
    angle = jnp.pi * phase.astype(jnp.float32) / (2.0 * n_cycle)
    weight = jnp.sin(jnp.pi * odd.astype(jnp.float32) / (2.0 * n_cycle)) * (
        2.0 / jnp.sqrt(jnp.float32(n_cycle))
    )
    return (jnp.cos(angle) * weight[None, :]).astype(jnp.bfloat16)


def sub_axes(n_blk, n_grp):
    return [
        ("blk", 2, 1, n_blk),
        ("blk", 4, 2, n_blk),
        ("blk", n_blk // 8, 8, n_blk),
        ("grp", n_grp, 1, n_grp),
    ]


def shift_perm(size, stride, total, k):
    pairs = []
    for i in range(total):
        c = (i // stride) % size
        pairs.append((i, i + ((c + k) % size - c) * stride))
    return pairs


def ring_sum(v, subs):
    for axis, size, stride, total in subs:
        parts = [lax.ppermute(v, axis, shift_perm(size, stride, total, k)) for k in range(1, size)]
        for part in parts:
            v = v + part
    return v


def body(sky_map, fg_templates, cycle_len, beam_profile, beam_index):
    n_blk = lax.axis_size("blk")
    n_grp = lax.axis_size("grp")
    cycle_dev = cycle_len.shape[0]
    n_chan = sky_map.shape[0]
    n_mode = fg_templates.shape[1]
    chan_dev = n_chan // n_blk
    m_width = M_DEV * n_grp
    n_cycle = cycle_dev * n_blk * n_grp
    slots = jnp.arange(RPIX, dtype=jnp.int32)
    valid = (slots[None, :] < cycle_len[:, None]).reshape(-1)
    masked = jnp.where(valid[None, :], sky_map, jnp.zeros((), jnp.bfloat16))
    mode_amps = jnp.dot(fg_templates.T, masked, preferred_element_type=jnp.float32).astype(
        jnp.bfloat16
    )
    gram_part = jnp.dot(mode_amps, mode_amps.T, preferred_element_type=jnp.float32)
    cross_part = lax.dot_general(
        mode_amps, masked, (((1,), (1,)), ((), ())), preferred_element_type=jnp.float32
    )
    amps_wide = mode_amps.astype(jnp.float32)
    tables = cycle_tables(cycle_len, m_width)
    subs = sub_axes(n_blk, n_grp)
    sums = ring_sum(jnp.concatenate([gram_part, cross_part], axis=1), subs)
    gram_sum = sums[:, :n_mode]
    cross_sum = sums[:, n_mode:]
    lower = jnp.linalg.cholesky(gram_sum)
    basis = jax.scipy.linalg.solve_triangular(lower, amps_wide, lower=True)
    projected = jax.scipy.linalg.solve_triangular(lower, cross_sum, lower=True)
    sendbuf = cycle_fourier(sky_map, projected.T, basis, tables, cycle_len, n_blk, n_grp)
    moved = lax.all_to_all(sendbuf, ("blk", "grp"), 0, 0, tiled=True)
    moved = moved.reshape(n_cycle, chan_dev * 2 * M_DEV)
    theta_tab = theta_table(jnp.arange(n_cycle, dtype=jnp.int32), n_cycle)
    onehot = (
        beam_index[:, None] == jnp.arange(beam_profile.shape[0], dtype=jnp.int32)[None, :]
    ).astype(jnp.float32)
    profiles = jnp.dot(onehot, beam_profile, precision=lax.Precision.HIGHEST)
    orders = lax.axis_index("grp") * M_DEV + jnp.arange(M_DEV, dtype=jnp.int32)
    mweight = 0.25 + orders.astype(jnp.float32) / m_width
    mw_row = jnp.concatenate([mweight, mweight])[None, :]
    prof_col = profiles[:, :, None]
    width = 2 * M_DEV
    specs = harmonic_specs(L, n_cycle, width)
    vmem = pltpu.CompilerParams(vmem_limit_bytes=32 * 1024 * 1024)
    power_part = pl.pallas_call(
        power_kernel,
        grid=(chan_dev // CH_STEP,),
        in_specs=specs,
        out_specs=pl.BlockSpec((CH_STEP, 1, 128), lambda c: (c, 0, 0)),
        out_shape=jax.ShapeDtypeStruct((chan_dev, 1, 128), jnp.float32),
        compiler_params=vmem,
    )(theta_tab, moved, prof_col, mw_row)[:, 0, 0]
    power = ring_sum(power_part, subs[3:])
    scale = lax.rsqrt(power / (2.0 * L * m_width) + 1e-06)
    scale = jnp.broadcast_to(scale[:, None, None], (chan_dev, 1, 128))
    return pl.pallas_call(
        output_kernel,
        grid=(chan_dev // CH_STEP,),
        in_specs=specs + [pl.BlockSpec((CH_STEP, 1, 128), lambda c: (c, 0, 0))],
        out_specs=pl.BlockSpec((L, CH_STEP, 2, M_DEV), lambda c: (0, c, 0, 0)),
        out_shape=jax.ShapeDtypeStruct((L, chan_dev, 2, M_DEV), jnp.float32),
        compiler_params=vmem,
    )(theta_tab, moved, prof_col, mw_row, scale)


def solution(mesh):
    return jax.shard_map(
        body,
        mesh=mesh,
        in_specs=(P(None, ("blk", "grp")), P(), P(("blk", "grp")), P(), P("blk")),
        out_specs=P(None, "blk", None, "grp"),
        check_vma=False,
    )
```

```python
import jax
import jax.numpy as jnp
from jax import lax
from jax.sharding import PartitionSpec as P
from jax.experimental import pallas as pl
from jax.experimental.pallas import tpu as pltpu

RPIX = 2048
L = 1024
M_DEV = 256
J_LO = 128


def cos_sin_of_phase(phase, length):
    angle = jnp.pi * phase.astype(jnp.float32) / length.astype(jnp.float32)
    return jnp.cos(angle), jnp.sin(angle)


def add_angles(ca, sa, cb, sb):
    return ca * cb - sa * sb, sa * cb + ca * sb


def small_tables(cycle_len, m_width):
    length = cycle_len[:, None, None]
    period = 2 * length
    orders = jnp.arange(m_width, dtype=jnp.int32)[None, None, :]
    j_hi = jnp.arange(RPIX // J_LO, dtype=jnp.int32)[None, :, None]
    j_mid = jnp.arange(J_LO // 16, dtype=jnp.int32)[None, :, None]
    j_q = jnp.arange(16, dtype=jnp.int32)[None, :, None]
    ca, sa = cos_sin_of_phase((2 * J_LO * j_hi) % period * orders % period, length)
    cm, sm = cos_sin_of_phase((32 * j_mid) % period * orders % period, length)
    cq, sq = cos_sin_of_phase(orders * (2 * j_q + 1) % period, length)
    cb, sb = add_angles(cm[:, :, None, :], sm[:, :, None, :], cq[:, None, :, :], sq[:, None, :, :])
    n_cyc = cycle_len.shape[0]
    cb = cb.reshape(n_cyc, J_LO, m_width)
    sb = sb.reshape(n_cyc, J_LO, m_width)
    return ca, sa, cb, sb


def table_kernel(ca_ref, sa_ref, cb_ref, sb_ref, inv_ref, len_ref, tab_ref):
    m_width = cb_ref.shape[2]
    inv = inv_ref[0][:, 0:1]
    length = len_ref[0][:, 0:1]

    def build(t, carry):
        ca = ca_ref[0, pl.ds(t, 1), :]
        sa = sa_ref[0, pl.ds(t, 1), :]
        cb = cb_ref[0]
        sb = sb_ref[0]
        rows = t * J_LO + lax.broadcasted_iota(jnp.int32, (J_LO, 1), 0)
        weight = jnp.where(rows < length, inv, 0.0)
        cos_t, sin_t = add_angles(ca, sa, cb, sb)
        r0 = pl.multiple_of(t * J_LO, J_LO)
        tab_ref[0, pl.ds(r0, J_LO), 0:m_width] = (cos_t * weight).astype(jnp.bfloat16)
        tab_ref[0, pl.ds(r0, J_LO), m_width : 2 * m_width] = (sin_t * -weight).astype(jnp.bfloat16)
        return carry

    lax.fori_loop(0, RPIX // J_LO, build, 0)


def cycle_tables(cycle_len, m_width):
    n_cyc = cycle_len.shape[0]
    ca, sa, cb, sb = small_tables(cycle_len, m_width)
    inv = jnp.broadcast_to(lax.rsqrt(cycle_len.astype(jnp.float32))[:, None, None], (n_cyc, 1, 128))
    lens = jnp.broadcast_to(cycle_len[:, None, None], (n_cyc, 1, 128))
    n_hi = RPIX // J_LO
    return pl.pallas_call(
        table_kernel,
        grid=(n_cyc,),
        in_specs=[
            pl.BlockSpec((1, n_hi, m_width), lambda k: (k, 0, 0)),
            pl.BlockSpec((1, n_hi, m_width), lambda k: (k, 0, 0)),
            pl.BlockSpec((1, J_LO, m_width), lambda k: (k, 0, 0)),
            pl.BlockSpec((1, J_LO, m_width), lambda k: (k, 0, 0)),
            pl.BlockSpec((1, 1, 128), lambda k: (k, 0, 0)),
            pl.BlockSpec((1, 1, 128), lambda k: (k, 0, 0)),
        ],
        out_specs=pl.BlockSpec((1, RPIX, 2 * m_width), lambda k: (k, 0, 0)),
        out_shape=jax.ShapeDtypeStruct((n_cyc, RPIX, 2 * m_width), jnp.bfloat16),
        compiler_params=pltpu.CompilerParams(vmem_limit_bytes=40 * 1024 * 1024),
    )(ca, sa, cb, sb, inv, lens)


def fourier_kernel(len_ref, sky_ref, proj_ref, basis_ref, tab_ref, o_ref, clean_ref):
    m_width = tab_ref.shape[2] // 2
    n_grp = o_ref.shape[0] // (sky_ref.shape[0] // o_ref.shape[1])
    chan_dev = o_ref.shape[1]
    length = len_ref[0][:, 0:1]
    cols = lax.broadcasted_iota(jnp.int32, (1, RPIX), 1)
    masked = jnp.where(cols < length, sky_ref[...].astype(jnp.float32), 0.0)
    correction = jnp.dot(
        proj_ref[...], basis_ref[...], preferred_element_type=jnp.float32,
        precision=lax.Precision.HIGHEST,
    )
    clean_ref[...] = (masked - correction).astype(jnp.bfloat16)
    m_dev = m_width // n_grp
    step = 2 * m_dev
    n_blk = sky_ref.shape[0] // chan_dev
    for q in range(2 * m_width // step):
        res = jnp.dot(
            clean_ref[...], tab_ref[0, :, q * step : (q + 1) * step], preferred_element_type=jnp.float32
        )
        part = (q * step) // m_width
        for h in range(step // m_dev):
            grp_dest = (q * step - part * m_width) // m_dev + h
            for blk_dest in range(n_blk):
                slab = res[blk_dest * chan_dev : (blk_dest + 1) * chan_dev, h * m_dev : (h + 1) * m_dev]
                o_ref[blk_dest * n_grp + grp_dest, :, part * m_dev : (part + 1) * m_dev] = slab.astype(
                    jnp.bfloat16
                )


def cycle_fourier(sky_map, projected_t, basis, tables, cycle_len, n_blk, n_grp):
    n_cyc = cycle_len.shape[0]
    n_chan = sky_map.shape[0]
    n_mode = basis.shape[0]
    n_dev = n_blk * n_grp
    chan_dev = n_chan // n_blk
    width = tables.shape[2]
    lens = jnp.broadcast_to(cycle_len[:, None, None], (n_cyc, 1, 128))
    m_dev = width // 2 // n_grp
    return pl.pallas_call(
        fourier_kernel,
        grid=(n_cyc,),
        in_specs=[
            pl.BlockSpec((1, 1, 128), lambda k: (k, 0, 0)),
            pl.BlockSpec((n_chan, RPIX), lambda k: (0, k)),
            pl.BlockSpec((n_chan, n_mode), lambda k: (0, 0)),
            pl.BlockSpec((n_mode, RPIX), lambda k: (0, k)),
            pl.BlockSpec((1, RPIX, width), lambda k: (k, 0, 0)),
        ],
        out_specs=pl.BlockSpec((n_dev, None, chan_dev, 2 * m_dev), lambda k: (0, k, 0, 0)),
        out_shape=jax.ShapeDtypeStruct((n_dev, n_cyc, chan_dev, 2 * m_dev), jnp.bfloat16),
        scratch_shapes=[pltpu.VMEM((n_chan, RPIX), jnp.bfloat16)],
        compiler_params=pltpu.CompilerParams(vmem_limit_bytes=48 * 1024 * 1024),
    )(lens, sky_map, projected_t, basis, tables)


POWER_STEP = 4
OUT_STEP = 1


def harmonic_tile(theta_ref, mv_ref, prof_ref, mw_ref, lc, ci):
    rows = pl.ds(lc * 256, 256)
    width = mw_ref.shape[1]
    h = jnp.dot(
        theta_ref[rows, :], mv_ref[:, ci * width : (ci + 1) * width], preferred_element_type=jnp.float32
    )
    return h * prof_ref[ci, rows, :] * mw_ref[...]


def power_kernel(theta_ref, mv_ref, prof_ref, mw_ref, o_ref):
    for ci in range(prof_ref.shape[0]):
        total = jnp.zeros((1, 1), jnp.float32)
        for lc in range(theta_ref.shape[0] // 256):
            w = harmonic_tile(theta_ref, mv_ref, prof_ref, mw_ref, lc, ci)
            total = total + jnp.sum(w * w, keepdims=True)
        o_ref[ci] = jnp.broadcast_to(total, (1, 128))


def output_kernel(theta_ref, mv_ref, prof_ref, mw_ref, scale_ref, o_ref):
    half = mw_ref.shape[1] // 2
    for ci in range(prof_ref.shape[0]):
        scale = scale_ref[ci][:, 0:1]
        for lc in range(theta_ref.shape[0] // 256):
            w = harmonic_tile(theta_ref, mv_ref, prof_ref, mw_ref, lc, ci) * scale
            for p in range(2):
                o_ref[pl.ds(lc * 256, 256), ci, p, :] = w[:, p * half : (p + 1) * half]


def harmonic_specs(n_l, n_cycle, width, step):
    return [
        pl.BlockSpec((n_l, n_cycle), lambda c: (0, 0)),
        pl.BlockSpec((n_cycle, step * width), lambda c: (0, c)),
        pl.BlockSpec((step, n_l, 1), lambda c: (c, 0, 0)),
        pl.BlockSpec((1, width), lambda c: (0, 0)),
    ]


def theta_table(cycle_ids, n_cycle):
    degrees = jnp.arange(L, dtype=jnp.int32)
    odd = 2 * cycle_ids + 1
    phase = degrees[:, None] * odd[None, :] % (4 * n_cycle)
    angle = jnp.pi * phase.astype(jnp.float32) / (2.0 * n_cycle)
    weight = jnp.sin(jnp.pi * odd.astype(jnp.float32) / (2.0 * n_cycle)) * (
        2.0 / jnp.sqrt(jnp.float32(n_cycle))
    )
    return (jnp.cos(angle) * weight[None, :]).astype(jnp.bfloat16)


def sub_axes(n_blk, n_grp):
    return [
        ("blk", 2, 1, n_blk),
        ("blk", 4, 2, n_blk),
        ("blk", n_blk // 8, 8, n_blk),
        ("grp", n_grp, 1, n_grp),
    ]


def shift_perm(size, stride, total, k):
    pairs = []
    for i in range(total):
        c = (i // stride) % size
        pairs.append((i, i + ((c + k) % size - c) * stride))
    return pairs


def ring_sum(v, subs):
    for axis, size, stride, total in subs:
        parts = [lax.ppermute(v, axis, shift_perm(size, stride, total, k)) for k in range(1, size)]
        for part in parts:
            v = v + part
    return v


def body(sky_map, fg_templates, cycle_len, beam_profile, beam_index):
    n_blk = lax.axis_size("blk")
    n_grp = lax.axis_size("grp")
    cycle_dev = cycle_len.shape[0]
    n_chan = sky_map.shape[0]
    n_mode = fg_templates.shape[1]
    chan_dev = n_chan // n_blk
    m_width = M_DEV * n_grp
    n_cycle = cycle_dev * n_blk * n_grp
    slots = jnp.arange(RPIX, dtype=jnp.int32)
    valid = (slots[None, :] < cycle_len[:, None]).reshape(-1)
    masked = jnp.where(valid[None, :], sky_map, jnp.zeros((), jnp.bfloat16))
    mode_amps = jnp.dot(fg_templates.T, masked, preferred_element_type=jnp.float32).astype(
        jnp.bfloat16
    )
    gram_part = jnp.dot(mode_amps, mode_amps.T, preferred_element_type=jnp.float32)
    cross_part = lax.dot_general(
        mode_amps, masked, (((1,), (1,)), ((), ())), preferred_element_type=jnp.float32
    )
    amps_wide = mode_amps.astype(jnp.float32)
    tables = cycle_tables(cycle_len, m_width)
    subs = sub_axes(n_blk, n_grp)
    sums = ring_sum(jnp.concatenate([gram_part, cross_part], axis=1), subs)
    gram_sum = sums[:, :n_mode]
    cross_sum = sums[:, n_mode:]
    lower = jnp.linalg.cholesky(gram_sum)
    basis = jax.scipy.linalg.solve_triangular(lower, amps_wide, lower=True)
    projected = jax.scipy.linalg.solve_triangular(lower, cross_sum, lower=True)
    sendbuf = cycle_fourier(sky_map, projected.T, basis, tables, cycle_len, n_blk, n_grp)
    moved = lax.all_to_all(sendbuf, ("blk", "grp"), 0, 0, tiled=True)
    moved = moved.reshape(n_cycle, chan_dev * 2 * M_DEV)
    theta_tab = theta_table(jnp.arange(n_cycle, dtype=jnp.int32), n_cycle)
    onehot = (
        beam_index[:, None] == jnp.arange(beam_profile.shape[0], dtype=jnp.int32)[None, :]
    ).astype(jnp.float32)
    profiles = jnp.dot(onehot, beam_profile, precision=lax.Precision.HIGHEST)
    orders = lax.axis_index("grp") * M_DEV + jnp.arange(M_DEV, dtype=jnp.int32)
    mweight = 0.25 + orders.astype(jnp.float32) / m_width
    mw_row = jnp.concatenate([mweight, mweight])[None, :]
    prof_col = profiles[:, :, None]
    width = 2 * M_DEV
    vmem = pltpu.CompilerParams(vmem_limit_bytes=32 * 1024 * 1024)
    power_part = pl.pallas_call(
        power_kernel,
        grid=(chan_dev // POWER_STEP,),
        in_specs=harmonic_specs(L, n_cycle, width, POWER_STEP),
        out_specs=pl.BlockSpec((POWER_STEP, 1, 128), lambda c: (c, 0, 0)),
        out_shape=jax.ShapeDtypeStruct((chan_dev, 1, 128), jnp.float32),
        compiler_params=vmem,
    )(theta_tab, moved, prof_col, mw_row)[:, 0, 0]
    power = ring_sum(power_part, subs[3:])
    scale = lax.rsqrt(power / (2.0 * L * m_width) + 1e-06)
    scale = jnp.broadcast_to(scale[:, None, None], (chan_dev, 1, 128))
    return pl.pallas_call(
        output_kernel,
        grid=(chan_dev // OUT_STEP,),
        in_specs=harmonic_specs(L, n_cycle, width, OUT_STEP)
        + [pl.BlockSpec((OUT_STEP, 1, 128), lambda c: (c, 0, 0))],
        out_specs=pl.BlockSpec((L, OUT_STEP, 2, M_DEV), lambda c: (0, c, 0, 0)),
        out_shape=jax.ShapeDtypeStruct((L, chan_dev, 2, M_DEV), jnp.float32),
        compiler_params=vmem,
    )(theta_tab, moved, prof_col, mw_row, scale)


def solution(mesh):
    return jax.shard_map(
        body,
        mesh=mesh,
        in_specs=(P(None, ("blk", "grp")), P(), P(("blk", "grp")), P(), P("blk")),
        out_specs=P(None, "blk", None, "grp"),
        check_vma=False,
    )
```

```python
import jax
import jax.numpy as jnp
from jax import lax
from jax.sharding import PartitionSpec as P
from jax.experimental import pallas as pl
from jax.experimental.pallas import tpu as pltpu

RPIX = 2048
L = 1024
M_DEV = 256
J_LO = 128


def cos_sin_of_phase(phase, length):
    angle = jnp.pi * phase.astype(jnp.float32) / length.astype(jnp.float32)
    return jnp.cos(angle), jnp.sin(angle)


def add_angles(ca, sa, cb, sb):
    return ca * cb - sa * sb, sa * cb + ca * sb


def small_tables(cycle_len, m_width):
    length = cycle_len[:, None, None]
    period = 2 * length
    orders = jnp.arange(m_width, dtype=jnp.int32)[None, None, :]
    j_hi = jnp.arange(RPIX // J_LO, dtype=jnp.int32)[None, :, None]
    j_mid = jnp.arange(J_LO // 16, dtype=jnp.int32)[None, :, None]
    j_q = jnp.arange(16, dtype=jnp.int32)[None, :, None]
    ca, sa = cos_sin_of_phase((2 * J_LO * j_hi) % period * orders % period, length)
    cm, sm = cos_sin_of_phase((32 * j_mid) % period * orders % period, length)
    cq, sq = cos_sin_of_phase(orders * (2 * j_q + 1) % period, length)
    cb, sb = add_angles(cm[:, :, None, :], sm[:, :, None, :], cq[:, None, :, :], sq[:, None, :, :])
    n_cyc = cycle_len.shape[0]
    cb = cb.reshape(n_cyc, J_LO, m_width)
    sb = sb.reshape(n_cyc, J_LO, m_width)
    return ca, sa, cb, sb


def table_kernel(ca_ref, sa_ref, cb_ref, sb_ref, inv_ref, len_ref, tab_ref):
    m_width = cb_ref.shape[2]
    inv = inv_ref[0][:, 0:1]
    length = len_ref[0][:, 0:1]

    def build(t, carry):
        ca = ca_ref[0, pl.ds(t, 1), :]
        sa = sa_ref[0, pl.ds(t, 1), :]
        cb = cb_ref[0]
        sb = sb_ref[0]
        rows = t * J_LO + lax.broadcasted_iota(jnp.int32, (J_LO, 1), 0)
        weight = jnp.where(rows < length, inv, 0.0)
        cos_t, sin_t = add_angles(ca, sa, cb, sb)
        r0 = pl.multiple_of(t * J_LO, J_LO)
        tab_ref[0, pl.ds(r0, J_LO), 0:m_width] = (cos_t * weight).astype(jnp.bfloat16)
        tab_ref[0, pl.ds(r0, J_LO), m_width : 2 * m_width] = (sin_t * -weight).astype(jnp.bfloat16)
        return carry

    lax.fori_loop(0, RPIX // J_LO, build, 0, unroll=2)


def cycle_tables(cycle_len, m_width):
    n_cyc = cycle_len.shape[0]
    ca, sa, cb, sb = small_tables(cycle_len, m_width)
    inv = jnp.broadcast_to(lax.rsqrt(cycle_len.astype(jnp.float32))[:, None, None], (n_cyc, 1, 128))
    lens = jnp.broadcast_to(cycle_len[:, None, None], (n_cyc, 1, 128))
    n_hi = RPIX // J_LO
    return pl.pallas_call(
        table_kernel,
        grid=(n_cyc,),
        in_specs=[
            pl.BlockSpec((1, n_hi, m_width), lambda k: (k, 0, 0)),
            pl.BlockSpec((1, n_hi, m_width), lambda k: (k, 0, 0)),
            pl.BlockSpec((1, J_LO, m_width), lambda k: (k, 0, 0)),
            pl.BlockSpec((1, J_LO, m_width), lambda k: (k, 0, 0)),
            pl.BlockSpec((1, 1, 128), lambda k: (k, 0, 0)),
            pl.BlockSpec((1, 1, 128), lambda k: (k, 0, 0)),
        ],
        out_specs=pl.BlockSpec((1, RPIX, 2 * m_width), lambda k: (k, 0, 0)),
        out_shape=jax.ShapeDtypeStruct((n_cyc, RPIX, 2 * m_width), jnp.bfloat16),
        compiler_params=pltpu.CompilerParams(vmem_limit_bytes=40 * 1024 * 1024),
    )(ca, sa, cb, sb, inv, lens)


def fourier_kernel(len_ref, sky_ref, proj_ref, basis_ref, tab_ref, o_ref, clean_ref):
    m_width = tab_ref.shape[2] // 2
    n_grp = o_ref.shape[0] // (sky_ref.shape[0] // o_ref.shape[1])
    chan_dev = o_ref.shape[1]
    length = len_ref[0][:, 0:1]
    cols = lax.broadcasted_iota(jnp.int32, (1, RPIX), 1)
    masked = jnp.where(cols < length, sky_ref[...].astype(jnp.float32), 0.0)
    correction = jnp.dot(
        proj_ref[...], basis_ref[...], preferred_element_type=jnp.float32,
        precision=lax.Precision.HIGHEST,
    )
    clean_ref[...] = (masked - correction).astype(jnp.bfloat16)
    m_dev = m_width // n_grp
    step = 2 * m_dev
    n_blk = sky_ref.shape[0] // chan_dev
    for q in range(2 * m_width // step):
        res = jnp.dot(
            clean_ref[...], tab_ref[0, :, q * step : (q + 1) * step], preferred_element_type=jnp.float32
        )
        part = (q * step) // m_width
        for h in range(step // m_dev):
            grp_dest = (q * step - part * m_width) // m_dev + h
            for blk_dest in range(n_blk):
                slab = res[blk_dest * chan_dev : (blk_dest + 1) * chan_dev, h * m_dev : (h + 1) * m_dev]
                o_ref[blk_dest * n_grp + grp_dest, :, part * m_dev : (part + 1) * m_dev] = slab.astype(
                    jnp.bfloat16
                )


def cycle_fourier(sky_map, projected_t, basis, tables, cycle_len, n_blk, n_grp):
    n_cyc = cycle_len.shape[0]
    n_chan = sky_map.shape[0]
    n_mode = basis.shape[0]
    n_dev = n_blk * n_grp
    chan_dev = n_chan // n_blk
    width = tables.shape[2]
    lens = jnp.broadcast_to(cycle_len[:, None, None], (n_cyc, 1, 128))
    m_dev = width // 2 // n_grp
    return pl.pallas_call(
        fourier_kernel,
        grid=(n_cyc,),
        in_specs=[
            pl.BlockSpec((1, 1, 128), lambda k: (k, 0, 0)),
            pl.BlockSpec((n_chan, RPIX), lambda k: (0, k)),
            pl.BlockSpec((n_chan, n_mode), lambda k: (0, 0)),
            pl.BlockSpec((n_mode, RPIX), lambda k: (0, k)),
            pl.BlockSpec((1, RPIX, width), lambda k: (k, 0, 0)),
        ],
        out_specs=pl.BlockSpec((n_dev, None, chan_dev, 2 * m_dev), lambda k: (0, k, 0, 0)),
        out_shape=jax.ShapeDtypeStruct((n_dev, n_cyc, chan_dev, 2 * m_dev), jnp.bfloat16),
        scratch_shapes=[pltpu.VMEM((n_chan, RPIX), jnp.bfloat16)],
        compiler_params=pltpu.CompilerParams(vmem_limit_bytes=48 * 1024 * 1024),
    )(lens, sky_map, projected_t, basis, tables)


POWER_STEP = 8
OUT_STEP = 1


def harmonic_tile(theta_ref, mv_ref, prof_ref, mw_ref, lc, ci):
    rows = pl.ds(lc * 256, 256)
    width = mw_ref.shape[1]
    h = jnp.dot(
        theta_ref[rows, :], mv_ref[:, ci * width : (ci + 1) * width], preferred_element_type=jnp.float32
    )
    return h * prof_ref[ci, rows, :] * mw_ref[...]


def power_kernel(theta_ref, mv_ref, prof_ref, mw_ref, o_ref):
    for ci in range(prof_ref.shape[0]):
        total = jnp.zeros((1, 1), jnp.float32)
        for lc in range(theta_ref.shape[0] // 256):
            w = harmonic_tile(theta_ref, mv_ref, prof_ref, mw_ref, lc, ci)
            total = total + jnp.sum(w * w, keepdims=True)
        o_ref[ci] = jnp.broadcast_to(total, (1, 128))


def output_kernel(theta_ref, mv_ref, prof_ref, mw_ref, scale_ref, o_ref):
    half = mw_ref.shape[1] // 2
    for ci in range(prof_ref.shape[0]):
        scale = scale_ref[ci][:, 0:1]
        for lc in range(theta_ref.shape[0] // 256):
            w = harmonic_tile(theta_ref, mv_ref, prof_ref, mw_ref, lc, ci) * scale
            for p in range(2):
                o_ref[pl.ds(lc * 256, 256), ci, p, :] = w[:, p * half : (p + 1) * half]


def harmonic_specs(n_l, n_cycle, width, step):
    return [
        pl.BlockSpec((n_l, n_cycle), lambda c: (0, 0)),
        pl.BlockSpec((n_cycle, step * width), lambda c: (0, c)),
        pl.BlockSpec((step, n_l, 1), lambda c: (c, 0, 0)),
        pl.BlockSpec((1, width), lambda c: (0, 0)),
    ]


def theta_table(cycle_ids, n_cycle):
    degrees = jnp.arange(L, dtype=jnp.int32)
    odd = 2 * cycle_ids + 1
    phase = degrees[:, None] * odd[None, :] % (4 * n_cycle)
    angle = jnp.pi * phase.astype(jnp.float32) / (2.0 * n_cycle)
    weight = jnp.sin(jnp.pi * odd.astype(jnp.float32) / (2.0 * n_cycle)) * (
        2.0 / jnp.sqrt(jnp.float32(n_cycle))
    )
    return (jnp.cos(angle) * weight[None, :]).astype(jnp.bfloat16)


def sub_axes(n_blk, n_grp):
    return [
        ("blk", 2, 1, n_blk),
        ("blk", 4, 2, n_blk),
        ("blk", n_blk // 8, 8, n_blk),
        ("grp", n_grp, 1, n_grp),
    ]


def shift_perm(size, stride, total, k):
    pairs = []
    for i in range(total):
        c = (i // stride) % size
        pairs.append((i, i + ((c + k) % size - c) * stride))
    return pairs


def ring_sum(v, subs):
    for axis, size, stride, total in subs:
        parts = [lax.ppermute(v, axis, shift_perm(size, stride, total, k)) for k in range(1, size)]
        for part in parts:
            v = v + part
    return v


def body(sky_map, fg_templates, cycle_len, beam_profile, beam_index):
    n_blk = lax.axis_size("blk")
    n_grp = lax.axis_size("grp")
    cycle_dev = cycle_len.shape[0]
    n_chan = sky_map.shape[0]
    n_mode = fg_templates.shape[1]
    chan_dev = n_chan // n_blk
    m_width = M_DEV * n_grp
    n_cycle = cycle_dev * n_blk * n_grp
    slots = jnp.arange(RPIX, dtype=jnp.int32)
    valid = (slots[None, :] < cycle_len[:, None]).reshape(-1)
    masked = jnp.where(valid[None, :], sky_map, jnp.zeros((), jnp.bfloat16))
    mode_amps = jnp.dot(fg_templates.T, masked, preferred_element_type=jnp.float32).astype(
        jnp.bfloat16
    )
    gram_part = jnp.dot(mode_amps, mode_amps.T, preferred_element_type=jnp.float32)
    cross_part = lax.dot_general(
        mode_amps, masked, (((1,), (1,)), ((), ())), preferred_element_type=jnp.float32
    )
    amps_wide = mode_amps.astype(jnp.float32)
    tables = cycle_tables(cycle_len, m_width)
    subs = sub_axes(n_blk, n_grp)
    sums = ring_sum(jnp.concatenate([gram_part, cross_part], axis=1), subs)
    gram_sum = sums[:, :n_mode]
    cross_sum = sums[:, n_mode:]
    lower = jnp.linalg.cholesky(gram_sum)
    basis = jax.scipy.linalg.solve_triangular(lower, amps_wide, lower=True)
    projected = jax.scipy.linalg.solve_triangular(lower, cross_sum, lower=True)
    sendbuf = cycle_fourier(sky_map, projected.T, basis, tables, cycle_len, n_blk, n_grp)
    moved = lax.all_to_all(sendbuf, ("blk", "grp"), 0, 0, tiled=True)
    moved = moved.reshape(n_cycle, chan_dev * 2 * M_DEV)
    theta_tab = theta_table(jnp.arange(n_cycle, dtype=jnp.int32), n_cycle)
    onehot = (
        beam_index[:, None] == jnp.arange(beam_profile.shape[0], dtype=jnp.int32)[None, :]
    ).astype(jnp.float32)
    profiles = jnp.dot(onehot, beam_profile, precision=lax.Precision.HIGHEST)
    orders = lax.axis_index("grp") * M_DEV + jnp.arange(M_DEV, dtype=jnp.int32)
    mweight = 0.25 + orders.astype(jnp.float32) / m_width
    mw_row = jnp.concatenate([mweight, mweight])[None, :]
    prof_col = profiles[:, :, None]
    width = 2 * M_DEV
    vmem = pltpu.CompilerParams(vmem_limit_bytes=32 * 1024 * 1024)
    power_part = pl.pallas_call(
        power_kernel,
        grid=(chan_dev // POWER_STEP,),
        in_specs=harmonic_specs(L, n_cycle, width, POWER_STEP),
        out_specs=pl.BlockSpec((POWER_STEP, 1, 128), lambda c: (c, 0, 0)),
        out_shape=jax.ShapeDtypeStruct((chan_dev, 1, 128), jnp.float32),
        compiler_params=vmem,
    )(theta_tab, moved, prof_col, mw_row)[:, 0, 0]
    power = ring_sum(power_part, subs[3:])
    scale = lax.rsqrt(power / (2.0 * L * m_width) + 1e-06)
    scale = jnp.broadcast_to(scale[:, None, None], (chan_dev, 1, 128))
    return pl.pallas_call(
        output_kernel,
        grid=(chan_dev // OUT_STEP,),
        in_specs=harmonic_specs(L, n_cycle, width, OUT_STEP)
        + [pl.BlockSpec((OUT_STEP, 1, 128), lambda c: (c, 0, 0))],
        out_specs=pl.BlockSpec((L, OUT_STEP, 2, M_DEV), lambda c: (0, c, 0, 0)),
        out_shape=jax.ShapeDtypeStruct((L, chan_dev, 2, M_DEV), jnp.float32),
        compiler_params=vmem,
    )(theta_tab, moved, prof_col, mw_row, scale)


def solution(mesh):
    return jax.shard_map(
        body,
        mesh=mesh,
        in_specs=(P(None, ("blk", "grp")), P(), P(("blk", "grp")), P(), P("blk")),
        out_specs=P(None, "blk", None, "grp"),
        check_vma=False,
    )
```

```python
import jax
import jax.numpy as jnp
from jax import lax
from jax.sharding import PartitionSpec as P
from jax.experimental import pallas as pl
from jax.experimental.pallas import tpu as pltpu

RPIX = 2048
L = 1024
M_DEV = 256
J_LO = 128


def cos_sin_of_phase(phase, length):
    angle = jnp.pi * phase.astype(jnp.float32) / length.astype(jnp.float32)
    return jnp.cos(angle), jnp.sin(angle)


def add_angles(ca, sa, cb, sb):
    return ca * cb - sa * sb, sa * cb + ca * sb


def small_tables(cycle_len, m_width):
    length = cycle_len[:, None, None]
    period = 2 * length
    orders = jnp.arange(m_width, dtype=jnp.int32)[None, None, :]
    j_hi = jnp.arange(RPIX // J_LO, dtype=jnp.int32)[None, :, None]
    j_mid = jnp.arange(J_LO // 16, dtype=jnp.int32)[None, :, None]
    j_q = jnp.arange(16, dtype=jnp.int32)[None, :, None]
    ca, sa = cos_sin_of_phase((2 * J_LO * j_hi) % period * orders % period, length)
    cm, sm = cos_sin_of_phase((32 * j_mid) % period * orders % period, length)
    cq, sq = cos_sin_of_phase(orders * (2 * j_q + 1) % period, length)
    cb, sb = add_angles(cm[:, :, None, :], sm[:, :, None, :], cq[:, None, :, :], sq[:, None, :, :])
    n_cyc = cycle_len.shape[0]
    cb = cb.reshape(n_cyc, J_LO, m_width)
    sb = sb.reshape(n_cyc, J_LO, m_width)
    return ca, sa, cb, sb


def table_kernel(ca_ref, sa_ref, cb_ref, sb_ref, inv_ref, len_ref, tab_ref):
    m_width = cb_ref.shape[2]
    inv = inv_ref[0][:, 0:1]
    length = len_ref[0][:, 0:1]

    def build(t, carry):
        ca = ca_ref[0, pl.ds(t, 1), :]
        sa = sa_ref[0, pl.ds(t, 1), :]
        cb = cb_ref[0]
        sb = sb_ref[0]
        rows = t * J_LO + lax.broadcasted_iota(jnp.int32, (J_LO, 1), 0)
        weight = jnp.where(rows < length, inv, 0.0)
        cos_t, sin_t = add_angles(ca, sa, cb, sb)
        r0 = pl.multiple_of(t * J_LO, J_LO)
        tab_ref[0, pl.ds(r0, J_LO), 0:m_width] = (cos_t * weight).astype(jnp.bfloat16)
        tab_ref[0, pl.ds(r0, J_LO), m_width : 2 * m_width] = (sin_t * -weight).astype(jnp.bfloat16)
        return carry

    lax.fori_loop(0, RPIX // J_LO, build, 0, unroll=4)


def cycle_tables(cycle_len, m_width):
    n_cyc = cycle_len.shape[0]
    ca, sa, cb, sb = small_tables(cycle_len, m_width)
    inv = jnp.broadcast_to(lax.rsqrt(cycle_len.astype(jnp.float32))[:, None, None], (n_cyc, 1, 128))
    lens = jnp.broadcast_to(cycle_len[:, None, None], (n_cyc, 1, 128))
    n_hi = RPIX // J_LO
    return pl.pallas_call(
        table_kernel,
        grid=(n_cyc,),
        in_specs=[
            pl.BlockSpec((1, n_hi, m_width), lambda k: (k, 0, 0)),
            pl.BlockSpec((1, n_hi, m_width), lambda k: (k, 0, 0)),
            pl.BlockSpec((1, J_LO, m_width), lambda k: (k, 0, 0)),
            pl.BlockSpec((1, J_LO, m_width), lambda k: (k, 0, 0)),
            pl.BlockSpec((1, 1, 128), lambda k: (k, 0, 0)),
            pl.BlockSpec((1, 1, 128), lambda k: (k, 0, 0)),
        ],
        out_specs=pl.BlockSpec((1, RPIX, 2 * m_width), lambda k: (k, 0, 0)),
        out_shape=jax.ShapeDtypeStruct((n_cyc, RPIX, 2 * m_width), jnp.bfloat16),
        compiler_params=pltpu.CompilerParams(vmem_limit_bytes=40 * 1024 * 1024),
    )(ca, sa, cb, sb, inv, lens)


def fourier_kernel(len_ref, sky_ref, proj_ref, basis_ref, tab_ref, o_ref, clean_ref):
    m_width = tab_ref.shape[2] // 2
    n_grp = o_ref.shape[0] // (sky_ref.shape[0] // o_ref.shape[1])
    chan_dev = o_ref.shape[1]
    length = len_ref[0][:, 0:1]
    cols = lax.broadcasted_iota(jnp.int32, (1, RPIX), 1)
    masked = jnp.where(cols < length, sky_ref[...].astype(jnp.float32), 0.0)
    correction = jnp.dot(
        proj_ref[...], basis_ref[...], preferred_element_type=jnp.float32,
        precision=lax.Precision.HIGHEST,
    )
    clean_ref[...] = (masked - correction).astype(jnp.bfloat16)
    m_dev = m_width // n_grp
    step = 2 * m_dev
    n_blk = sky_ref.shape[0] // chan_dev
    for q in range(2 * m_width // step):
        res = jnp.dot(
            clean_ref[...], tab_ref[0, :, q * step : (q + 1) * step], preferred_element_type=jnp.float32
        )
        part = (q * step) // m_width
        for h in range(step // m_dev):
            grp_dest = (q * step - part * m_width) // m_dev + h
            for blk_dest in range(n_blk):
                slab = res[blk_dest * chan_dev : (blk_dest + 1) * chan_dev, h * m_dev : (h + 1) * m_dev]
                o_ref[blk_dest * n_grp + grp_dest, :, part * m_dev : (part + 1) * m_dev] = slab.astype(
                    jnp.bfloat16
                )


def cycle_fourier(sky_map, projected_t, basis, tables, cycle_len, n_blk, n_grp):
    n_cyc = cycle_len.shape[0]
    n_chan = sky_map.shape[0]
    n_mode = basis.shape[0]
    n_dev = n_blk * n_grp
    chan_dev = n_chan // n_blk
    width = tables.shape[2]
    lens = jnp.broadcast_to(cycle_len[:, None, None], (n_cyc, 1, 128))
    m_dev = width // 2 // n_grp
    return pl.pallas_call(
        fourier_kernel,
        grid=(n_cyc,),
        in_specs=[
            pl.BlockSpec((1, 1, 128), lambda k: (k, 0, 0)),
            pl.BlockSpec((n_chan, RPIX), lambda k: (0, k)),
            pl.BlockSpec((n_chan, n_mode), lambda k: (0, 0)),
            pl.BlockSpec((n_mode, RPIX), lambda k: (0, k)),
            pl.BlockSpec((1, RPIX, width), lambda k: (k, 0, 0)),
        ],
        out_specs=pl.BlockSpec((n_dev, None, chan_dev, 2 * m_dev), lambda k: (0, k, 0, 0)),
        out_shape=jax.ShapeDtypeStruct((n_dev, n_cyc, chan_dev, 2 * m_dev), jnp.bfloat16),
        scratch_shapes=[pltpu.VMEM((n_chan, RPIX), jnp.bfloat16)],
        compiler_params=pltpu.CompilerParams(vmem_limit_bytes=48 * 1024 * 1024),
    )(lens, sky_map, projected_t, basis, tables)


POWER_STEP = 8
OUT_STEP = 1


def harmonic_tile(theta_ref, mv_ref, prof_ref, mw_ref, lc, ci):
    rows = pl.ds(lc * 256, 256)
    width = mw_ref.shape[1]
    h = jnp.dot(
        theta_ref[rows, :], mv_ref[:, ci * width : (ci + 1) * width], preferred_element_type=jnp.float32
    )
    return h * prof_ref[ci, rows, :] * mw_ref[...]


def power_kernel(theta_ref, mv_ref, prof_ref, mw_ref, o_ref):
    for ci in range(prof_ref.shape[0]):
        total = jnp.zeros((1, 1), jnp.float32)
        for lc in range(theta_ref.shape[0] // 256):
            w = harmonic_tile(theta_ref, mv_ref, prof_ref, mw_ref, lc, ci)
            total = total + jnp.sum(w * w, keepdims=True)
        o_ref[ci] = jnp.broadcast_to(total, (1, 128))


def output_kernel(theta_ref, mv_ref, prof_ref, mw_ref, scale_ref, o_ref):
    half = mw_ref.shape[1] // 2
    for ci in range(prof_ref.shape[0]):
        scale = scale_ref[ci][:, 0:1]
        for lc in range(theta_ref.shape[0] // 256):
            w = harmonic_tile(theta_ref, mv_ref, prof_ref, mw_ref, lc, ci) * scale
            for p in range(2):
                o_ref[pl.ds(lc * 256, 256), ci, p, :] = w[:, p * half : (p + 1) * half]


def harmonic_specs(n_l, n_cycle, width, step):
    return [
        pl.BlockSpec((n_l, n_cycle), lambda c: (0, 0)),
        pl.BlockSpec((n_cycle, step * width), lambda c: (0, c)),
        pl.BlockSpec((step, n_l, 1), lambda c: (c, 0, 0)),
        pl.BlockSpec((1, width), lambda c: (0, 0)),
    ]


def theta_table(cycle_ids, n_cycle):
    degrees = jnp.arange(L, dtype=jnp.int32)
    odd = 2 * cycle_ids + 1
    phase = degrees[:, None] * odd[None, :] % (4 * n_cycle)
    angle = jnp.pi * phase.astype(jnp.float32) / (2.0 * n_cycle)
    weight = jnp.sin(jnp.pi * odd.astype(jnp.float32) / (2.0 * n_cycle)) * (
        2.0 / jnp.sqrt(jnp.float32(n_cycle))
    )
    return (jnp.cos(angle) * weight[None, :]).astype(jnp.bfloat16)


def sub_axes(n_blk, n_grp):
    return [
        ("blk", 2, 1, n_blk),
        ("blk", 4, 2, n_blk),
        ("blk", n_blk // 8, 8, n_blk),
        ("grp", n_grp, 1, n_grp),
    ]


def shift_perm(size, stride, total, k):
    pairs = []
    for i in range(total):
        c = (i // stride) % size
        pairs.append((i, i + ((c + k) % size - c) * stride))
    return pairs


def ring_sum(v, subs):
    for axis, size, stride, total in subs:
        parts = [lax.ppermute(v, axis, shift_perm(size, stride, total, k)) for k in range(1, size)]
        for part in parts:
            v = v + part
    return v


def body(sky_map, fg_templates, cycle_len, beam_profile, beam_index):
    n_blk = lax.axis_size("blk")
    n_grp = lax.axis_size("grp")
    cycle_dev = cycle_len.shape[0]
    n_chan = sky_map.shape[0]
    n_mode = fg_templates.shape[1]
    chan_dev = n_chan // n_blk
    m_width = M_DEV * n_grp
    n_cycle = cycle_dev * n_blk * n_grp
    slots = jnp.arange(RPIX, dtype=jnp.int32)
    valid = (slots[None, :] < cycle_len[:, None]).reshape(-1)
    masked = jnp.where(valid[None, :], sky_map, jnp.zeros((), jnp.bfloat16))
    mode_amps = jnp.dot(fg_templates.T, masked, preferred_element_type=jnp.float32).astype(
        jnp.bfloat16
    )
    gram_part = jnp.dot(mode_amps, mode_amps.T, preferred_element_type=jnp.float32)
    cross_part = lax.dot_general(
        mode_amps, masked, (((1,), (1,)), ((), ())), preferred_element_type=jnp.float32
    )
    amps_wide = mode_amps.astype(jnp.float32)
    tables = cycle_tables(cycle_len, m_width)
    subs = sub_axes(n_blk, n_grp)
    sums = ring_sum(jnp.concatenate([gram_part, cross_part], axis=1), subs)
    gram_sum = sums[:, :n_mode]
    cross_sum = sums[:, n_mode:]
    lower = jnp.linalg.cholesky(gram_sum)
    basis = jax.scipy.linalg.solve_triangular(lower, amps_wide, lower=True)
    projected = jax.scipy.linalg.solve_triangular(lower, cross_sum, lower=True)
    sendbuf = cycle_fourier(sky_map, projected.T, basis, tables, cycle_len, n_blk, n_grp)
    moved = lax.all_to_all(sendbuf, ("blk", "grp"), 0, 0, tiled=True)
    moved = moved.reshape(n_cycle, chan_dev * 2 * M_DEV)
    theta_tab = theta_table(jnp.arange(n_cycle, dtype=jnp.int32), n_cycle)
    onehot = (
        beam_index[:, None] == jnp.arange(beam_profile.shape[0], dtype=jnp.int32)[None, :]
    ).astype(jnp.float32)
    profiles = jnp.dot(onehot, beam_profile, precision=lax.Precision.HIGHEST)
    orders = lax.axis_index("grp") * M_DEV + jnp.arange(M_DEV, dtype=jnp.int32)
    mweight = 0.25 + orders.astype(jnp.float32) / m_width
    mw_row = jnp.concatenate([mweight, mweight])[None, :]
    prof_col = profiles[:, :, None]
    width = 2 * M_DEV
    vmem = pltpu.CompilerParams(vmem_limit_bytes=32 * 1024 * 1024)
    power_part = pl.pallas_call(
        power_kernel,
        grid=(chan_dev // POWER_STEP,),
        in_specs=harmonic_specs(L, n_cycle, width, POWER_STEP),
        out_specs=pl.BlockSpec((POWER_STEP, 1, 128), lambda c: (c, 0, 0)),
        out_shape=jax.ShapeDtypeStruct((chan_dev, 1, 128), jnp.float32),
        compiler_params=vmem,
    )(theta_tab, moved, prof_col, mw_row)[:, 0, 0]
    power = ring_sum(power_part, subs[3:])
    scale = lax.rsqrt(power / (2.0 * L * m_width) + 1e-06)
    scale = jnp.broadcast_to(scale[:, None, None], (chan_dev, 1, 128))
    return pl.pallas_call(
        output_kernel,
        grid=(chan_dev // OUT_STEP,),
        in_specs=harmonic_specs(L, n_cycle, width, OUT_STEP)
        + [pl.BlockSpec((OUT_STEP, 1, 128), lambda c: (c, 0, 0))],
        out_specs=pl.BlockSpec((L, OUT_STEP, 2, M_DEV), lambda c: (0, c, 0, 0)),
        out_shape=jax.ShapeDtypeStruct((L, chan_dev, 2, M_DEV), jnp.float32),
        compiler_params=vmem,
    )(theta_tab, moved, prof_col, mw_row, scale)


def solution(mesh):
    return jax.shard_map(
        body,
        mesh=mesh,
        in_specs=(P(None, ("blk", "grp")), P(), P(("blk", "grp")), P(), P("blk")),
        out_specs=P(None, "blk", None, "grp"),
        check_vma=False,
    )
```
